32 devices in a mesh: grp: 2 (over y), gx: 16 (over z, x, core).
Axes of the slice: x: 2, y: 2, z: 4, core: 2. Of those that a mesh axis runs over, the one named last changes fastest.
Arguments:
- adjoint_state: float32 [16, 512, 1024], P(None, ('grp', 'gx')), parts along dimension 1, may hold values from -6 to 6
- speed_x: float32 [16, 512, 1024], P(None, ('grp', 'gx')), parts along dimension 1, may hold values from 0.2 to 2
- speed_y: float32 [16, 512, 1024], P(None, ('grp', 'gx')), parts along dimension 1, may hold values from 0.2 to 2
- speed_z: float32 [16, 512, 1024], P(None, ('grp', 'gx')), parts along dimension 1, may hold values from 0.2 to 2
- dispersion: float32 [16, 512, 1024], P(None, ('grp', 'gx')), parts along dimension 1, may hold values from 0.05 to 0.5
- face_flags: int32 [16, 512, 1024], P(None, ('grp', 'gx')), parts along dimension 1, may hold values from 0 to 7
- layer_weight: float32 [16], replicated, may hold values from 0.1 to 1
- cov_x: bfloat16 [256, 4, 128], P('gx'), may hold values from -0.25 to 0.25
- offsets_x: int32 [2, 4], replicated, may hold values from 0 to 1, as said below
- cov_y: float32 [1024, 4, 128], replicated, may hold values from -0.25 to 0.25
- offsets_y: int32 [8, 4], replicated, may hold values from 0 to 7, as said below
Outputs:
- recharge: float32 [512, 1024], P(('grp', 'gx')), parts along dimension 0
- prior: float32 [512, 1024], P(('grp', 'gx')), parts along dimension 0
The draws below stay inside these ranges and needn't reach their ends.
There are 2 independent parts, one for each index of `grp`. The reference program is written for one: setup_inputs(seed, part) draws one part's arguments, and reference() takes and returns one part's arrays. A program takes and returns all parts, laid end to end along the dimension named above; an argument that names none is the same for every part. Nothing has to cross between parts.
Inputs may be any that keep to these rules, and one draw needn't show every extreme that they name: `offsets_x`: in every row, column 0 is 0, column 1 is 1 and column 2 is 1; the others are arbitrary. `offsets_y`: in every row, column 0 is 0, column 1 is 7 and column 2 is 4; the others are arbitrary.
All inputs are finite; a program needn't handle non-finite values.
Results may differ from the reference program's by a relative error of at most 0.00035.
Values may be sent and summed in bfloat16 or wider, within the bound.
No kernel may reach another device: no remote copies, remote signals or barrier semaphores. Data moves between devices by JAX's collectives and lax.ppermute only.
A program may use at most 128 MiB of HBM per device.

```python
import math
import jax
import jax.numpy as jnp
from jax import lax

BLK = 128
KB = 4
NY = 1024
NZ = 16
NX = 256
NXB = 2
NYB = 8


def offset_table(key, blocks):
    first = jnp.zeros((blocks, 1), jnp.int32)
    second = jnp.full((blocks, 1), blocks - 1, jnp.int32)
    third = jnp.full((blocks, 1), blocks // 2, jnp.int32)
    others = jax.random.randint(key, (blocks, KB - 3), 0, blocks, dtype=jnp.int32)
    return jnp.concatenate([first, second, third, others], axis=1)


def draw_offsets_x(key, part):
    return offset_table(jax.random.fold_in(key, 11), NXB)


def draw_offsets_y(key, part):
    return offset_table(jax.random.fold_in(key, 23), NYB)


def touch_ends(values, stream_key, low, top_value):
    shape = values.shape
    spot = [jax.random.randint(jax.random.fold_in(stream_key, axis), (), 0, shape[axis]) for axis in range(len(shape))]
    values = values.at[tuple(spot)].set(low)
    longest = shape.index(max(shape))
    spot[longest] = (spot[longest] + 1) % shape[longest]
    return values.at[tuple(spot)].set(top_value)


def level_of(rng, dims, split, least, largest):
    gain, own = 1.0, jax.random.fold_in(rng, 6)
    for dim, parts in split:
        heights = jnp.exp(jax.random.uniform(jax.random.fold_in(own, dim), (parts,), jnp.float32, least / len(split), largest / len(split)))
        gain = gain * jnp.repeat(heights, dims[dim] // parts).reshape([-1 if axis == dim else 1 for axis in range(len(dims))])
    return gain


def noise(stream_key, shape, width, reach, pieces=(), held_as=jnp.bfloat16):
    array = width * jax.random.normal(stream_key, shape, jnp.float32)
    if pieces:
        array = array * level_of(stream_key, shape, pieces, -0.22, 0.18)
    return jnp.clip(array, -reach, reach).astype(held_as)


def setup_inputs(seed: int = 0, part: int = 0) -> dict:
    key_of = jax.random.split(jax.random.key(seed), 12)
    own_keys = jax.random.split(jax.random.fold_in(key_of[11], part), 12)
    return {
        "adjoint_state": noise(own_keys[0], (NZ, NX, NY), 1.0, 6.0, ((1, 16),), jnp.float32),
        "speed_x": jnp.clip(jnp.exp(math.log(2.0) - 2.3025851 * jax.random.uniform(own_keys[1], (NZ, NX, NY), jnp.float32) ** level_of(own_keys[1], (NZ, NX, NY), ((1, 16),), -0.2, 0.2)), 0.2, 2.0),
        "speed_y": jnp.clip(jnp.exp(math.log(2.0) - 2.3025851 * jax.random.uniform(own_keys[2], (NZ, NX, NY), jnp.float32) ** level_of(own_keys[2], (NZ, NX, NY), ((1, 16),), -0.2, 0.2)), 0.2, 2.0),
        "speed_z": jnp.clip(jnp.exp(math.log(2.0) - 2.3025851 * jax.random.uniform(own_keys[3], (NZ, NX, NY), jnp.float32) ** level_of(own_keys[3], (NZ, NX, NY), ((1, 16),), -0.2, 0.2)), 0.2, 2.0),
        "dispersion": jnp.clip(jnp.exp(math.log(0.5) - 2.3025851 * jax.random.uniform(own_keys[4], (NZ, NX, NY), jnp.float32) ** level_of(own_keys[4], (NZ, NX, NY), ((1, 16),), -0.2, 0.2)), 0.05, 0.5),
        "face_flags": touch_ends(jax.random.randint(own_keys[5], (NZ, NX, NY), 0, 8), jax.random.fold_in(own_keys[5], 1), 0, 7).astype(jnp.int32),
        "layer_weight": jnp.clip(jnp.exp(jax.random.uniform(key_of[6], (NZ,), jnp.float32, math.log(0.1), math.log(1.0))), 0.1, 1.0),
        "cov_x": noise(key_of[7], (NX, KB, BLK), (KB * BLK) ** -0.5, 0.25, ((0, 16),)),
        "offsets_x": draw_offsets_x(jax.random.fold_in(key_of[11], 71), part),
        "cov_y": noise(key_of[9], (NY, KB, BLK), (KB * BLK) ** -0.5, 0.25, (), jnp.float32),
        "offsets_y": draw_offsets_y(jax.random.fold_in(key_of[11], 71), part),
    }


precise = lax.Precision.HIGHEST


def step_back(field, axis_number):
    length = field.shape[axis_number]
    leading = jnp.zeros_like(lax.slice_in_dim(field, 0, 1, axis=axis_number))
    return jnp.concatenate([leading, lax.slice_in_dim(field, 0, length - 1, axis=axis_number)], axis=axis_number)


def step_ahead(field, axis_number):
    length = field.shape[axis_number]
    trailing = jnp.zeros_like(lax.slice_in_dim(field, 0, 1, axis=axis_number))
    return jnp.concatenate([lax.slice_in_dim(field, 1, length, axis=axis_number), trailing], axis=axis_number)


def face_term(field, speed, upwind, spread, axis_number):
    lower_coef = speed * upwind + spread
    upper_coef = speed * (1.0 - upwind) + spread
    jump = field - step_back(field, axis_number)
    return upper_coef * jump + step_ahead(-lower_coef * jump, axis_number)


def band_matrix(values, offsets):
    rows = values.shape[0]
    blocks = offsets.shape[0]
    row_block = jnp.arange(rows).astype(jnp.int32) // BLK
    target = (row_block[:, None] + offsets[row_block]) % blocks
    picks = (target[:, :, None] == jnp.arange(blocks).astype(jnp.int32)[None, None, :]).astype(jnp.float32)
    dense = jnp.einsum("rkb,rkc->rbc", picks, values.astype(jnp.float32), precision=precise)
    return dense.reshape(rows, blocks * BLK)


def reference(adjoint_state, speed_x, speed_y, speed_z, dispersion, face_flags, layer_weight, cov_x, offsets_x, cov_y, offsets_y):
    upwind_x = (face_flags % 2).astype(jnp.float32)
    upwind_y = ((face_flags // 2) % 2).astype(jnp.float32)
    upwind_z = ((face_flags // 4) % 2).astype(jnp.float32)
    image = face_term(adjoint_state, speed_x, upwind_x, dispersion, 1)
    image = image + face_term(adjoint_state, speed_y, upwind_y, dispersion, 2)
    image = image + face_term(adjoint_state, speed_z, upwind_z, dispersion, 0)
    recharge = jnp.einsum("z,zxy->xy", layer_weight, image, precision=precise)
    dense_y = band_matrix(cov_y, offsets_y)
    smoothed = jnp.einsum("xc,rc->xr", recharge, dense_y, precision=precise)
    dense_x = band_matrix(cov_x, offsets_x)
    prior = jnp.dot(dense_x, smoothed, precision=precise)
    return recharge, prior
```

```python
import jax
import jax.numpy as jnp
from jax import lax
from jax.experimental import pallas as pl
from jax.experimental.pallas import tpu as pltpu
from jax.sharding import PartitionSpec as P

BLK = 128
Z_CHUNK = 4

precise = lax.Precision.HIGHEST


def passed_along(value, axis, steps):
    count = lax.axis_size(axis)
    first, last = (max(0, -steps), min(count, count - steps))
    return lax.ppermute(value, axis, [(source, source + steps) for source in range(first, last)])


def coefs(flags, bit, speed, spread):
    on = (flags & bit) != 0
    lower = spread + jnp.where(on, speed, 0.0)
    upper = spread + jnp.where(on, 0.0, speed)
    return lower, upper


def stencil_kernel(w_ref, s_ref, sprev_ref, f_ref, vx_ref, vy_ref, vz_ref, d_ref, out_ref):
    c = pl.program_id(0)
    rows, cols = out_ref.shape
    sub = lax.broadcasted_iota(jnp.int32, (rows, cols), 0)
    lane = lax.broadcasted_iota(jnp.int32, (rows, cols), 1)

    @pl.when(c == 0)
    def _():
        out_ref[...] = jnp.zeros_like(out_ref)

    prev = jnp.where(c > 0, sprev_ref[0], 0.0)
    acc = jnp.zeros((rows, cols), jnp.float32)
    for j in range(s_ref.shape[0]):
        z = c * s_ref.shape[0] + j
        s = s_ref[j]
        f = f_ref[j]
        d = d_ref[j]
        lo_x, up_x = coefs(f, 1, vx_ref[j], d)
        lo_y, up_y = coefs(f, 2, vy_ref[j], d)
        lo_z, up_z = coefs(f, 4, vz_ref[j], d)
        s_xm = jnp.where(sub == 0, 0.0, pltpu.roll(s, 1, 0))
        jx = s - s_xm
        ax = -lo_x * jx
        ax_next = jnp.where(sub == rows - 1, 0.0, pltpu.roll(ax, rows - 1, 0))
        img = up_x * jx + ax_next
        s_ym = jnp.where(lane == 0, 0.0, pltpu.roll(s, 1, 1))
        jy = s - s_ym
        ay = -lo_y * jy
        ay_next = jnp.where(lane == cols - 1, 0.0, pltpu.roll(ay, cols - 1, 1))
        img = img + (up_y * jy + ay_next)
        jz = s - prev
        img = img + up_z * jz
        acc = acc + w_ref[z] * img
        w_before = jnp.where(z > 0, w_ref[jnp.maximum(z - 1, 0)], 0.0)
        acc = acc + w_before * (-lo_z * jz)
        prev = s
    out_ref[...] += acc


def stencil(layer_weight, s, f, vx, vy, vz, d):
    depth, rows, cols = s.shape
    zc = Z_CHUNK if depth % Z_CHUNK == 0 else depth
    block = pl.BlockSpec((zc, rows, cols), lambda c: (c, 0, 0))
    prev_block = pl.BlockSpec((1, rows, cols), lambda c: (jnp.maximum(c * zc - 1, 0), 0, 0))
    return pl.pallas_call(
        stencil_kernel,
        grid=(depth // zc,),
        in_specs=[
            pl.BlockSpec(memory_space=pltpu.SMEM),
            block,
            prev_block,
            block,
            block,
            block,
            block,
            block,
        ],
        out_specs=pl.BlockSpec((rows, cols), lambda c: (0, 0)),
        out_shape=jax.ShapeDtypeStruct((rows, cols), jnp.float32),
        compiler_params=pltpu.CompilerParams(dimension_semantics=("arbitrary",)),
    )(layer_weight, s, s, f, vx, vy, vz, d)


def bit_reversed(count):
    bits = count.bit_length() - 1
    return [int(format(p, f"0{bits}b")[::-1], 2) if bits else 0 for p in range(count)]


def gather_rows(local, axis):
    count = lax.axis_size(axis)
    buf = local[None]
    bit = count // 2
    while bit >= 1:
        other = lax.ppermute(buf, axis, [(i, i ^ bit) for i in range(count)])
        buf = jnp.concatenate([buf, other], axis=0)
        bit //= 2
    return buf


def body(
    adjoint_state,
    speed_x,
    speed_y,
    speed_z,
    dispersion,
    face_flags,
    layer_weight,
    cov_x,
    offsets_x,
    cov_y,
    offsets_y,
):
    count = lax.axis_size("gx")
    me = lax.axis_index("gx")
    depth, rows, cols = adjoint_state.shape

    first_s = adjoint_state[:, 0, :]
    lo_x0, up_x0 = coefs(face_flags[:, 0, :], 1, speed_x[:, 0, :], dispersion[:, 0, :])
    last_s = adjoint_state[:, rows - 1, :]
    from_next = passed_along(jnp.stack([first_s, lo_x0]), "gx", -1)
    from_prev = passed_along(last_s, "gx", 1)

    partial = stencil(layer_weight, adjoint_state, face_flags, speed_x, speed_y, speed_z, dispersion)

    corr_first = jnp.sum(layer_weight[:, None] * (-up_x0 * from_prev), axis=0)
    ax_next = -from_next[1] * (from_next[0] - last_s)
    corr_last = jnp.sum(layer_weight[:, None] * ax_next, axis=0)
    recharge = partial.at[0].add(corr_first).at[rows - 1].add(corr_last)

    gathered = gather_rows(recharge, "gx")
    order = me ^ jnp.array(bit_reversed(count), jnp.int32)

    nxb = offsets_x.shape[0]
    global_rows = me * rows + jnp.arange(rows)
    row_block = global_rows // BLK
    target = (row_block[:, None] + offsets_x[row_block]) % nxb
    blocks = jnp.arange(nxb)
    hit = target[:, :, None, None] == blocks[None, None, :, None]
    slab = jnp.sum(jnp.where(hit, cov_x.astype(jnp.float32)[:, :, None, :], 0.0), axis=1)
    slab = slab.reshape(rows, count, rows)
    slab = jnp.take(slab, order, axis=1).reshape(rows, count * rows)
    mixed = jnp.dot(slab, gathered.reshape(count * rows, cols), precision=precise, preferred_element_type=jnp.float32)

    nyb = offsets_y.shape[0]
    col_block = (jnp.arange(nyb)[:, None] + offsets_y) % nyb
    picked = jnp.take(mixed.reshape(rows, nyb, BLK), col_block, axis=1)
    prior = jnp.einsum(
        "xrkc,rikc->xri",
        picked,
        cov_y.reshape(nyb, BLK, cov_y.shape[1], BLK),
        precision=precise,
        preferred_element_type=jnp.float32,
    ).reshape(rows, cols)
    return (recharge, prior)


def solution(mesh):
    return jax.shard_map(
        body,
        mesh=mesh,
        in_specs=(
            P(None, ("grp", "gx"), None),
            P(None, ("grp", "gx"), None),
            P(None, ("grp", "gx"), None),
            P(None, ("grp", "gx"), None),
            P(None, ("grp", "gx"), None),
            P(None, ("grp", "gx"), None),
            P(),
            P("gx", None, None),
            P(),
            P(),
            P(),
        ),
        out_specs=(P(("grp", "gx"), None), P(("grp", "gx"), None)),
        check_vma=False,
    )
```

```python
import jax
import jax.numpy as jnp
from jax import lax
from jax.experimental import pallas as pl
from jax.experimental.pallas import tpu as pltpu
from jax.sharding import PartitionSpec as P

BLK = 128
Z_CHUNK = 4

precise = lax.Precision.HIGHEST


def passed_along(value, axis, steps):
    count = lax.axis_size(axis)
    first, last = (max(0, -steps), min(count, count - steps))
    return lax.ppermute(value, axis, [(source, source + steps) for source in range(first, last)])


def coefs(flags, bit, speed, spread):
    on = (flags & bit) != 0
    lower = spread + jnp.where(on, speed, 0.0)
    upper = spread + jnp.where(on, 0.0, speed)
    return lower, upper


def stencil_kernel(w_ref, s_ref, sprev_ref, f_ref, vx_ref, vy_ref, vz_ref, d_ref, out_ref):
    c = pl.program_id(0)
    rows, cols = out_ref.shape
    sub = lax.broadcasted_iota(jnp.int32, (rows, cols), 0)
    lane = lax.broadcasted_iota(jnp.int32, (rows, cols), 1)

    @pl.when(c == 0)
    def _():
        out_ref[...] = jnp.zeros_like(out_ref)

    prev = jnp.where(c > 0, sprev_ref[0], 0.0)
    acc = jnp.zeros((rows, cols), jnp.float32)
    for j in range(s_ref.shape[0]):
        z = c * s_ref.shape[0] + j
        s = s_ref[j]
        f = f_ref[j]
        d = d_ref[j]
        lo_x, up_x = coefs(f, 1, vx_ref[j], d)
        lo_y, up_y = coefs(f, 2, vy_ref[j], d)
        lo_z, up_z = coefs(f, 4, vz_ref[j], d)
        s_xm = jnp.where(sub == 0, 0.0, pltpu.roll(s, 1, 0))
        jx = s - s_xm
        ax = -lo_x * jx
        ax_next = jnp.where(sub == rows - 1, 0.0, pltpu.roll(ax, rows - 1, 0))
        img = up_x * jx + ax_next
        s_ym = jnp.where(lane == 0, 0.0, pltpu.roll(s, 1, 1))
        jy = s - s_ym
        ay = -lo_y * jy
        ay_next = jnp.where(lane == cols - 1, 0.0, pltpu.roll(ay, cols - 1, 1))
        img = img + (up_y * jy + ay_next)
        jz = s - prev
        img = img + up_z * jz
        acc = acc + w_ref[z] * img
        w_before = jnp.where(z > 0, w_ref[jnp.maximum(z - 1, 0)], 0.0)
        acc = acc + w_before * (-lo_z * jz)
        prev = s
    out_ref[...] += acc


def stencil(layer_weight, s, f, vx, vy, vz, d):
    depth, rows, cols = s.shape
    zc = Z_CHUNK if depth % Z_CHUNK == 0 else depth
    block = pl.BlockSpec((zc, rows, cols), lambda c: (c, 0, 0))
    prev_block = pl.BlockSpec((1, rows, cols), lambda c: (jnp.maximum(c * zc - 1, 0), 0, 0))
    return pl.pallas_call(
        stencil_kernel,
        grid=(depth // zc,),
        in_specs=[
            pl.BlockSpec(memory_space=pltpu.SMEM),
            block,
            prev_block,
            block,
            block,
            block,
            block,
            block,
        ],
        out_specs=pl.BlockSpec((rows, cols), lambda c: (0, 0)),
        out_shape=jax.ShapeDtypeStruct((rows, cols), jnp.float32),
        compiler_params=pltpu.CompilerParams(dimension_semantics=("arbitrary",)),
    )(layer_weight, s, s, f, vx, vy, vz, d)


def gather_rounds(count):
    bits = []
    bit = count // 2
    while bit >= 1:
        bits.append(bit)
        bit //= 2
    if len(bits) < 2:
        return [bits] if bits else []
    return [[bits[1], bits[0], bits[0] | bits[1]]] + [[b] for b in bits[2:]]


def gather_rows(local, axis):
    count = lax.axis_size(axis)
    buf = local[None]
    entries = [0]
    for masks in gather_rounds(count):
        others = [lax.ppermute(buf, axis, [(i, i ^ m) for i in range(count)]) for m in masks]
        buf = jnp.concatenate([buf] + others, axis=0)
        entries = entries + [m ^ q for m in masks for q in entries]
    return buf, entries


def edges_kernel(s_lo_ref, s_hi_ref, f_ref, vx_ref, d_ref, first_ref, last_ref, lo_ref, up_ref):
    first_ref[...] = s_lo_ref[:, 0, :]
    last_ref[...] = s_hi_ref[:, s_hi_ref.shape[1] - 1, :]
    lo, up = coefs(f_ref[:, 0, :], 1, vx_ref[:, 0, :], d_ref[:, 0, :])
    lo_ref[...] = lo
    up_ref[...] = up


def edges(s, f, vx, d):
    depth, rows, cols = s.shape
    part = 8 if rows % 8 == 0 else rows
    lo_block = pl.BlockSpec((depth, part, cols), lambda i: (0, 0, 0))
    hi_block = pl.BlockSpec((depth, part, cols), lambda i: (0, rows // part - 1, 0))
    plane = jax.ShapeDtypeStruct((depth, cols), jnp.float32)
    whole = pl.BlockSpec((depth, cols), lambda i: (0, 0))
    return pl.pallas_call(
        edges_kernel,
        grid=(1,),
        in_specs=[lo_block, hi_block, lo_block, lo_block, lo_block],
        out_specs=[whole] * 4,
        out_shape=[plane] * 4,
    )(s, s, f, vx, d)


def prior_kernel(cb_ref, slab_ref, buf_ref, cy_ref, out_ref, mixed_ref):
    rb = pl.program_id(0)
    kb = cy_ref.shape[1] // BLK

    @pl.when(rb == 0)
    def _():
        mixed_ref[...] = jnp.dot(slab_ref[...], buf_ref[...], precision=precise, preferred_element_type=jnp.float32)

    acc = jnp.zeros(out_ref.shape, jnp.float32)
    for k in range(kb):
        start = pl.multiple_of(cb_ref[rb * kb + k] * BLK, BLK)
        picked = mixed_ref[:, pl.ds(start, BLK)]
        weights = cy_ref[:, k * BLK:(k + 1) * BLK]
        acc = acc + lax.dot_general(
            picked, weights, (((1,), (1,)), ((), ())), precision=precise, preferred_element_type=jnp.float32
        )
    out_ref[...] = acc


def apply_prior(col_block, slab, buf, cy2):
    rows, inner = slab.shape
    cols = cy2.shape[0]
    nyb = cols // BLK
    grid_spec = pltpu.PrefetchScalarGridSpec(
        num_scalar_prefetch=1,
        grid=(nyb,),
        in_specs=[
            pl.BlockSpec((rows, inner), lambda r, cb: (0, 0)),
            pl.BlockSpec((inner, cols), lambda r, cb: (0, 0)),
            pl.BlockSpec((BLK, cy2.shape[1]), lambda r, cb: (r, 0)),
        ],
        out_specs=pl.BlockSpec((rows, BLK), lambda r, cb: (0, r)),
        scratch_shapes=[pltpu.VMEM((rows, cols), jnp.float32)],
    )
    return pl.pallas_call(
        prior_kernel,
        grid_spec=grid_spec,
        out_shape=jax.ShapeDtypeStruct((rows, cols), jnp.float32),
        compiler_params=pltpu.CompilerParams(dimension_semantics=("arbitrary",)),
    )(col_block, slab, buf, cy2)


def body(
    adjoint_state,
    speed_x,
    speed_y,
    speed_z,
    dispersion,
    face_flags,
    layer_weight,
    cov_x,
    offsets_x,
    cov_y,
    offsets_y,
):
    count = lax.axis_size("gx")
    me = lax.axis_index("gx")
    depth, rows, cols = adjoint_state.shape

    first_s, last_s, lo_x0, up_x0 = edges(adjoint_state, face_flags, speed_x, dispersion)
    from_next = passed_along(jnp.stack([first_s, lo_x0]), "gx", -1)
    from_prev = passed_along(last_s, "gx", 1)

    partial = stencil(layer_weight, adjoint_state, face_flags, speed_x, speed_y, speed_z, dispersion)

    corr_first = jnp.sum(layer_weight[:, None] * (-up_x0 * from_prev), axis=0)
    ax_next = -from_next[1] * (from_next[0] - last_s)
    corr_last = jnp.sum(layer_weight[:, None] * ax_next, axis=0)
    row = lax.broadcasted_iota(jnp.int32, (rows, cols), 0)
    recharge = partial + jnp.where(row == 0, corr_first[None, :], 0.0) + jnp.where(row == rows - 1, corr_last[None, :], 0.0)

    gathered, entries = gather_rows(recharge, "gx")
    order = me ^ jnp.array(entries, jnp.int32)

    nxb = offsets_x.shape[0]
    global_rows = me * rows + jnp.arange(rows)
    row_block = global_rows // BLK
    target = (row_block[:, None] + offsets_x[row_block]) % nxb
    blocks = jnp.arange(nxb)
    hit = target[:, :, None, None] == blocks[None, None, :, None]
    slab = jnp.sum(jnp.where(hit, cov_x.astype(jnp.float32)[:, :, None, :], 0.0), axis=1)
    slab = slab.reshape(rows, count, rows)
    slab = jnp.take(slab, order, axis=1).reshape(rows, count * rows)

    nyb = offsets_y.shape[0]
    col_block = ((jnp.arange(nyb)[:, None] + offsets_y) % nyb).reshape(-1).astype(jnp.int32)
    cy2 = cov_y.reshape(cov_y.shape[0], cov_y.shape[1] * cov_y.shape[2])
    prior = apply_prior(col_block, slab, gathered.reshape(count * rows, cols), cy2)
    return (recharge, prior)


def solution(mesh):
    return jax.shard_map(
        body,
        mesh=mesh,
        in_specs=(
            P(None, ("grp", "gx"), None),
            P(None, ("grp", "gx"), None),
            P(None, ("grp", "gx"), None),
            P(None, ("grp", "gx"), None),
            P(None, ("grp", "gx"), None),
            P(None, ("grp", "gx"), None),
            P(),
            P("gx", None, None),
            P(),
            P(),
            P(),
        ),
        out_specs=(P(("grp", "gx"), None), P(("grp", "gx"), None)),
        check_vma=False,
    )
```

```python
import jax
import jax.numpy as jnp
from jax import lax
from jax.experimental import pallas as pl
from jax.experimental.pallas import tpu as pltpu
from jax.sharding import PartitionSpec as P

BLK = 128
Z_CHUNK = 4

precise = lax.Precision.HIGHEST


def passed_along(value, axis, steps):
    count = lax.axis_size(axis)
    first, last = (max(0, -steps), min(count, count - steps))
    return lax.ppermute(value, axis, [(source, source + steps) for source in range(first, last)])


def coefs(flags, bit, speed, spread):
    on = (flags & bit) != 0
    lower = spread + jnp.where(on, speed, 0.0)
    upper = spread + jnp.where(on, 0.0, speed)
    return lower, upper


def stencil_kernel(w_ref, s_ref, sprev_ref, f_ref, vx_ref, vy_ref, vz_ref, d_ref, out_ref):
    c = pl.program_id(0)
    rows, cols = out_ref.shape
    sub = lax.broadcasted_iota(jnp.int32, (rows, cols), 0)
    lane = lax.broadcasted_iota(jnp.int32, (rows, cols), 1)

    @pl.when(c == 0)
    def _():
        out_ref[...] = jnp.zeros_like(out_ref)

    prev = jnp.where(c > 0, sprev_ref[0], 0.0)
    acc = jnp.zeros((rows, cols), jnp.float32)
    for j in range(s_ref.shape[0]):
        z = c * s_ref.shape[0] + j
        s = s_ref[j]
        f = f_ref[j]
        d = d_ref[j]
        lo_x, up_x = coefs(f, 1, vx_ref[j], d)
        lo_y, up_y = coefs(f, 2, vy_ref[j], d)
        lo_z, up_z = coefs(f, 4, vz_ref[j], d)
        s_xm = jnp.where(sub == 0, 0.0, pltpu.roll(s, 1, 0))
        jx = s - s_xm
        ax = -lo_x * jx
        ax_next = jnp.where(sub == rows - 1, 0.0, pltpu.roll(ax, rows - 1, 0))
        img = up_x * jx + ax_next
        s_ym = jnp.where(lane == 0, 0.0, pltpu.roll(s, 1, 1))
        jy = s - s_ym
        ay = -lo_y * jy
        ay_next = jnp.where(lane == cols - 1, 0.0, pltpu.roll(ay, cols - 1, 1))
        img = img + (up_y * jy + ay_next)
        jz = s - prev
        img = img + up_z * jz
        acc = acc + w_ref[z] * img
        w_before = jnp.where(z > 0, w_ref[jnp.maximum(z - 1, 0)], 0.0)
        acc = acc + w_before * (-lo_z * jz)
        prev = s
    out_ref[...] += acc


def stencil(layer_weight, s, f, vx, vy, vz, d):
    depth, rows, cols = s.shape
    zc = Z_CHUNK if depth % Z_CHUNK == 0 else depth
    block = pl.BlockSpec((zc, rows, cols), lambda c: (c, 0, 0))
    prev_block = pl.BlockSpec((1, rows, cols), lambda c: (jnp.maximum(c * zc - 1, 0), 0, 0))
    return pl.pallas_call(
        stencil_kernel,
        grid=(depth // zc,),
        in_specs=[
            pl.BlockSpec(memory_space=pltpu.SMEM),
            block,
            prev_block,
            block,
            block,
            block,
            block,
            block,
        ],
        out_specs=pl.BlockSpec((rows, cols), lambda c: (0, 0)),
        out_shape=jax.ShapeDtypeStruct((rows, cols), jnp.float32),
        compiler_params=pltpu.CompilerParams(dimension_semantics=("arbitrary",)),
    )(layer_weight, s, s, f, vx, vy, vz, d)


def gather_rounds(count):
    bits = []
    bit = count // 2
    while bit >= 2:
        bits.append(bit)
        bit //= 2
    if len(bits) < 2:
        return [[b] for b in bits]
    return [[bits[1], bits[0], bits[0] | bits[1]]] + [[b] for b in bits[2:]]


def cx_slab(cov_rows, offsets, device, rows):
    nxb = offsets.shape[0]
    global_rows = device * rows + jnp.arange(rows)
    row_block = global_rows // BLK
    target = (row_block[:, None] + offsets[row_block]) % nxb
    blocks = jnp.arange(nxb)
    hit = target[:, :, None, None] == blocks[None, None, :, None]
    slab = jnp.sum(jnp.where(hit, cov_rows.astype(jnp.float32)[:, :, None, :], 0.0), axis=1)
    return slab.reshape(rows, -1)


def mixed_rows(local, slab, axis):
    count = lax.axis_size(axis)
    me = lax.axis_index(axis)
    rows = local.shape[0]
    per_device = slab.reshape(slab.shape[0], count, rows)

    def product(piece, masks):
        cols = jnp.take(per_device, me ^ jnp.array(masks, jnp.int32), axis=1).reshape(slab.shape[0], -1)
        return jnp.dot(cols, piece.reshape(-1, piece.shape[-1]), precision=precise, preferred_element_type=jnp.float32)

    buf = local[None]
    entries = [0]
    total = product(buf, entries)
    for masks in gather_rounds(count):
        others = [lax.ppermute(buf, axis, [(i, i ^ m) for i in range(count)]) for m in masks]
        for m, other in zip(masks, others):
            total = total + product(other, [m ^ q for q in entries])
        buf = jnp.concatenate([buf] + others, axis=0)
        entries = entries + [m ^ q for m in masks for q in entries]
    own, for_partner = total[:rows], total[rows:]
    if count == 1:
        return own
    return own + lax.ppermute(for_partner, axis, [(i, i ^ 1) for i in range(count)])


def edges_kernel(s_lo_ref, s_hi_ref, f_ref, vx_ref, d_ref, first_ref, last_ref, lo_ref, up_ref):
    first_ref[...] = s_lo_ref[:, 0, :]
    last_ref[...] = s_hi_ref[:, s_hi_ref.shape[1] - 1, :]
    lo, up = coefs(f_ref[:, 0, :], 1, vx_ref[:, 0, :], d_ref[:, 0, :])
    lo_ref[...] = lo
    up_ref[...] = up


def edges(s, f, vx, d):
    depth, rows, cols = s.shape
    part = 8 if rows % 8 == 0 else rows
    lo_block = pl.BlockSpec((depth, part, cols), lambda i: (0, 0, 0))
    hi_block = pl.BlockSpec((depth, part, cols), lambda i: (0, rows // part - 1, 0))
    plane = jax.ShapeDtypeStruct((depth, cols), jnp.float32)
    whole = pl.BlockSpec((depth, cols), lambda i: (0, 0))
    return pl.pallas_call(
        edges_kernel,
        grid=(1,),
        in_specs=[lo_block, hi_block, lo_block, lo_block, lo_block],
        out_specs=[whole] * 4,
        out_shape=[plane] * 4,
    )(s, s, f, vx, d)


def body(
    adjoint_state,
    speed_x,
    speed_y,
    speed_z,
    dispersion,
    face_flags,
    layer_weight,
    cov_x,
    offsets_x,
    cov_y,
    offsets_y,
):
    count = lax.axis_size("gx")
    me = lax.axis_index("gx")
    depth, rows, cols = adjoint_state.shape

    first_s, last_s, lo_x0, up_x0 = edges(adjoint_state, face_flags, speed_x, dispersion)
    from_next = passed_along(jnp.stack([first_s, lo_x0]), "gx", -1)
    from_prev = passed_along(last_s, "gx", 1)

    partial = stencil(layer_weight, adjoint_state, face_flags, speed_x, speed_y, speed_z, dispersion)

    corr_first = jnp.sum(layer_weight[:, None] * (-up_x0 * from_prev), axis=0)
    ax_next = -from_next[1] * (from_next[0] - last_s)
    corr_last = jnp.sum(layer_weight[:, None] * ax_next, axis=0)
    row = lax.broadcasted_iota(jnp.int32, (rows, cols), 0)
    recharge = partial + jnp.where(row == 0, corr_first[None, :], 0.0) + jnp.where(row == rows - 1, corr_last[None, :], 0.0)

    partner_cov = lax.ppermute(cov_x, "gx", [(i, i ^ 1) for i in range(count)]) if count > 1 else cov_x
    slab = jnp.concatenate(
        [cx_slab(cov_x, offsets_x, me, rows), cx_slab(partner_cov, offsets_x, me ^ 1, rows)], axis=0
    )
    mixed = mixed_rows(recharge, slab, "gx")

    nyb = offsets_y.shape[0]
    col_block = (jnp.arange(nyb)[:, None] + offsets_y) % nyb
    picked = jnp.take(mixed.reshape(rows, nyb, BLK), col_block, axis=1)
    prior = jnp.einsum(
        "xrkc,rikc->xri",
        picked,
        cov_y.reshape(nyb, BLK, cov_y.shape[1], BLK),
        precision=precise,
        preferred_element_type=jnp.float32,
    ).reshape(rows, cols)
    return (recharge, prior)


def solution(mesh):
    return jax.shard_map(
        body,
        mesh=mesh,
        in_specs=(
            P(None, ("grp", "gx"), None),
            P(None, ("grp", "gx"), None),
            P(None, ("grp", "gx"), None),
            P(None, ("grp", "gx"), None),
            P(None, ("grp", "gx"), None),
            P(None, ("grp", "gx"), None),
            P(),
            P("gx", None, None),
            P(),
            P(),
            P(),
        ),
        out_specs=(P(("grp", "gx"), None), P(("grp", "gx"), None)),
        check_vma=False,
    )
```

```python
import jax
import jax.numpy as jnp
from jax import lax
from jax.experimental import pallas as pl
from jax.experimental.pallas import tpu as pltpu
from jax.sharding import PartitionSpec as P

BLK = 128
Z_CHUNK = 4

precise = lax.Precision.HIGH


def passed_along(value, axis, steps):
    count = lax.axis_size(axis)
    first, last = (max(0, -steps), min(count, count - steps))
    return lax.ppermute(value, axis, [(source, source + steps) for source in range(first, last)])


def coefs(flags, bit, speed, spread):
    on = (flags & bit) != 0
    lower = spread + jnp.where(on, speed, 0.0)
    upper = spread + jnp.where(on, 0.0, speed)
    return lower, upper


def stencil_kernel(w_ref, s_ref, sprev_ref, f_ref, vx_ref, vy_ref, vz_ref, d_ref, out_ref, to_prev_ref, edge_ref):
    c = pl.program_id(0)
    rows, cols = out_ref.shape
    sub = lax.broadcasted_iota(jnp.int32, (rows, cols), 0)
    lane = lax.broadcasted_iota(jnp.int32, (rows, cols), 1)

    @pl.when(c == 0)
    def _():
        out_ref[...] = jnp.zeros_like(out_ref)

    prev = jnp.where(c > 0, sprev_ref[0], 0.0)
    acc = jnp.zeros((rows, cols), jnp.float32)
    for j in range(s_ref.shape[0]):
        z = c * s_ref.shape[0] + j
        s = s_ref[j]
        f = f_ref[j]
        d = d_ref[j]
        lo_x, up_x = coefs(f, 1, vx_ref[j], d)
        to_prev_ref[0, pl.ds(z, 1), :] = s[0:1, :]
        to_prev_ref[1, pl.ds(z, 1), :] = lo_x[0:1, :]
        edge_ref[0, pl.ds(z, 1), :] = s[rows - 1:rows, :]
        edge_ref[1, pl.ds(z, 1), :] = up_x[0:1, :]
        lo_y, up_y = coefs(f, 2, vy_ref[j], d)
        lo_z, up_z = coefs(f, 4, vz_ref[j], d)
        s_xm = jnp.where(sub == 0, 0.0, pltpu.roll(s, 1, 0))
        jx = s - s_xm
        ax = -lo_x * jx
        ax_next = jnp.where(sub == rows - 1, 0.0, pltpu.roll(ax, rows - 1, 0))
        img = up_x * jx + ax_next
        s_ym = jnp.where(lane == 0, 0.0, pltpu.roll(s, 1, 1))
        jy = s - s_ym
        ay = -lo_y * jy
        ay_next = jnp.where(lane == cols - 1, 0.0, pltpu.roll(ay, cols - 1, 1))
        img = img + (up_y * jy + ay_next)
        jz = s - prev
        img = img + up_z * jz
        acc = acc + w_ref[z] * img
        w_before = jnp.where(z > 0, w_ref[jnp.maximum(z - 1, 0)], 0.0)
        acc = acc + w_before * (-lo_z * jz)
        prev = s
    out_ref[...] += acc


def stencil(layer_weight, s, f, vx, vy, vz, d):
    depth, rows, cols = s.shape
    zc = Z_CHUNK if depth % Z_CHUNK == 0 else depth
    block = pl.BlockSpec((zc, rows, cols), lambda c: (c, 0, 0))
    prev_block = pl.BlockSpec((1, rows, cols), lambda c: (jnp.maximum(c * zc - 1, 0), 0, 0))
    return pl.pallas_call(
        stencil_kernel,
        grid=(depth // zc,),
        in_specs=[
            pl.BlockSpec(memory_space=pltpu.SMEM),
            block,
            prev_block,
            block,
            block,
            block,
            block,
            block,
        ],
        out_specs=[
            pl.BlockSpec((rows, cols), lambda c: (0, 0)),
            pl.BlockSpec((2, depth, cols), lambda c: (0, 0, 0)),
            pl.BlockSpec((2, depth, cols), lambda c: (0, 0, 0)),
        ],
        out_shape=[
            jax.ShapeDtypeStruct((rows, cols), jnp.float32),
            jax.ShapeDtypeStruct((2, depth, cols), jnp.float32),
            jax.ShapeDtypeStruct((2, depth, cols), jnp.float32),
        ],
        compiler_params=pltpu.CompilerParams(dimension_semantics=("arbitrary",)),
    )(layer_weight, s, s, f, vx, vy, vz, d)


def gather_rounds(count):
    bits = []
    bit = count // 2
    while bit >= 2:
        bits.append(bit)
        bit //= 2
    if len(bits) < 2:
        return [[b] for b in bits]
    return [[bits[1], bits[0], bits[0] | bits[1]]] + [[b] for b in bits[2:]]


def cx_slab(cov_rows, offsets, device, rows):
    nxb = offsets.shape[0]
    global_rows = device * rows + jnp.arange(rows)
    row_block = global_rows // BLK
    target = (row_block[:, None] + offsets[row_block]) % nxb
    blocks = jnp.arange(nxb)
    hit = target[:, :, None, None] == blocks[None, None, :, None]
    slab = jnp.sum(jnp.where(hit, cov_rows.astype(jnp.float32)[:, :, None, :], 0.0), axis=1)
    return slab.reshape(rows, -1)


def mixed_rows(local, slab, axis):
    count = lax.axis_size(axis)
    me = lax.axis_index(axis)
    rows = local.shape[0]
    per_device = slab.reshape(slab.shape[0], count, rows)

    def product(piece, masks):
        cols = jnp.take(per_device, me ^ jnp.array(masks, jnp.int32), axis=1).reshape(slab.shape[0], -1)
        return jnp.dot(cols, piece.reshape(-1, piece.shape[-1]), precision=precise, preferred_element_type=jnp.float32)

    buf = local[None]
    entries = [0]
    total = product(buf, entries)
    for masks in gather_rounds(count):
        others = [lax.ppermute(buf, axis, [(i, i ^ m) for i in range(count)]) for m in masks]
        for m, other in zip(masks, others):
            total = total + product(other, [m ^ q for q in entries])
        buf = jnp.concatenate([buf] + others, axis=0)
        entries = entries + [m ^ q for m in masks for q in entries]
    own, for_partner = total[:rows], total[rows:]
    if count == 1:
        return own
    return own + lax.ppermute(for_partner, axis, [(i, i ^ 1) for i in range(count)])


def body(
    adjoint_state,
    speed_x,
    speed_y,
    speed_z,
    dispersion,
    face_flags,
    layer_weight,
    cov_x,
    offsets_x,
    cov_y,
    offsets_y,
):
    count = lax.axis_size("gx")
    me = lax.axis_index("gx")
    depth, rows, cols = adjoint_state.shape

    partial, to_prev, edge = stencil(layer_weight, adjoint_state, face_flags, speed_x, speed_y, speed_z, dispersion)
    last_s, up_x0 = edge[0], edge[1]
    from_next = passed_along(to_prev, "gx", -1)
    from_prev = passed_along(last_s, "gx", 1)

    corr_first = jnp.sum(layer_weight[:, None] * (-up_x0 * from_prev), axis=0)
    ax_next = -from_next[1] * (from_next[0] - last_s)
    corr_last = jnp.sum(layer_weight[:, None] * ax_next, axis=0)
    row = lax.broadcasted_iota(jnp.int32, (rows, cols), 0)
    recharge = partial + jnp.where(row == 0, corr_first[None, :], 0.0) + jnp.where(row == rows - 1, corr_last[None, :], 0.0)

    partner_cov = lax.ppermute(cov_x, "gx", [(i, i ^ 1) for i in range(count)]) if count > 1 else cov_x
    slab = jnp.concatenate(
        [cx_slab(cov_x, offsets_x, me, rows), cx_slab(partner_cov, offsets_x, me ^ 1, rows)], axis=0
    )
    mixed = mixed_rows(recharge, slab, "gx")

    nyb = offsets_y.shape[0]
    col_block = (jnp.arange(nyb)[:, None] + offsets_y) % nyb
    picked = jnp.take(mixed.reshape(rows, nyb, BLK), col_block, axis=1)
    prior = jnp.einsum(
        "xrkc,rikc->xri",
        picked,
        cov_y.reshape(nyb, BLK, cov_y.shape[1], BLK),
        precision=precise,
        preferred_element_type=jnp.float32,
    ).reshape(rows, cols)
    return (recharge, prior)


def solution(mesh):
    return jax.shard_map(
        body,
        mesh=mesh,
        in_specs=(
            P(None, ("grp", "gx"), None),
            P(None, ("grp", "gx"), None),
            P(None, ("grp", "gx"), None),
            P(None, ("grp", "gx"), None),
            P(None, ("grp", "gx"), None),
            P(None, ("grp", "gx"), None),
            P(),
            P("gx", None, None),
            P(),
            P(),
            P(),
        ),
        out_specs=(P(("grp", "gx"), None), P(("grp", "gx"), None)),
        check_vma=False,
    )
```

```python
import jax
import jax.numpy as jnp
from jax import lax
from jax.experimental import pallas as pl
from jax.experimental.pallas import tpu as pltpu
from jax.sharding import PartitionSpec as P

BLK = 128
Z_CHUNK = 4

precise = lax.Precision.HIGH


def passed_along(value, axis, steps):
    count = lax.axis_size(axis)
    first, last = (max(0, -steps), min(count, count - steps))
    return lax.ppermute(value, axis, [(source, source + steps) for source in range(first, last)])


def coefs(flags, bit, speed, spread):
    on = (flags & bit) != 0
    lower = spread + jnp.where(on, speed, 0.0)
    upper = spread + jnp.where(on, 0.0, speed)
    return lower, upper


def stencil_kernel(w_ref, s_ref, sprev_ref, f_ref, vx_ref, vy_ref, vz_ref, d_ref, out_ref, to_prev_ref, edge_ref):
    c = pl.program_id(0)
    rows, cols = out_ref.shape
    sub = lax.broadcasted_iota(jnp.int32, (rows, cols), 0)
    lane = lax.broadcasted_iota(jnp.int32, (rows, cols), 1)

    @pl.when(c == 0)
    def _():
        out_ref[...] = jnp.zeros_like(out_ref)

    prev = jnp.where(c > 0, sprev_ref[0], 0.0)
    acc = jnp.zeros((rows, cols), jnp.float32)
    for j in range(s_ref.shape[0]):
        z = c * s_ref.shape[0] + j
        s = s_ref[j]
        f = f_ref[j]
        d = d_ref[j]
        lo_x, up_x = coefs(f, 1, vx_ref[j], d)
        to_prev_ref[0, pl.ds(z, 1), :] = s[0:1, :]
        to_prev_ref[1, pl.ds(z, 1), :] = lo_x[0:1, :]
        edge_ref[0, pl.ds(z, 1), :] = s[rows - 1:rows, :]
        edge_ref[1, pl.ds(z, 1), :] = up_x[0:1, :]
        lo_y, up_y = coefs(f, 2, vy_ref[j], d)
        lo_z, up_z = coefs(f, 4, vz_ref[j], d)
        s_xm = jnp.where(sub == 0, 0.0, pltpu.roll(s, 1, 0))
        jx = s - s_xm
        ax = -lo_x * jx
        ax_next = jnp.where(sub == rows - 1, 0.0, pltpu.roll(ax, rows - 1, 0))
        img = up_x * jx + ax_next
        s_ym = jnp.where(lane == 0, 0.0, pltpu.roll(s, 1, 1))
        jy = s - s_ym
        ay = -lo_y * jy
        ay_next = jnp.where(lane == cols - 1, 0.0, pltpu.roll(ay, cols - 1, 1))
        img = img + (up_y * jy + ay_next)
        jz = s - prev
        img = img + up_z * jz
        acc = acc + w_ref[z] * img
        w_before = jnp.where(z > 0, w_ref[jnp.maximum(z - 1, 0)], 0.0)
        acc = acc + w_before * (-lo_z * jz)
        prev = s
    out_ref[...] += acc


def stencil(layer_weight, s, f, vx, vy, vz, d):
    depth, rows, cols = s.shape
    zc = Z_CHUNK if depth % Z_CHUNK == 0 else depth
    block = pl.BlockSpec((zc, rows, cols), lambda c: (c, 0, 0))
    prev_block = pl.BlockSpec((1, rows, cols), lambda c: (jnp.maximum(c * zc - 1, 0), 0, 0))
    return pl.pallas_call(
        stencil_kernel,
        grid=(depth // zc,),
        in_specs=[
            pl.BlockSpec(memory_space=pltpu.SMEM),
            block,
            prev_block,
            block,
            block,
            block,
            block,
            block,
        ],
        out_specs=[
            pl.BlockSpec((rows, cols), lambda c: (0, 0)),
            pl.BlockSpec((2, depth, cols), lambda c: (0, 0, 0)),
            pl.BlockSpec((2, depth, cols), lambda c: (0, 0, 0)),
        ],
        out_shape=[
            jax.ShapeDtypeStruct((rows, cols), jnp.float32),
            jax.ShapeDtypeStruct((2, depth, cols), jnp.float32),
            jax.ShapeDtypeStruct((2, depth, cols), jnp.float32),
        ],
        compiler_params=pltpu.CompilerParams(dimension_semantics=("arbitrary",)),
    )(layer_weight, s, s, f, vx, vy, vz, d)


def gather_rounds(count):
    bits = []
    bit = count // 2
    while bit >= 4:
        bits.append(bit)
        bit //= 2
    if len(bits) < 2:
        return [[b] for b in bits]
    return [[bits[1], bits[0], bits[0] | bits[1]]] + [[b] for b in bits[2:]]


def swap(value, axis, mask):
    count = lax.axis_size(axis)
    return lax.ppermute(value, axis, [(i, i ^ mask) for i in range(count)])


def cx_slab(cov_rows, offsets, device, rows):
    nxb = offsets.shape[0]
    global_rows = device * rows + jnp.arange(rows)
    row_block = global_rows // BLK
    target = (row_block[:, None] + offsets[row_block]) % nxb
    blocks = jnp.arange(nxb)
    hit = target[:, :, None, None] == blocks[None, None, :, None]
    slab = jnp.sum(jnp.where(hit, cov_rows.astype(jnp.float32)[:, :, None, :], 0.0), axis=1)
    return slab.reshape(rows, -1)


def mixed_rows(local, slab, axis):
    count = lax.axis_size(axis)
    me = lax.axis_index(axis)
    rows = local.shape[0]
    per_device = slab.reshape(slab.shape[0], count, rows)

    def product(piece, masks):
        cols = jnp.take(per_device, me ^ jnp.array(masks, jnp.int32), axis=1).reshape(slab.shape[0], -1)
        return jnp.dot(cols, piece.reshape(-1, piece.shape[-1]), precision=precise, preferred_element_type=jnp.float32)

    buf = local[None]
    entries = [0]
    total = product(buf, entries)
    for masks in gather_rounds(count):
        others = [swap(buf, axis, m) for m in masks]
        for m, other in zip(masks, others):
            total = total + product(other, [m ^ q for q in entries])
        buf = jnp.concatenate([buf] + others, axis=0)
        entries = entries + [m ^ q for m in masks for q in entries]
    parts = total.reshape(4, rows, total.shape[-1])
    got = swap(parts[1::2], axis, 1)
    near = parts[0::2] + got
    return near[0] + swap(near[1], axis, 2)


def body(
    adjoint_state,
    speed_x,
    speed_y,
    speed_z,
    dispersion,
    face_flags,
    layer_weight,
    cov_x,
    offsets_x,
    cov_y,
    offsets_y,
):
    count = lax.axis_size("gx")
    me = lax.axis_index("gx")
    depth, rows, cols = adjoint_state.shape

    partial, to_prev, edge = stencil(layer_weight, adjoint_state, face_flags, speed_x, speed_y, speed_z, dispersion)
    last_s, up_x0 = edge[0], edge[1]
    from_next = passed_along(to_prev, "gx", -1)
    from_prev = passed_along(last_s, "gx", 1)

    corr_first = jnp.sum(layer_weight[:, None] * (-up_x0 * from_prev), axis=0)
    ax_next = -from_next[1] * (from_next[0] - last_s)
    corr_last = jnp.sum(layer_weight[:, None] * ax_next, axis=0)
    row = lax.broadcasted_iota(jnp.int32, (rows, cols), 0)
    recharge = partial + jnp.where(row == 0, corr_first[None, :], 0.0) + jnp.where(row == rows - 1, corr_last[None, :], 0.0)

    pair_cov = jnp.stack([cov_x, swap(cov_x, "gx", 1)])
    quad_cov = jnp.concatenate([pair_cov, swap(pair_cov, "gx", 2)], axis=0)
    slab = jnp.concatenate([cx_slab(quad_cov[m], offsets_x, me ^ m, rows) for m in range(4)], axis=0)
    mixed = mixed_rows(recharge, slab, "gx")

    nyb = offsets_y.shape[0]
    col_block = (jnp.arange(nyb)[:, None] + offsets_y) % nyb
    picked = jnp.take(mixed.reshape(rows, nyb, BLK), col_block, axis=1)
    prior = jnp.einsum(
        "xrkc,rikc->xri",
        picked,
        cov_y.reshape(nyb, BLK, cov_y.shape[1], BLK),
        precision=precise,
        preferred_element_type=jnp.float32,
    ).reshape(rows, cols)
    return (recharge, prior)


def solution(mesh):
    return jax.shard_map(
        body,
        mesh=mesh,
        in_specs=(
            P(None, ("grp", "gx"), None),
            P(None, ("grp", "gx"), None),
            P(None, ("grp", "gx"), None),
            P(None, ("grp", "gx"), None),
            P(None, ("grp", "gx"), None),
            P(None, ("grp", "gx"), None),
            P(),
            P("gx", None, None),
            P(),
            P(),
            P(),
        ),
        out_specs=(P(("grp", "gx"), None), P(("grp", "gx"), None)),
        check_vma=False,
    )
```

```python
import jax
import jax.numpy as jnp
from jax import lax
from jax.experimental import pallas as pl
from jax.experimental.pallas import tpu as pltpu
from jax.sharding import PartitionSpec as P

BLK = 128
Z_CHUNK = 8

precise = lax.Precision.HIGH


def passed_along(value, axis, steps):
    count = lax.axis_size(axis)
    first, last = (max(0, -steps), min(count, count - steps))
    return lax.ppermute(value, axis, [(source, source + steps) for source in range(first, last)])


def coefs(flags, bit, speed, spread):
    on = (flags & bit) != 0
    lower = spread + jnp.where(on, speed, 0.0)
    upper = spread + jnp.where(on, 0.0, speed)
    return lower, upper


def stencil_kernel(w_ref, s_ref, sprev_ref, f_ref, vx_ref, vy_ref, vz_ref, d_ref, out_ref, to_prev_ref, last_ref, up_ref):
    c = pl.program_id(0)
    rows, cols = out_ref.shape
    sub = lax.broadcasted_iota(jnp.int32, (rows, cols), 0)
    lane = lax.broadcasted_iota(jnp.int32, (rows, cols), 1)

    @pl.when(c == 0)
    def _():
        out_ref[...] = jnp.zeros_like(out_ref)

    prev = jnp.where(c > 0, sprev_ref[0], 0.0)
    acc = jnp.zeros((rows, cols), jnp.float32)
    for j in range(s_ref.shape[0]):
        z = c * s_ref.shape[0] + j
        s = s_ref[j]
        f = f_ref[j]
        d = d_ref[j]
        lo_x, up_x = coefs(f, 1, vx_ref[j], d)
        to_prev_ref[0, pl.ds(z, 1), :] = s[0:1, :]
        to_prev_ref[1, pl.ds(z, 1), :] = lo_x[0:1, :]
        last_ref[pl.ds(z, 1), :] = s[rows - 1:rows, :]
        up_ref[pl.ds(z, 1), :] = up_x[0:1, :]
        lo_y, up_y = coefs(f, 2, vy_ref[j], d)
        lo_z, up_z = coefs(f, 4, vz_ref[j], d)
        s_xm = jnp.where(sub == 0, 0.0, pltpu.roll(s, 1, 0))
        jx = s - s_xm
        ax = -lo_x * jx
        ax_next = jnp.where(sub == rows - 1, 0.0, pltpu.roll(ax, rows - 1, 0))
        img = up_x * jx + ax_next
        s_ym = jnp.where(lane == 0, 0.0, pltpu.roll(s, 1, 1))
        jy = s - s_ym
        ay = -lo_y * jy
        ay_next = jnp.where(lane == cols - 1, 0.0, pltpu.roll(ay, cols - 1, 1))
        img = img + (up_y * jy + ay_next)
        jz = s - prev
        img = img + up_z * jz
        acc = acc + w_ref[z] * img
        w_before = jnp.where(z > 0, w_ref[jnp.maximum(z - 1, 0)], 0.0)
        acc = acc + w_before * (-lo_z * jz)
        prev = s
    out_ref[...] += acc


def stencil(layer_weight, s, f, vx, vy, vz, d):
    depth, rows, cols = s.shape
    zc = Z_CHUNK if depth % Z_CHUNK == 0 else depth
    block = pl.BlockSpec((zc, rows, cols), lambda c: (c, 0, 0))
    prev_block = pl.BlockSpec((1, rows, cols), lambda c: (jnp.maximum(c * zc - 1, 0), 0, 0))
    return pl.pallas_call(
        stencil_kernel,
        grid=(depth // zc,),
        in_specs=[
            pl.BlockSpec(memory_space=pltpu.SMEM),
            block,
            prev_block,
            block,
            block,
            block,
            block,
            block,
        ],
        out_specs=[
            pl.BlockSpec((rows, cols), lambda c: (0, 0)),
            pl.BlockSpec((2, depth, cols), lambda c: (0, 0, 0)),
            pl.BlockSpec((depth, cols), lambda c: (0, 0)),
            pl.BlockSpec((depth, cols), lambda c: (0, 0)),
        ],
        out_shape=[
            jax.ShapeDtypeStruct((rows, cols), jnp.float32),
            jax.ShapeDtypeStruct((2, depth, cols), jnp.float32),
            jax.ShapeDtypeStruct((depth, cols), jnp.float32),
            jax.ShapeDtypeStruct((depth, cols), jnp.float32),
        ],
        compiler_params=pltpu.CompilerParams(dimension_semantics=("arbitrary",)),
    )(layer_weight, s, s, f, vx, vy, vz, d)


def gather_rounds(count):
    bits = []
    bit = count // 2
    while bit >= 4:
        bits.append(bit)
        bit //= 2
    if len(bits) < 2:
        return [[b] for b in bits]
    return [[bits[1], bits[0], bits[0] | bits[1]]] + [[b] for b in bits[2:]]


def swap(value, axis, mask):
    count = lax.axis_size(axis)
    return lax.ppermute(value, axis, [(i, i ^ mask) for i in range(count)])


def cx_slab(cov_rows, offsets, device, rows):
    nxb = offsets.shape[0]
    global_rows = device * rows + jnp.arange(rows)
    row_block = global_rows // BLK
    target = (row_block[:, None] + offsets[row_block]) % nxb
    blocks = jnp.arange(nxb)
    hit = target[:, :, None, None] == blocks[None, None, :, None]
    slab = jnp.sum(jnp.where(hit, cov_rows.astype(jnp.float32)[:, :, None, :], 0.0), axis=1)
    return slab.reshape(rows, -1)


def mixed_rows(local, slab, axis):
    count = lax.axis_size(axis)
    me = lax.axis_index(axis)
    rows = local.shape[0]
    per_device = slab.reshape(slab.shape[0], count, rows)

    def product(piece, masks):
        cols = jnp.take(per_device, me ^ jnp.array(masks, jnp.int32), axis=1).reshape(slab.shape[0], -1)
        return jnp.dot(cols, piece.reshape(-1, piece.shape[-1]), precision=precise, preferred_element_type=jnp.float32)

    buf = local[None]
    entries = [0]
    total = product(buf, entries)
    for masks in gather_rounds(count):
        others = [swap(buf, axis, m) for m in masks]
        for m, other in zip(masks, others):
            total = total + product(other, [m ^ q for q in entries])
        buf = jnp.concatenate([buf] + others, axis=0)
        entries = entries + [m ^ q for m in masks for q in entries]
    parts = total.reshape(4, rows, total.shape[-1])
    got = swap(parts[1::2], axis, 1)
    near = parts[0::2] + got
    return near[0] + swap(near[1], axis, 2)


def body(
    adjoint_state,
    speed_x,
    speed_y,
    speed_z,
    dispersion,
    face_flags,
    layer_weight,
    cov_x,
    offsets_x,
    cov_y,
    offsets_y,
):
    count = lax.axis_size("gx")
    me = lax.axis_index("gx")
    depth, rows, cols = adjoint_state.shape

    partial, to_prev, last_s, up_x0 = stencil(
        layer_weight, adjoint_state, face_flags, speed_x, speed_y, speed_z, dispersion
    )
    from_next = passed_along(to_prev, "gx", -1)
    from_prev = passed_along(last_s, "gx", 1)

    corr_first = jnp.sum(layer_weight[:, None] * (-up_x0 * from_prev), axis=0)
    ax_next = -from_next[1] * (from_next[0] - last_s)
    corr_last = jnp.sum(layer_weight[:, None] * ax_next, axis=0)
    row = lax.broadcasted_iota(jnp.int32, (rows, cols), 0)
    recharge = partial + jnp.where(row == 0, corr_first[None, :], 0.0) + jnp.where(row == rows - 1, corr_last[None, :], 0.0)

    own_slab = cx_slab(cov_x, offsets_x, me, rows)
    pair_slab = jnp.concatenate([own_slab, swap(own_slab, "gx", 1)], axis=0)
    slab = jnp.concatenate([pair_slab, swap(pair_slab, "gx", 2)], axis=0)
    mixed = mixed_rows(recharge, slab, "gx")

    nyb = offsets_y.shape[0]
    col_block = (jnp.arange(nyb)[:, None] + offsets_y) % nyb
    picked = jnp.take(mixed.reshape(rows, nyb, BLK), col_block, axis=1)
    prior = jnp.einsum(
        "xrkc,rikc->xri",
        picked,
        cov_y.reshape(nyb, BLK, cov_y.shape[1], BLK),
        precision=precise,
        preferred_element_type=jnp.float32,
    ).reshape(rows, cols)
    return (recharge, prior)


def solution(mesh):
    return jax.shard_map(
        body,
        mesh=mesh,
        in_specs=(
            P(None, ("grp", "gx"), None),
            P(None, ("grp", "gx"), None),
            P(None, ("grp", "gx"), None),
            P(None, ("grp", "gx"), None),
            P(None, ("grp", "gx"), None),
            P(None, ("grp", "gx"), None),
            P(),
            P("gx", None, None),
            P(),
            P(),
            P(),
        ),
        out_specs=(P(("grp", "gx"), None), P(("grp", "gx"), None)),
        check_vma=False,
    )
```

```python
import jax
import jax.numpy as jnp
from jax import lax
from jax.experimental import pallas as pl
from jax.experimental.pallas import tpu as pltpu
from jax.sharding import PartitionSpec as P

BLK = 128
Z_CHUNK = 8

precise = lax.Precision.HIGH


def passed_along(value, axis, steps):
    count = lax.axis_size(axis)
    first, last = (max(0, -steps), min(count, count - steps))
    return lax.ppermute(value, axis, [(source, source + steps) for source in range(first, last)])


def coefs(flags, bit, speed, spread):
    on = (flags & bit) != 0
    lower = spread + jnp.where(on, speed, 0.0)
    upper = spread + jnp.where(on, 0.0, speed)
    return lower, upper


def stencil_kernel(w_ref, s_ref, sprev_ref, f_ref, vx_ref, vy_ref, vz_ref, d_ref, out_ref, to_prev_ref, last_ref, up_ref):
    c = pl.program_id(0)
    rows, cols = out_ref.shape
    sub = lax.broadcasted_iota(jnp.int32, (rows, cols), 0)
    lane = lax.broadcasted_iota(jnp.int32, (rows, cols), 1)

    @pl.when(c == 0)
    def _():
        out_ref[...] = jnp.zeros_like(out_ref)

    prev = jnp.where(c > 0, sprev_ref[0], 0.0)
    acc = jnp.zeros((rows, cols), jnp.float32)
    for j in range(s_ref.shape[0]):
        z = c * s_ref.shape[0] + j
        s = s_ref[j]
        f = f_ref[j]
        d = d_ref[j]
        lo_x, up_x = coefs(f, 1, vx_ref[j], d)
        to_prev_ref[0, pl.ds(z, 1), :] = s[0:1, :]
        to_prev_ref[1, pl.ds(z, 1), :] = lo_x[0:1, :]
        last_ref[pl.ds(z, 1), :] = s[rows - 1:rows, :]
        up_ref[pl.ds(z, 1), :] = up_x[0:1, :]
        lo_y, up_y = coefs(f, 2, vy_ref[j], d)
        lo_z, up_z = coefs(f, 4, vz_ref[j], d)
        s_xm = jnp.where(sub == 0, 0.0, pltpu.roll(s, 1, 0))
        jx = s - s_xm
        ax = -lo_x * jx
        ax_next = jnp.where(sub == rows - 1, 0.0, pltpu.roll(ax, rows - 1, 0))
        img = up_x * jx + ax_next
        s_ym = jnp.where(lane == 0, 0.0, pltpu.roll(s, 1, 1))
        jy = s - s_ym
        ay = -lo_y * jy
        ay_next = jnp.where(lane == cols - 1, 0.0, pltpu.roll(ay, cols - 1, 1))
        img = img + (up_y * jy + ay_next)
        jz = s - prev
        img = img + up_z * jz
        acc = acc + w_ref[z] * img
        w_before = jnp.where(z > 0, w_ref[jnp.maximum(z - 1, 0)], 0.0)
        acc = acc + w_before * (-lo_z * jz)
        prev = s
    out_ref[...] += acc


def stencil(layer_weight, s, f, vx, vy, vz, d):
    depth, rows, cols = s.shape
    zc = Z_CHUNK if depth % Z_CHUNK == 0 else depth
    block = pl.BlockSpec((zc, rows, cols), lambda c: (c, 0, 0))
    prev_block = pl.BlockSpec((1, rows, cols), lambda c: (jnp.maximum(c * zc - 1, 0), 0, 0))
    return pl.pallas_call(
        stencil_kernel,
        grid=(depth // zc,),
        in_specs=[
            pl.BlockSpec(memory_space=pltpu.SMEM),
            block,
            prev_block,
            block,
            block,
            block,
            block,
            block,
        ],
        out_specs=[
            pl.BlockSpec((rows, cols), lambda c: (0, 0)),
            pl.BlockSpec((2, depth, cols), lambda c: (0, 0, 0)),
            pl.BlockSpec((depth, cols), lambda c: (0, 0)),
            pl.BlockSpec((depth, cols), lambda c: (0, 0)),
        ],
        out_shape=[
            jax.ShapeDtypeStruct((rows, cols), jnp.float32),
            jax.ShapeDtypeStruct((2, depth, cols), jnp.float32),
            jax.ShapeDtypeStruct((depth, cols), jnp.float32),
            jax.ShapeDtypeStruct((depth, cols), jnp.float32),
        ],
        compiler_params=pltpu.CompilerParams(dimension_semantics=("arbitrary",)),
    )(layer_weight, s, s, f, vx, vy, vz, d)


def fix_kernel(w_ref, partial_ref, up_ref, prev_ref, next_ref, last_ref, out_ref):
    rows, cols = partial_ref.shape
    w = w_ref[...]
    corr_first = jnp.sum(w * (-up_ref[...] * prev_ref[...]), axis=0, keepdims=True)
    ax_next = -next_ref[1] * (next_ref[0] - last_ref[...])
    corr_last = jnp.sum(w * ax_next, axis=0, keepdims=True)
    row = lax.broadcasted_iota(jnp.int32, (rows, cols), 0)
    out_ref[...] = (
        partial_ref[...] + jnp.where(row == 0, corr_first, 0.0) + jnp.where(row == rows - 1, corr_last, 0.0)
    )


def corrected(w_col, partial, up_x0, from_prev, from_next, last_s):
    return pl.pallas_call(
        fix_kernel,
        out_shape=jax.ShapeDtypeStruct(partial.shape, jnp.float32),
    )(w_col, partial, up_x0, from_prev, from_next, last_s)


def gather_rounds(count):
    bits = []
    bit = count // 2
    while bit >= 4:
        bits.append(bit)
        bit //= 2
    if len(bits) < 2:
        return [[b] for b in bits]
    return [[bits[1], bits[0], bits[0] | bits[1]]] + [[b] for b in bits[2:]]


def swap(value, axis, mask):
    count = lax.axis_size(axis)
    return lax.ppermute(value, axis, [(i, i ^ mask) for i in range(count)])


def cx_slab(cov_rows, offsets, device, rows):
    nxb = offsets.shape[0]
    global_rows = device * rows + jnp.arange(rows)
    row_block = global_rows // BLK
    target = (row_block[:, None] + offsets[row_block]) % nxb
    blocks = jnp.arange(nxb)
    hit = target[:, :, None, None] == blocks[None, None, :, None]
    slab = jnp.sum(jnp.where(hit, cov_rows.astype(jnp.float32)[:, :, None, :], 0.0), axis=1)
    return slab.reshape(rows, -1)


def mixed_rows(local, slab, axis):
    count = lax.axis_size(axis)
    me = lax.axis_index(axis)
    rows = local.shape[0]
    per_device = slab.reshape(slab.shape[0], count, rows)

    def product(piece, masks):
        cols = jnp.take(per_device, me ^ jnp.array(masks, jnp.int32), axis=1).reshape(slab.shape[0], -1)
        return jnp.dot(cols, piece.reshape(-1, piece.shape[-1]), precision=precise, preferred_element_type=jnp.float32)

    buf = local[None]
    entries = [0]
    total = product(buf, entries)
    for masks in gather_rounds(count):
        others = [swap(buf, axis, m) for m in masks]
        for m, other in zip(masks, others):
            total = total + product(other, [m ^ q for q in entries])
        buf = jnp.concatenate([buf] + others, axis=0)
        entries = entries + [m ^ q for m in masks for q in entries]
    parts = total.reshape(4, rows, total.shape[-1])
    got = swap(parts[1::2], axis, 1)
    near = parts[0::2] + got
    return near[0] + swap(near[1], axis, 2)


def body(
    adjoint_state,
    speed_x,
    speed_y,
    speed_z,
    dispersion,
    face_flags,
    layer_weight,
    cov_x,
    offsets_x,
    cov_y,
    offsets_y,
):
    count = lax.axis_size("gx")
    me = lax.axis_index("gx")
    depth, rows, cols = adjoint_state.shape

    partial, to_prev, last_s, up_x0 = stencil(
        layer_weight, adjoint_state, face_flags, speed_x, speed_y, speed_z, dispersion
    )
    from_next = passed_along(to_prev, "gx", -1)
    from_prev = passed_along(last_s, "gx", 1)

    recharge = corrected(layer_weight[:, None], partial, up_x0, from_prev, from_next, last_s)

    own_slab = cx_slab(cov_x, offsets_x, me, rows)
    slab = jnp.concatenate([own_slab] + [swap(own_slab, "gx", m) for m in (1, 2, 3)], axis=0)
    mixed = mixed_rows(recharge, slab, "gx")

    nyb = offsets_y.shape[0]
    col_block = (jnp.arange(nyb)[:, None] + offsets_y) % nyb
    picked = jnp.take(mixed.reshape(rows, nyb, BLK), col_block, axis=1)
    prior = jnp.einsum(
        "xrkc,rikc->xri",
        picked,
        cov_y.reshape(nyb, BLK, cov_y.shape[1], BLK),
        precision=precise,
        preferred_element_type=jnp.float32,
    ).reshape(rows, cols)
    return (recharge, prior)


def solution(mesh):
    return jax.shard_map(
        body,
        mesh=mesh,
        in_specs=(
            P(None, ("grp", "gx"), None),
            P(None, ("grp", "gx"), None),
            P(None, ("grp", "gx"), None),
            P(None, ("grp", "gx"), None),
            P(None, ("grp", "gx"), None),
            P(None, ("grp", "gx"), None),
            P(),
            P("gx", None, None),
            P(),
            P(),
            P(),
        ),
        out_specs=(P(("grp", "gx"), None), P(("grp", "gx"), None)),
        check_vma=False,
    )
```

```python
import jax
import jax.numpy as jnp
from jax import lax
from jax.experimental import pallas as pl
from jax.experimental.pallas import tpu as pltpu
from jax.sharding import PartitionSpec as P

BLK = 128
Z_CHUNK = 8

precise = lax.Precision.HIGH


def passed_along(value, axis, steps):
    count = lax.axis_size(axis)
    first, last = (max(0, -steps), min(count, count - steps))
    return lax.ppermute(value, axis, [(source, source + steps) for source in range(first, last)])


def coefs(flags, bit, speed, spread):
    on = (flags & bit) != 0
    lower = spread + jnp.where(on, speed, 0.0)
    upper = spread + jnp.where(on, 0.0, speed)
    return lower, upper


def stencil_kernel(w_ref, s_ref, sprev_ref, f_ref, vx_ref, vy_ref, vz_ref, d_ref, out_ref, to_prev_ref, last_ref, up_ref):
    c = pl.program_id(0)
    rows, cols = out_ref.shape
    sub = lax.broadcasted_iota(jnp.int32, (rows, cols), 0)
    lane = lax.broadcasted_iota(jnp.int32, (rows, cols), 1)

    @pl.when(c == 0)
    def _():
        out_ref[...] = jnp.zeros_like(out_ref)

    prev = jnp.where(c > 0, sprev_ref[0], 0.0)
    acc = jnp.zeros((rows, cols), jnp.float32)
    for j in range(s_ref.shape[0]):
        z = c * s_ref.shape[0] + j
        s = s_ref[j]
        f = f_ref[j]
        d = d_ref[j]
        lo_x, up_x = coefs(f, 1, vx_ref[j], d)
        to_prev_ref[0, pl.ds(z, 1), :] = s[0:1, :]
        to_prev_ref[1, pl.ds(z, 1), :] = lo_x[0:1, :]
        last_ref[pl.ds(z, 1), :] = s[rows - 1:rows, :]
        up_ref[pl.ds(z, 1), :] = up_x[0:1, :]
        lo_y, up_y = coefs(f, 2, vy_ref[j], d)
        lo_z, up_z = coefs(f, 4, vz_ref[j], d)
        s_xm = jnp.where(sub == 0, 0.0, pltpu.roll(s, 1, 0))
        jx = s - s_xm
        ax = -lo_x * jx
        ax_next = jnp.where(sub == rows - 1, 0.0, pltpu.roll(ax, rows - 1, 0))
        img = up_x * jx + ax_next
        s_ym = jnp.where(lane == 0, 0.0, pltpu.roll(s, 1, 1))
        jy = s - s_ym
        ay = -lo_y * jy
        ay_next = jnp.where(lane == cols - 1, 0.0, pltpu.roll(ay, cols - 1, 1))
        img = img + (up_y * jy + ay_next)
        jz = s - prev
        img = img + up_z * jz
        acc = acc + w_ref[z] * img
        w_before = jnp.where(z > 0, w_ref[jnp.maximum(z - 1, 0)], 0.0)
        acc = acc + w_before * (-lo_z * jz)
        prev = s
    out_ref[...] += acc


def stencil(layer_weight, s, f, vx, vy, vz, d):
    depth, rows, cols = s.shape
    zc = Z_CHUNK if depth % Z_CHUNK == 0 else depth
    block = pl.BlockSpec((zc, rows, cols), lambda c: (c, 0, 0))
    prev_block = pl.BlockSpec((1, rows, cols), lambda c: (jnp.maximum(c * zc - 1, 0), 0, 0))
    return pl.pallas_call(
        stencil_kernel,
        grid=(depth // zc,),
        in_specs=[
            pl.BlockSpec(memory_space=pltpu.SMEM),
            block,
            prev_block,
            block,
            block,
            block,
            block,
            block,
        ],
        out_specs=[
            pl.BlockSpec((rows, cols), lambda c: (0, 0)),
            pl.BlockSpec((2, depth, cols), lambda c: (0, 0, 0)),
            pl.BlockSpec((depth, cols), lambda c: (0, 0)),
            pl.BlockSpec((depth, cols), lambda c: (0, 0)),
        ],
        out_shape=[
            jax.ShapeDtypeStruct((rows, cols), jnp.float32),
            jax.ShapeDtypeStruct((2, depth, cols), jnp.float32),
            jax.ShapeDtypeStruct((depth, cols), jnp.float32),
            jax.ShapeDtypeStruct((depth, cols), jnp.float32),
        ],
        compiler_params=pltpu.CompilerParams(dimension_semantics=("arbitrary",)),
    )(layer_weight, s, s, f, vx, vy, vz, d)


def fix_kernel(w_ref, partial_ref, up_ref, prev_ref, next_ref, last_ref, out_ref):
    rows, cols = partial_ref.shape
    w = w_ref[...]
    corr_first = jnp.sum(w * (-up_ref[...] * prev_ref[...]), axis=0, keepdims=True)
    ax_next = -next_ref[1] * (next_ref[0] - last_ref[...])
    corr_last = jnp.sum(w * ax_next, axis=0, keepdims=True)
    row = lax.broadcasted_iota(jnp.int32, (rows, cols), 0)
    out_ref[...] = (
        partial_ref[...] + jnp.where(row == 0, corr_first, 0.0) + jnp.where(row == rows - 1, corr_last, 0.0)
    )


def corrected(w_col, partial, up_x0, from_prev, from_next, last_s):
    return pl.pallas_call(
        fix_kernel,
        out_shape=jax.ShapeDtypeStruct(partial.shape, jnp.float32),
    )(w_col, partial, up_x0, from_prev, from_next, last_s)


def gather_rounds(count):
    bits = []
    bit = count // 2
    while bit >= 4:
        bits.append(bit)
        bit //= 2
    if len(bits) < 2:
        return [[b] for b in bits]
    return [[bits[1], bits[0], bits[0] | bits[1]]] + [[b] for b in bits[2:]]


def swap(value, axis, mask):
    count = lax.axis_size(axis)
    return lax.ppermute(value, axis, [(i, i ^ mask) for i in range(count)])


def cx_slab(cov_rows, offsets, device, rows):
    nxb = offsets.shape[0]
    global_rows = device * rows + jnp.arange(rows)
    row_block = global_rows // BLK
    target = (row_block[:, None] + offsets[row_block]) % nxb
    blocks = jnp.arange(nxb)
    hit = target[:, :, None, None] == blocks[None, None, :, None]
    slab = jnp.sum(jnp.where(hit, cov_rows.astype(jnp.float32)[:, :, None, :], 0.0), axis=1)
    return slab.reshape(rows, -1)


def mixed_rows(local, slab, axis):
    count = lax.axis_size(axis)
    me = lax.axis_index(axis)
    rows = local.shape[0]
    per_device = slab.reshape(slab.shape[0], count, rows)
    relative = jnp.take(per_device, me ^ jnp.arange(count, dtype=jnp.int32), axis=1)

    def product(piece, masks):
        cols = jnp.concatenate([relative[:, m, :] for m in masks], axis=1)
        return jnp.dot(cols, piece.reshape(-1, piece.shape[-1]), precision=precise, preferred_element_type=jnp.float32)

    buf = local[None]
    entries = [0]
    total = product(buf, entries)
    for masks in gather_rounds(count):
        others = [swap(buf, axis, m) for m in masks]
        for m, other in zip(masks, others):
            total = total + product(other, [m ^ q for q in entries])
        buf = jnp.concatenate([buf] + others, axis=0)
        entries = entries + [m ^ q for m in masks for q in entries]
    parts = total.reshape(4, rows, total.shape[-1])
    got = swap(parts[1::2], axis, 1)
    near = parts[0::2] + got
    return near[0] + swap(near[1], axis, 2)


def body(
    adjoint_state,
    speed_x,
    speed_y,
    speed_z,
    dispersion,
    face_flags,
    layer_weight,
    cov_x,
    offsets_x,
    cov_y,
    offsets_y,
):
    count = lax.axis_size("gx")
    me = lax.axis_index("gx")
    depth, rows, cols = adjoint_state.shape

    partial, to_prev, last_s, up_x0 = stencil(
        layer_weight, adjoint_state, face_flags, speed_x, speed_y, speed_z, dispersion
    )
    from_next = passed_along(to_prev, "gx", -1)
    from_prev = passed_along(last_s, "gx", 1)

    recharge = corrected(layer_weight[:, None], partial, up_x0, from_prev, from_next, last_s)

    own_slab = cx_slab(cov_x, offsets_x, me, rows)
    slab = jnp.concatenate([own_slab] + [swap(own_slab, "gx", m) for m in (1, 2, 3)], axis=0)
    mixed = mixed_rows(recharge, slab, "gx")

    nyb = offsets_y.shape[0]
    col_block = (jnp.arange(nyb)[:, None] + offsets_y) % nyb
    picked = jnp.take(mixed.reshape(rows, nyb, BLK), col_block, axis=1)
    prior = jnp.einsum(
        "xrkc,rikc->xri",
        picked,
        cov_y.reshape(nyb, BLK, cov_y.shape[1], BLK),
        precision=precise,
        preferred_element_type=jnp.float32,
    ).reshape(rows, cols)
    return (recharge, prior)


def solution(mesh):
    return jax.shard_map(
        body,
        mesh=mesh,
        in_specs=(
            P(None, ("grp", "gx"), None),
            P(None, ("grp", "gx"), None),
            P(None, ("grp", "gx"), None),
            P(None, ("grp", "gx"), None),
            P(None, ("grp", "gx"), None),
            P(None, ("grp", "gx"), None),
            P(),
            P("gx", None, None),
            P(),
            P(),
            P(),
        ),
        out_specs=(P(("grp", "gx"), None), P(("grp", "gx"), None)),
        check_vma=False,
    )
```

```python
import jax
import jax.numpy as jnp
from jax import lax
from jax.experimental import pallas as pl
from jax.experimental.pallas import tpu as pltpu
from jax.sharding import PartitionSpec as P

BLK = 128
Z_CHUNK = 8

precise = lax.Precision.HIGH


def passed_along(value, axis, steps):
    count = lax.axis_size(axis)
    first, last = (max(0, -steps), min(count, count - steps))
    return lax.ppermute(value, axis, [(source, source + steps) for source in range(first, last)])


def coefs(flags, bit, speed, spread):
    on = (flags & bit) != 0
    lower = spread + jnp.where(on, speed, 0.0)
    upper = spread + jnp.where(on, 0.0, speed)
    return lower, upper


def stencil_kernel(w_ref, s_ref, sprev_ref, f_ref, vx_ref, vy_ref, vz_ref, d_ref, out_ref, to_prev_ref, last_ref, up_ref):
    c = pl.program_id(0)
    rows, cols = out_ref.shape
    sub = lax.broadcasted_iota(jnp.int32, (rows, cols), 0)
    lane = lax.broadcasted_iota(jnp.int32, (rows, cols), 1)

    @pl.when(c == 0)
    def _():
        out_ref[...] = jnp.zeros_like(out_ref)

    prev = jnp.where(c > 0, sprev_ref[0], 0.0)
    acc = jnp.zeros((rows, cols), jnp.float32)
    for j in range(s_ref.shape[0]):
        z = c * s_ref.shape[0] + j
        s = s_ref[j]
        f = f_ref[j]
        d = d_ref[j]
        lo_x, up_x = coefs(f, 1, vx_ref[j], d)
        to_prev_ref[0, pl.ds(z, 1), :] = s[0:1, :]
        to_prev_ref[1, pl.ds(z, 1), :] = lo_x[0:1, :]
        last_ref[pl.ds(z, 1), :] = s[rows - 1:rows, :]
        up_ref[pl.ds(z, 1), :] = up_x[0:1, :]
        lo_y, up_y = coefs(f, 2, vy_ref[j], d)
        lo_z, up_z = coefs(f, 4, vz_ref[j], d)
        s_xm = jnp.where(sub == 0, 0.0, pltpu.roll(s, 1, 0))
        jx = s - s_xm
        ax = lo_x * jx
        ax_next = jnp.where(sub == rows - 1, 0.0, pltpu.roll(ax, rows - 1, 0))
        img = up_x * jx - ax_next
        s_ym = jnp.where(lane == 0, 0.0, pltpu.roll(s, 1, 1))
        jy = s - s_ym
        ay = lo_y * jy
        ay_next = jnp.where(lane == cols - 1, 0.0, pltpu.roll(ay, cols - 1, 1))
        img = img + (up_y * jy - ay_next)
        jz = s - prev
        img = img + up_z * jz
        acc = acc + w_ref[z] * img
        w_before = jnp.where(z > 0, w_ref[jnp.maximum(z - 1, 0)], 0.0)
        acc = acc - w_before * (lo_z * jz)
        prev = s
    out_ref[...] += acc


def stencil(layer_weight, s, f, vx, vy, vz, d):
    depth, rows, cols = s.shape
    zc = Z_CHUNK if depth % Z_CHUNK == 0 else depth
    block = pl.BlockSpec((zc, rows, cols), lambda c: (c, 0, 0))
    prev_block = pl.BlockSpec((1, rows, cols), lambda c: (jnp.maximum(c * zc - 1, 0), 0, 0))
    return pl.pallas_call(
        stencil_kernel,
        grid=(depth // zc,),
        in_specs=[
            pl.BlockSpec(memory_space=pltpu.SMEM),
            block,
            prev_block,
            block,
            block,
            block,
            block,
            block,
        ],
        out_specs=[
            pl.BlockSpec((rows, cols), lambda c: (0, 0)),
            pl.BlockSpec((2, depth, cols), lambda c: (0, 0, 0)),
            pl.BlockSpec((depth, cols), lambda c: (0, 0)),
            pl.BlockSpec((depth, cols), lambda c: (0, 0)),
        ],
        out_shape=[
            jax.ShapeDtypeStruct((rows, cols), jnp.float32),
            jax.ShapeDtypeStruct((2, depth, cols), jnp.float32),
            jax.ShapeDtypeStruct((depth, cols), jnp.float32),
            jax.ShapeDtypeStruct((depth, cols), jnp.float32),
        ],
        compiler_params=pltpu.CompilerParams(dimension_semantics=("arbitrary",)),
    )(layer_weight, s, s, f, vx, vy, vz, d)


def fix_kernel(w_ref, partial_ref, up_ref, prev_ref, next_ref, last_ref, out_ref):
    rows, cols = partial_ref.shape
    depth = up_ref.shape[0]
    corr_first = jnp.zeros((1, cols), jnp.float32)
    corr_last = jnp.zeros((1, cols), jnp.float32)
    for z in range(depth):
        w = w_ref[z]
        corr_first = corr_first - w * (up_ref[pl.ds(z, 1), :] * prev_ref[pl.ds(z, 1), :])
        jump = next_ref[0, pl.ds(z, 1), :] - last_ref[pl.ds(z, 1), :]
        corr_last = corr_last - w * (next_ref[1, pl.ds(z, 1), :] * jump)
    row = lax.broadcasted_iota(jnp.int32, (rows, cols), 0)
    out_ref[...] = (
        partial_ref[...] + jnp.where(row == 0, corr_first, 0.0) + jnp.where(row == rows - 1, corr_last, 0.0)
    )


def corrected(w, partial, up_x0, from_prev, from_next, last_s):
    vmem = pl.BlockSpec(memory_space=pltpu.VMEM)
    return pl.pallas_call(
        fix_kernel,
        in_specs=[pl.BlockSpec(memory_space=pltpu.SMEM)] + [vmem] * 5,
        out_shape=jax.ShapeDtypeStruct(partial.shape, jnp.float32),
    )(w, partial, up_x0, from_prev, from_next, last_s)


def gather_rounds(count):
    bits = []
    bit = count // 2
    while bit >= 4:
        bits.append(bit)
        bit //= 2
    if len(bits) < 2:
        return [[b] for b in bits]
    return [[bits[1], bits[0], bits[0] | bits[1]]] + [[b] for b in bits[2:]]


def swap(value, axis, mask):
    count = lax.axis_size(axis)
    return lax.ppermute(value, axis, [(i, i ^ mask) for i in range(count)])


def cx_slab(cov_rows, offsets, device, rows):
    nxb = offsets.shape[0]
    global_rows = device * rows + jnp.arange(rows)
    row_block = global_rows // BLK
    target = (row_block[:, None] + offsets[row_block]) % nxb
    blocks = jnp.arange(nxb)
    hit = target[:, :, None, None] == blocks[None, None, :, None]
    slab = jnp.sum(jnp.where(hit, cov_rows.astype(jnp.float32)[:, :, None, :], 0.0), axis=1)
    return slab.reshape(rows, -1)


def mixed_rows(local, slab, axis):
    count = lax.axis_size(axis)
    me = lax.axis_index(axis)
    rows = local.shape[0]
    per_device = slab.reshape(slab.shape[0], count, rows)

    def product(piece, masks):
        cols = jnp.take(per_device, me ^ jnp.array(masks, jnp.int32), axis=1).reshape(slab.shape[0], -1)
        return jnp.dot(cols, piece.reshape(-1, piece.shape[-1]), precision=precise, preferred_element_type=jnp.float32)

    buf = local[None]
    entries = [0]
    total = product(buf, entries)
    for masks in gather_rounds(count):
        others = [swap(buf, axis, m) for m in masks]
        for m, other in zip(masks, others):
            total = total + product(other, [m ^ q for q in entries])
        buf = jnp.concatenate([buf] + others, axis=0)
        entries = entries + [m ^ q for m in masks for q in entries]
    parts = total.reshape(4, rows, total.shape[-1])
    got = swap(parts[1::2], axis, 1)
    near = parts[0::2] + got
    return near[0] + swap(near[1], axis, 2)


def body(
    adjoint_state,
    speed_x,
    speed_y,
    speed_z,
    dispersion,
    face_flags,
    layer_weight,
    cov_x,
    offsets_x,
    cov_y,
    offsets_y,
):
    count = lax.axis_size("gx")
    me = lax.axis_index("gx")
    depth, rows, cols = adjoint_state.shape

    partial, to_prev, last_s, up_x0 = stencil(
        layer_weight, adjoint_state, face_flags, speed_x, speed_y, speed_z, dispersion
    )
    from_next = passed_along(to_prev, "gx", -1)
    from_prev = passed_along(last_s, "gx", 1)

    recharge = corrected(layer_weight, partial, up_x0, from_prev, from_next, last_s)

    own_slab = cx_slab(cov_x, offsets_x, me, rows)
    slab = jnp.concatenate([own_slab] + [swap(own_slab, "gx", m) for m in (1, 2, 3)], axis=0)
    mixed = mixed_rows(recharge, slab, "gx")

    nyb = offsets_y.shape[0]
    col_block = (jnp.arange(nyb)[:, None] + offsets_y) % nyb
    picked = jnp.take(mixed.reshape(rows, nyb, BLK), col_block, axis=1)
    prior = jnp.einsum(
        "xrkc,rikc->xri",
        picked,
        cov_y.reshape(nyb, BLK, cov_y.shape[1], BLK),
        precision=precise,
        preferred_element_type=jnp.float32,
    ).reshape(rows, cols)
    return (recharge, prior)


def solution(mesh):
    return jax.shard_map(
        body,
        mesh=mesh,
        in_specs=(
            P(None, ("grp", "gx"), None),
            P(None, ("grp", "gx"), None),
            P(None, ("grp", "gx"), None),
            P(None, ("grp", "gx"), None),
            P(None, ("grp", "gx"), None),
            P(None, ("grp", "gx"), None),
            P(),
            P("gx", None, None),
            P(),
            P(),
            P(),
        ),
        out_specs=(P(("grp", "gx"), None), P(("grp", "gx"), None)),
        check_vma=False,
    )
```

```python
import jax
import jax.numpy as jnp
from jax import lax
from jax.experimental import pallas as pl
from jax.experimental.pallas import tpu as pltpu
from jax.sharding import PartitionSpec as P

BLK = 128
Z_CHUNK = 8

precise = lax.Precision.HIGH


def passed_along(value, axis, steps):
    count = lax.axis_size(axis)
    first, last = (max(0, -steps), min(count, count - steps))
    return lax.ppermute(value, axis, [(source, source + steps) for source in range(first, last)])


def coefs(flags, bit, speed, spread):
    on = (flags & bit) != 0
    lower = spread + jnp.where(on, speed, 0.0)
    upper = spread + jnp.where(on, 0.0, speed)
    return lower, upper


def stencil_kernel(w_ref, s_ref, sprev_ref, f_ref, vx_ref, vy_ref, vz_ref, d_ref, out_ref, to_prev_ref, last_ref, up_ref):
    c = pl.program_id(0)
    rows, cols = out_ref.shape
    sub = lax.broadcasted_iota(jnp.int32, (rows, cols), 0)
    lane = lax.broadcasted_iota(jnp.int32, (rows, cols), 1)

    @pl.when(c == 0)
    def _():
        out_ref[...] = jnp.zeros_like(out_ref)

    prev = jnp.where(c > 0, sprev_ref[0], 0.0)
    acc = jnp.zeros((rows, cols), jnp.float32)
    for j in range(s_ref.shape[0]):
        z = c * s_ref.shape[0] + j
        s = s_ref[j]
        f = f_ref[j]
        d = d_ref[j]
        lo_x, up_x = coefs(f, 1, vx_ref[j], d)
        to_prev_ref[0, pl.ds(z, 1), :] = s[0:1, :]
        to_prev_ref[1, pl.ds(z, 1), :] = lo_x[0:1, :]
        last_ref[pl.ds(z, 1), :] = s[rows - 1:rows, :]
        up_ref[pl.ds(z, 1), :] = up_x[0:1, :]
        lo_y, up_y = coefs(f, 2, vy_ref[j], d)
        lo_z, up_z = coefs(f, 4, vz_ref[j], d)
        s_xm = jnp.where(sub == 0, 0.0, pltpu.roll(s, 1, 0))
        jx = s - s_xm
        ax = lo_x * jx
        ax_next = jnp.where(sub == rows - 1, 0.0, pltpu.roll(ax, rows - 1, 0))
        img = up_x * jx - ax_next
        s_ym = jnp.where(lane == 0, 0.0, pltpu.roll(s, 1, 1))
        jy = s - s_ym
        ay = lo_y * jy
        ay_next = jnp.where(lane == cols - 1, 0.0, pltpu.roll(ay, cols - 1, 1))
        img = img + (up_y * jy - ay_next)
        jz = s - prev
        img = img + up_z * jz
        acc = acc + w_ref[z] * img
        w_before = jnp.where(z > 0, w_ref[jnp.maximum(z - 1, 0)], 0.0)
        acc = acc - w_before * (lo_z * jz)
        prev = s
    out_ref[...] += acc


def stencil(layer_weight, s, f, vx, vy, vz, d):
    depth, rows, cols = s.shape
    zc = Z_CHUNK if depth % Z_CHUNK == 0 else depth
    block = pl.BlockSpec((zc, rows, cols), lambda c: (c, 0, 0))
    prev_block = pl.BlockSpec((1, rows, cols), lambda c: (jnp.maximum(c * zc - 1, 0), 0, 0))
    return pl.pallas_call(
        stencil_kernel,
        grid=(depth // zc,),
        in_specs=[
            pl.BlockSpec(memory_space=pltpu.SMEM),
            block,
            prev_block,
            block,
            block,
            block,
            block,
            block,
        ],
        out_specs=[
            pl.BlockSpec((rows, cols), lambda c: (0, 0)),
            pl.BlockSpec((2, depth, cols), lambda c: (0, 0, 0)),
            pl.BlockSpec((depth, cols), lambda c: (0, 0)),
            pl.BlockSpec((depth, cols), lambda c: (0, 0)),
        ],
        out_shape=[
            jax.ShapeDtypeStruct((rows, cols), jnp.float32),
            jax.ShapeDtypeStruct((2, depth, cols), jnp.float32),
            jax.ShapeDtypeStruct((depth, cols), jnp.float32),
            jax.ShapeDtypeStruct((depth, cols), jnp.float32),
        ],
        compiler_params=pltpu.CompilerParams(dimension_semantics=("arbitrary",)),
    )(layer_weight, s, s, f, vx, vy, vz, d)


def fix_kernel(w_ref, partial_ref, up_ref, prev_ref, next_ref, last_ref, out_ref, corr_ref):
    rows, cols = partial_ref.shape
    depth = up_ref.shape[0]
    corr_first = jnp.zeros((1, cols), jnp.float32)
    corr_last = jnp.zeros((1, cols), jnp.float32)
    for z in range(depth):
        w = w_ref[z]
        corr_first = corr_first - w * (up_ref[pl.ds(z, 1), :] * prev_ref[pl.ds(z, 1), :])
        jump = next_ref[0, pl.ds(z, 1), :] - last_ref[pl.ds(z, 1), :]
        corr_last = corr_last - w * (next_ref[1, pl.ds(z, 1), :] * jump)
    row = lax.broadcasted_iota(jnp.int32, (rows, cols), 0)
    out_ref[...] = (
        partial_ref[...] + jnp.where(row == 0, corr_first, 0.0) + jnp.where(row == rows - 1, corr_last, 0.0)
    )
    corr_ref[0:1, :] = corr_first
    corr_ref[1:2, :] = corr_last


def corrected(w, partial, up_x0, from_prev, from_next, last_s):
    vmem = pl.BlockSpec(memory_space=pltpu.VMEM)
    return pl.pallas_call(
        fix_kernel,
        in_specs=[pl.BlockSpec(memory_space=pltpu.SMEM)] + [vmem] * 5,
        out_specs=[vmem, vmem],
        out_shape=[
            jax.ShapeDtypeStruct(partial.shape, jnp.float32),
            jax.ShapeDtypeStruct((2, partial.shape[1]), jnp.float32),
        ],
    )(w, partial, up_x0, from_prev, from_next, last_s)


def gather_rounds(count):
    bits = []
    bit = count // 2
    while bit >= 4:
        bits.append(bit)
        bit //= 2
    if len(bits) < 2:
        return [[b] for b in bits]
    return [[bits[1], bits[0], bits[0] | bits[1]]] + [[b] for b in bits[2:]]


def swap(value, axis, mask):
    count = lax.axis_size(axis)
    return lax.ppermute(value, axis, [(i, i ^ mask) for i in range(count)])


def cx_slab(cov_rows, offsets, device, rows):
    nxb = offsets.shape[0]
    global_rows = device * rows + jnp.arange(rows)
    row_block = global_rows // BLK
    target = (row_block[:, None] + offsets[row_block]) % nxb
    blocks = jnp.arange(nxb)
    hit = target[:, :, None, None] == blocks[None, None, :, None]
    slab = jnp.sum(jnp.where(hit, cov_rows.astype(jnp.float32)[:, :, None, :], 0.0), axis=1)
    return slab.reshape(rows, -1)


def gather_pieces(local, axis):
    buf = local[None]
    entries = [0]
    pieces = []
    for masks in gather_rounds(lax.axis_size(axis)):
        others = [swap(buf, axis, m) for m in masks]
        for m, other in zip(masks, others):
            pieces.append((other, [m ^ q for q in entries]))
        buf = jnp.concatenate([buf] + others, axis=0)
        entries = entries + [m ^ q for m in masks for q in entries]
    return pieces


def mixed_rows(partial, recharge, corr, slab, axis):
    count = lax.axis_size(axis)
    me = lax.axis_index(axis)
    rows = partial.shape[0]
    per_device = slab.reshape(slab.shape[0], count, rows)

    def columns(masks):
        return jnp.take(per_device, me ^ jnp.array(masks, jnp.int32), axis=1)

    def dot(cols, piece):
        return jnp.dot(
            cols.reshape(slab.shape[0], -1),
            piece.reshape(-1, piece.shape[-1]),
            precision=precise,
            preferred_element_type=jnp.float32,
        )

    bulk = gather_pieces(partial, axis)
    total = dot(columns([0]), recharge[None])
    taken = []
    for piece, masks in bulk:
        cols = columns(masks)
        taken.append(cols)
        total = total + dot(cols, piece)
    fixes = gather_pieces(corr, axis)
    for (piece, masks), cols in zip(fixes, taken):
        edge_cols = jnp.stack([cols[:, :, 0], cols[:, :, rows - 1]], axis=2)
        total = total + dot(edge_cols, piece)
    parts = total.reshape(4, rows, total.shape[-1])
    got = swap(parts[1::2], axis, 1)
    near = parts[0::2] + got
    return near[0] + swap(near[1], axis, 2)


def body(
    adjoint_state,
    speed_x,
    speed_y,
    speed_z,
    dispersion,
    face_flags,
    layer_weight,
    cov_x,
    offsets_x,
    cov_y,
    offsets_y,
):
    count = lax.axis_size("gx")
    me = lax.axis_index("gx")
    depth, rows, cols = adjoint_state.shape

    partial, to_prev, last_s, up_x0 = stencil(
        layer_weight, adjoint_state, face_flags, speed_x, speed_y, speed_z, dispersion
    )
    from_next = passed_along(to_prev, "gx", -1)
    from_prev = passed_along(last_s, "gx", 1)

    recharge, corr = corrected(layer_weight, partial, up_x0, from_prev, from_next, last_s)

    own_slab = cx_slab(cov_x, offsets_x, me, rows)
    slab = jnp.concatenate([own_slab] + [swap(own_slab, "gx", m) for m in (1, 2, 3)], axis=0)
    mixed = mixed_rows(partial, recharge, corr, slab, "gx")

    nyb = offsets_y.shape[0]
    col_block = (jnp.arange(nyb)[:, None] + offsets_y) % nyb
    picked = jnp.take(mixed.reshape(rows, nyb, BLK), col_block, axis=1)
    prior = jnp.einsum(
        "xrkc,rikc->xri",
        picked,
        cov_y.reshape(nyb, BLK, cov_y.shape[1], BLK),
        precision=precise,
        preferred_element_type=jnp.float32,
    ).reshape(rows, cols)
    return (recharge, prior)


def solution(mesh):
    return jax.shard_map(
        body,
        mesh=mesh,
        in_specs=(
            P(None, ("grp", "gx"), None),
            P(None, ("grp", "gx"), None),
            P(None, ("grp", "gx"), None),
            P(None, ("grp", "gx"), None),
            P(None, ("grp", "gx"), None),
            P(None, ("grp", "gx"), None),
            P(),
            P("gx", None, None),
            P(),
            P(),
            P(),
        ),
        out_specs=(P(("grp", "gx"), None), P(("grp", "gx"), None)),
        check_vma=False,
    )
```

```python
import jax
import jax.numpy as jnp
from jax import lax
from jax.experimental import pallas as pl
from jax.experimental.pallas import tpu as pltpu
from jax.sharding import PartitionSpec as P

BLK = 128
Z_CHUNK = 8

precise = lax.Precision.HIGH


def passed_along(value, axis, steps):
    count = lax.axis_size(axis)
    first, last = (max(0, -steps), min(count, count - steps))
    return lax.ppermute(value, axis, [(source, source + steps) for source in range(first, last)])


def coefs(flags, bit, speed, spread):
    on = (flags & bit) != 0
    lower = spread + jnp.where(on, speed, 0.0)
    upper = spread + jnp.where(on, 0.0, speed)
    return lower, upper


def stencil_kernel(w_ref, s_ref, sprev_ref, f_ref, vx_ref, vy_ref, vz_ref, d_ref, out_ref, to_prev_ref, last_ref, up_ref):
    c = pl.program_id(0)
    rows, cols = out_ref.shape
    sub = lax.broadcasted_iota(jnp.int32, (rows, cols), 0)
    lane = lax.broadcasted_iota(jnp.int32, (rows, cols), 1)

    @pl.when(c == 0)
    def _():
        out_ref[...] = jnp.zeros_like(out_ref)

    prev = jnp.where(c > 0, sprev_ref[0], 0.0)
    acc = jnp.zeros((rows, cols), jnp.float32)
    for j in range(s_ref.shape[0]):
        z = c * s_ref.shape[0] + j
        s = s_ref[j]
        f = f_ref[j]
        d = d_ref[j]
        lo_x, up_x = coefs(f, 1, vx_ref[j], d)
        to_prev_ref[0, pl.ds(z, 1), :] = s[0:1, :]
        to_prev_ref[1, pl.ds(z, 1), :] = lo_x[0:1, :]
        last_ref[pl.ds(z, 1), :] = s[rows - 1:rows, :]
        up_ref[pl.ds(z, 1), :] = up_x[0:1, :]
        lo_y, up_y = coefs(f, 2, vy_ref[j], d)
        lo_z, up_z = coefs(f, 4, vz_ref[j], d)
        s_xm = jnp.where(sub == 0, 0.0, pltpu.roll(s, 1, 0))
        jx = s - s_xm
        ax = lo_x * jx
        ax_next = jnp.where(sub == rows - 1, 0.0, pltpu.roll(ax, rows - 1, 0))
        img = up_x * jx - ax_next
        s_ym = jnp.where(lane == 0, 0.0, pltpu.roll(s, 1, 1))
        jy = s - s_ym
        ay = lo_y * jy
        ay_next = jnp.where(lane == cols - 1, 0.0, pltpu.roll(ay, cols - 1, 1))
        img = img + (up_y * jy - ay_next)
        jz = s - prev
        img = img + up_z * jz
        acc = acc + w_ref[z] * img
        w_before = jnp.where(z > 0, w_ref[jnp.maximum(z - 1, 0)], 0.0)
        acc = acc - w_before * (lo_z * jz)
        prev = s
    out_ref[...] += acc


def stencil(layer_weight, s, f, vx, vy, vz, d):
    depth, rows, cols = s.shape
    zc = Z_CHUNK if depth % Z_CHUNK == 0 else depth
    block = pl.BlockSpec((zc, rows, cols), lambda c: (c, 0, 0))
    prev_block = pl.BlockSpec((1, rows, cols), lambda c: (jnp.maximum(c * zc - 1, 0), 0, 0))
    return pl.pallas_call(
        stencil_kernel,
        grid=(depth // zc,),
        in_specs=[
            pl.BlockSpec(memory_space=pltpu.SMEM),
            block,
            prev_block,
            block,
            block,
            block,
            block,
            block,
        ],
        out_specs=[
            pl.BlockSpec((rows, cols), lambda c: (0, 0)),
            pl.BlockSpec((2, depth, cols), lambda c: (0, 0, 0)),
            pl.BlockSpec((depth, cols), lambda c: (0, 0)),
            pl.BlockSpec((depth, cols), lambda c: (0, 0)),
        ],
        out_shape=[
            jax.ShapeDtypeStruct((rows, cols), jnp.float32),
            jax.ShapeDtypeStruct((2, depth, cols), jnp.float32),
            jax.ShapeDtypeStruct((depth, cols), jnp.float32),
            jax.ShapeDtypeStruct((depth, cols), jnp.float32),
        ],
        compiler_params=pltpu.CompilerParams(dimension_semantics=("arbitrary",)),
    )(layer_weight, s, s, f, vx, vy, vz, d)


def fix_kernel(w_ref, partial_ref, up_ref, prev_ref, next_ref, last_ref, out_ref):
    rows, cols = partial_ref.shape
    depth = up_ref.shape[0]
    corr_first = jnp.zeros((1, cols), jnp.float32)
    corr_last = jnp.zeros((1, cols), jnp.float32)
    for z in range(depth):
        w = w_ref[z]
        corr_first = corr_first - w * (up_ref[pl.ds(z, 1), :] * prev_ref[pl.ds(z, 1), :])
        jump = next_ref[0, pl.ds(z, 1), :] - last_ref[pl.ds(z, 1), :]
        corr_last = corr_last - w * (next_ref[1, pl.ds(z, 1), :] * jump)
    row = lax.broadcasted_iota(jnp.int32, (rows, cols), 0)
    out_ref[...] = (
        partial_ref[...] + jnp.where(row == 0, corr_first, 0.0) + jnp.where(row == rows - 1, corr_last, 0.0)
    )


def corrected(w, partial, up_x0, from_prev, from_next, last_s):
    vmem = pl.BlockSpec(memory_space=pltpu.VMEM)
    return pl.pallas_call(
        fix_kernel,
        in_specs=[pl.BlockSpec(memory_space=pltpu.SMEM)] + [vmem] * 5,
        out_shape=jax.ShapeDtypeStruct(partial.shape, jnp.float32),
    )(w, partial, up_x0, from_prev, from_next, last_s)


def gather_rounds(count):
    bits = []
    bit = count // 2
    while bit >= 4:
        bits.append(bit)
        bit //= 2
    if len(bits) < 2:
        return [[b] for b in bits]
    return [[bits[1], bits[0], bits[0] | bits[1]]] + [[b] for b in bits[2:]]


def swap(value, axis, mask):
    count = lax.axis_size(axis)
    return lax.ppermute(value, axis, [(i, i ^ mask) for i in range(count)])


def cx_slab(cov_rows, offsets, device, rows):
    nxb = offsets.shape[0]
    global_rows = device * rows + jnp.arange(rows)
    row_block = global_rows // BLK
    target = (row_block[:, None] + offsets[row_block]) % nxb
    blocks = jnp.arange(nxb)
    hit = target[:, :, None, None] == blocks[None, None, :, None]
    slab = jnp.sum(jnp.where(hit, cov_rows.astype(jnp.float32)[:, :, None, :], 0.0), axis=1)
    return slab.reshape(rows, -1)


def mixed_rows(local, slab, axis):
    count = lax.axis_size(axis)
    me = lax.axis_index(axis)
    rows = local.shape[0]
    per_device = slab.reshape(slab.shape[0], count, rows)

    def product(piece, masks):
        cols = jnp.take(per_device, me ^ jnp.array(masks, jnp.int32), axis=1).reshape(slab.shape[0], -1)
        return jnp.dot(cols, piece.reshape(-1, piece.shape[-1]), precision=precise, preferred_element_type=jnp.float32)

    buf = local[None]
    entries = [0]
    total = product(buf, entries)
    for masks in gather_rounds(count):
        others = [swap(buf, axis, m) for m in masks]
        for m, other in zip(masks, others):
            total = total + product(other, [m ^ q for q in entries])
        buf = jnp.concatenate([buf] + others, axis=0)
        entries = entries + [m ^ q for m in masks for q in entries]
    parts = total.reshape(4, rows, total.shape[-1])
    got = swap(parts[1::2], axis, 1)
    near = parts[0::2] + got
    return near[0] + swap(near[1], axis, 2)


def body(
    adjoint_state,
    speed_x,
    speed_y,
    speed_z,
    dispersion,
    face_flags,
    layer_weight,
    cov_x,
    offsets_x,
    cov_y,
    offsets_y,
):
    count = lax.axis_size("gx")
    me = lax.axis_index("gx")
    depth, rows, cols = adjoint_state.shape

    partial, to_prev, last_s, up_x0 = stencil(
        layer_weight, adjoint_state, face_flags, speed_x, speed_y, speed_z, dispersion
    )
    from_next = passed_along(to_prev, "gx", -1)
    from_prev = passed_along(last_s, "gx", 1)

    recharge = corrected(layer_weight, partial, up_x0, from_prev, from_next, last_s)

    own_slab = cx_slab(cov_x, offsets_x, me, rows)
    slab = jnp.concatenate([own_slab] + [swap(own_slab, "gx", m) for m in (1, 2, 3)], axis=0)
    mixed = mixed_rows(recharge, slab, "gx")

    nyb = offsets_y.shape[0]
    col_block = (jnp.arange(nyb)[:, None] + offsets_y) % nyb
    ny = cov_y.shape[0]
    row_target = jnp.repeat(col_block, BLK, axis=0)
    hit = row_target[:, :, None, None] == jnp.arange(nyb)[None, None, :, None]
    dense_y = jnp.sum(jnp.where(hit, cov_y[:, :, None, :], 0.0), axis=1).reshape(ny, nyb * BLK)
    prior = lax.dot_general(
        mixed, dense_y, (((1,), (1,)), ((), ())), precision=precise, preferred_element_type=jnp.float32
    )
    return (recharge, prior)


def solution(mesh):
    return jax.shard_map(
        body,
        mesh=mesh,
        in_specs=(
            P(None, ("grp", "gx"), None),
            P(None, ("grp", "gx"), None),
            P(None, ("grp", "gx"), None),
            P(None, ("grp", "gx"), None),
            P(None, ("grp", "gx"), None),
            P(None, ("grp", "gx"), None),
            P(),
            P("gx", None, None),
            P(),
            P(),
            P(),
        ),
        out_specs=(P(("grp", "gx"), None), P(("grp", "gx"), None)),
        check_vma=False,
    )
```

```python
import jax
import jax.numpy as jnp
from jax import lax
from jax.experimental import pallas as pl
from jax.experimental.pallas import tpu as pltpu
from jax.sharding import PartitionSpec as P

BLK = 128
Z_CHUNK = 8

precise = lax.Precision.HIGH


def passed_along(value, axis, steps):
    count = lax.axis_size(axis)
    first, last = (max(0, -steps), min(count, count - steps))
    return lax.ppermute(value, axis, [(source, source + steps) for source in range(first, last)])


def coefs(flags, bit, speed, spread):
    on = (flags & bit) != 0
    lower = spread + jnp.where(on, speed, 0.0)
    upper = spread + jnp.where(on, 0.0, speed)
    return lower, upper


def stencil_kernel(w_ref, s_ref, sprev_ref, f_ref, vx_ref, vy_ref, vz_ref, d_ref, out_ref, to_prev_ref, last_ref, up_ref):
    c = pl.program_id(0)
    rows, cols = out_ref.shape
    sub = lax.broadcasted_iota(jnp.int32, (rows, cols), 0)
    lane = lax.broadcasted_iota(jnp.int32, (rows, cols), 1)

    @pl.when(c == 0)
    def _():
        out_ref[...] = jnp.zeros_like(out_ref)

    prev = jnp.where(c > 0, sprev_ref[0], 0.0)
    acc = jnp.zeros((rows, cols), jnp.float32)
    for j in range(s_ref.shape[0]):
        z = c * s_ref.shape[0] + j
        s = s_ref[j]
        f = f_ref[j]
        d = d_ref[j]
        lo_x, up_x = coefs(f, 1, vx_ref[j], d)
        to_prev_ref[0, pl.ds(z, 1), :] = s[0:1, :]
        to_prev_ref[1, pl.ds(z, 1), :] = lo_x[0:1, :]
        last_ref[pl.ds(z, 1), :] = s[rows - 1:rows, :]
        up_ref[pl.ds(z, 1), :] = up_x[0:1, :]
        lo_y, up_y = coefs(f, 2, vy_ref[j], d)
        lo_z, up_z = coefs(f, 4, vz_ref[j], d)
        s_xm = jnp.where(sub == 0, 0.0, pltpu.roll(s, 1, 0))
        jx = s - s_xm
        ax = lo_x * jx
        ax_next = jnp.where(sub == rows - 1, 0.0, pltpu.roll(ax, rows - 1, 0))
        img = up_x * jx - ax_next
        s_ym = jnp.where(lane == 0, 0.0, pltpu.roll(s, 1, 1))
        jy = s - s_ym
        ay = lo_y * jy
        ay_next = jnp.where(lane == cols - 1, 0.0, pltpu.roll(ay, cols - 1, 1))
        img = img + (up_y * jy - ay_next)
        jz = s - prev
        img = img + up_z * jz
        acc = acc + w_ref[z] * img
        w_before = jnp.where(z > 0, w_ref[jnp.maximum(z - 1, 0)], 0.0)
        acc = acc - w_before * (lo_z * jz)
        prev = s
    out_ref[...] += acc


def stencil(layer_weight, s, f, vx, vy, vz, d):
    depth, rows, cols = s.shape
    zc = Z_CHUNK if depth % Z_CHUNK == 0 else depth
    block = pl.BlockSpec((zc, rows, cols), lambda c: (c, 0, 0))
    prev_block = pl.BlockSpec((1, rows, cols), lambda c: (jnp.maximum(c * zc - 1, 0), 0, 0))
    return pl.pallas_call(
        stencil_kernel,
        grid=(depth // zc,),
        in_specs=[
            pl.BlockSpec(memory_space=pltpu.SMEM),
            block,
            prev_block,
            block,
            block,
            block,
            block,
            block,
        ],
        out_specs=[
            pl.BlockSpec((rows, cols), lambda c: (0, 0)),
            pl.BlockSpec((2, depth, cols), lambda c: (0, 0, 0)),
            pl.BlockSpec((depth, cols), lambda c: (0, 0)),
            pl.BlockSpec((depth, cols), lambda c: (0, 0)),
        ],
        out_shape=[
            jax.ShapeDtypeStruct((rows, cols), jnp.float32),
            jax.ShapeDtypeStruct((2, depth, cols), jnp.float32),
            jax.ShapeDtypeStruct((depth, cols), jnp.float32),
            jax.ShapeDtypeStruct((depth, cols), jnp.float32),
        ],
        compiler_params=pltpu.CompilerParams(dimension_semantics=("arbitrary",)),
    )(layer_weight, s, s, f, vx, vy, vz, d)


def fix_kernel(w_ref, partial_ref, up_ref, prev_ref, next_ref, last_ref, out_ref):
    rows, cols = partial_ref.shape
    depth = up_ref.shape[0]
    corr_first = jnp.zeros((1, cols), jnp.float32)
    corr_last = jnp.zeros((1, cols), jnp.float32)
    for z in range(depth):
        w = w_ref[z]
        corr_first = corr_first - w * (up_ref[pl.ds(z, 1), :] * prev_ref[pl.ds(z, 1), :])
        jump = next_ref[0, pl.ds(z, 1), :] - last_ref[pl.ds(z, 1), :]
        corr_last = corr_last - w * (next_ref[1, pl.ds(z, 1), :] * jump)
    row = lax.broadcasted_iota(jnp.int32, (rows, cols), 0)
    out_ref[...] = (
        partial_ref[...] + jnp.where(row == 0, corr_first, 0.0) + jnp.where(row == rows - 1, corr_last, 0.0)
    )


def corrected(w, partial, up_x0, from_prev, from_next, last_s):
    vmem = pl.BlockSpec(memory_space=pltpu.VMEM)
    return pl.pallas_call(
        fix_kernel,
        in_specs=[pl.BlockSpec(memory_space=pltpu.SMEM)] + [vmem] * 5,
        out_shape=jax.ShapeDtypeStruct(partial.shape, jnp.float32),
    )(w, partial, up_x0, from_prev, from_next, last_s)


def gather_rounds(count):
    bits = []
    bit = count // 2
    while bit >= 4:
        bits.append(bit)
        bit //= 2
    if len(bits) < 2:
        return [[b] for b in bits]
    return [[bits[1], bits[0], bits[0] | bits[1]]] + [[b] for b in bits[2:]]


def swap(value, axis, mask):
    count = lax.axis_size(axis)
    return lax.ppermute(value, axis, [(i, i ^ mask) for i in range(count)])


def cx_slab(cov_rows, offsets, device, rows):
    nxb = offsets.shape[0]
    global_rows = device * rows + jnp.arange(rows)
    row_block = global_rows // BLK
    target = (row_block[:, None] + offsets[row_block]) % nxb
    blocks = jnp.arange(nxb)
    hit = target[:, :, None, None] == blocks[None, None, :, None]
    slab = jnp.sum(jnp.where(hit, cov_rows.astype(jnp.float32)[:, :, None, :], 0.0), axis=1)
    return slab.reshape(rows, -1)


def mixed_rows(local, slab, axis):
    count = lax.axis_size(axis)
    me = lax.axis_index(axis)
    rows = local.shape[0]
    per_device = slab.reshape(slab.shape[0], count, rows)

    def product(piece, masks):
        cols = jnp.take(per_device, me ^ jnp.array(masks, jnp.int32), axis=1).reshape(slab.shape[0], -1)
        return jnp.dot(cols, piece.reshape(-1, piece.shape[-1]), precision=precise, preferred_element_type=jnp.float32)

    buf = local[None]
    entries = [0]
    total = product(buf, entries)
    for masks in gather_rounds(count):
        others = [swap(buf, axis, m) for m in masks]
        for m, other in zip(masks, others):
            total = total + product(other, [m ^ q for q in entries])
        buf = jnp.concatenate([buf] + others, axis=0)
        entries = entries + [m ^ q for m in masks for q in entries]
    parts = total.reshape(4, rows, total.shape[-1])
    return parts[0] + (swap(parts[1], axis, 1) + swap(parts[2], axis, 2) + swap(parts[3], axis, 3))


def body(
    adjoint_state,
    speed_x,
    speed_y,
    speed_z,
    dispersion,
    face_flags,
    layer_weight,
    cov_x,
    offsets_x,
    cov_y,
    offsets_y,
):
    count = lax.axis_size("gx")
    me = lax.axis_index("gx")
    depth, rows, cols = adjoint_state.shape

    partial, to_prev, last_s, up_x0 = stencil(
        layer_weight, adjoint_state, face_flags, speed_x, speed_y, speed_z, dispersion
    )
    from_next = passed_along(to_prev, "gx", -1)
    from_prev = passed_along(last_s, "gx", 1)

    recharge = corrected(layer_weight, partial, up_x0, from_prev, from_next, last_s)

    own_slab = cx_slab(cov_x, offsets_x, me, rows)
    slab = jnp.concatenate([own_slab] + [swap(own_slab, "gx", m) for m in (1, 2, 3)], axis=0)
    mixed = mixed_rows(recharge, slab, "gx")

    nyb = offsets_y.shape[0]
    col_block = (jnp.arange(nyb)[:, None] + offsets_y) % nyb
    picked = jnp.take(mixed.reshape(rows, nyb, BLK), col_block, axis=1)
    prior = jnp.einsum(
        "xrkc,rikc->xri",
        picked,
        cov_y.reshape(nyb, BLK, cov_y.shape[1], BLK),
        precision=precise,
        preferred_element_type=jnp.float32,
    ).reshape(rows, cols)
    return (recharge, prior)


def solution(mesh):
    return jax.shard_map(
        body,
        mesh=mesh,
        in_specs=(
            P(None, ("grp", "gx"), None),
            P(None, ("grp", "gx"), None),
            P(None, ("grp", "gx"), None),
            P(None, ("grp", "gx"), None),
            P(None, ("grp", "gx"), None),
            P(None, ("grp", "gx"), None),
            P(),
            P("gx", None, None),
            P(),
            P(),
            P(),
        ),
        out_specs=(P(("grp", "gx"), None), P(("grp", "gx"), None)),
        check_vma=False,
    )
```

```python
import jax
import jax.numpy as jnp
from jax import lax
from jax.experimental import pallas as pl
from jax.experimental.pallas import tpu as pltpu
from jax.sharding import PartitionSpec as P

BLK = 128
Z_CHUNK = 8

precise = lax.Precision.HIGH


def passed_along(value, axis, steps):
    count = lax.axis_size(axis)
    first, last = (max(0, -steps), min(count, count - steps))
    return lax.ppermute(value, axis, [(source, source + steps) for source in range(first, last)])


def coefs(flags, bit, speed, spread):
    on = (flags & bit) != 0
    lower = spread + jnp.where(on, speed, 0.0)
    upper = spread + jnp.where(on, 0.0, speed)
    return lower, upper


def stencil_kernel(w_ref, s_ref, sprev_ref, f_ref, vx_ref, vy_ref, vz_ref, d_ref, out_ref, to_prev_ref, last_ref, up_ref):
    c = pl.program_id(0)
    rows, cols = out_ref.shape
    sub = lax.broadcasted_iota(jnp.int32, (rows, cols), 0)
    lane = lax.broadcasted_iota(jnp.int32, (rows, cols), 1)

    @pl.when(c == 0)
    def _():
        out_ref[...] = jnp.zeros_like(out_ref)

    prev = jnp.where(c > 0, sprev_ref[0], 0.0)
    acc = jnp.zeros((rows, cols), jnp.float32)
    for j in range(s_ref.shape[0]):
        z = c * s_ref.shape[0] + j
        s = s_ref[j]
        f = f_ref[j]
        d = d_ref[j]
        lo_x, up_x = coefs(f, 1, vx_ref[j], d)
        to_prev_ref[0, pl.ds(z, 1), :] = s[0:1, :]
        to_prev_ref[1, pl.ds(z, 1), :] = lo_x[0:1, :]
        last_ref[pl.ds(z, 1), :] = s[rows - 1:rows, :]
        up_ref[pl.ds(z, 1), :] = up_x[0:1, :]
        lo_y, up_y = coefs(f, 2, vy_ref[j], d)
        lo_z, up_z = coefs(f, 4, vz_ref[j], d)
        s_xm = jnp.where(sub == 0, 0.0, pltpu.roll(s, 1, 0))
        jx = s - s_xm
        ax = lo_x * jx
        ax_next = jnp.where(sub == rows - 1, 0.0, pltpu.roll(ax, rows - 1, 0))
        img = up_x * jx - ax_next
        s_ym = jnp.where(lane == 0, 0.0, pltpu.roll(s, 1, 1))
        jy = s - s_ym
        ay = lo_y * jy
        ay_next = jnp.where(lane == cols - 1, 0.0, pltpu.roll(ay, cols - 1, 1))
        img = img + (up_y * jy - ay_next)
        jz = s - prev
        img = img + up_z * jz
        acc = acc + w_ref[z] * img
        w_before = jnp.where(z > 0, w_ref[jnp.maximum(z - 1, 0)], 0.0)
        acc = acc - w_before * (lo_z * jz)
        prev = s
    out_ref[...] += acc


def stencil(layer_weight, s, f, vx, vy, vz, d):
    depth, rows, cols = s.shape
    zc = Z_CHUNK if depth % Z_CHUNK == 0 else depth
    block = pl.BlockSpec((zc, rows, cols), lambda c: (c, 0, 0))
    prev_block = pl.BlockSpec((1, rows, cols), lambda c: (jnp.maximum(c * zc - 1, 0), 0, 0))
    return pl.pallas_call(
        stencil_kernel,
        grid=(depth // zc,),
        in_specs=[
            pl.BlockSpec(memory_space=pltpu.SMEM),
            block,
            prev_block,
            block,
            block,
            block,
            block,
            block,
        ],
        out_specs=[
            pl.BlockSpec((rows, cols), lambda c: (0, 0)),
            pl.BlockSpec((2, depth, cols), lambda c: (0, 0, 0)),
            pl.BlockSpec((depth, cols), lambda c: (0, 0)),
            pl.BlockSpec((depth, cols), lambda c: (0, 0)),
        ],
        out_shape=[
            jax.ShapeDtypeStruct((rows, cols), jnp.float32),
            jax.ShapeDtypeStruct((2, depth, cols), jnp.float32),
            jax.ShapeDtypeStruct((depth, cols), jnp.float32),
            jax.ShapeDtypeStruct((depth, cols), jnp.float32),
        ],
        compiler_params=pltpu.CompilerParams(dimension_semantics=("arbitrary",)),
    )(layer_weight, s, s, f, vx, vy, vz, d)


def fix_kernel(w_ref, partial_ref, up_ref, prev_ref, next_ref, last_ref, out_ref):
    rows, cols = partial_ref.shape
    depth = up_ref.shape[0]
    corr_first = jnp.zeros((1, cols), jnp.float32)
    corr_last = jnp.zeros((1, cols), jnp.float32)
    for z in range(depth):
        w = w_ref[z]
        corr_first = corr_first - w * (up_ref[pl.ds(z, 1), :] * prev_ref[pl.ds(z, 1), :])
        jump = next_ref[0, pl.ds(z, 1), :] - last_ref[pl.ds(z, 1), :]
        corr_last = corr_last - w * (next_ref[1, pl.ds(z, 1), :] * jump)
    row = lax.broadcasted_iota(jnp.int32, (rows, cols), 0)
    out_ref[...] = (
        partial_ref[...] + jnp.where(row == 0, corr_first, 0.0) + jnp.where(row == rows - 1, corr_last, 0.0)
    )


def corrected(w, partial, up_x0, from_prev, from_next, last_s):
    vmem = pl.BlockSpec(memory_space=pltpu.VMEM)
    return pl.pallas_call(
        fix_kernel,
        in_specs=[pl.BlockSpec(memory_space=pltpu.SMEM)] + [vmem] * 5,
        out_shape=jax.ShapeDtypeStruct(partial.shape, jnp.float32),
    )(w, partial, up_x0, from_prev, from_next, last_s)


def gather_rounds(count):
    bits = []
    bit = count // 2
    while bit >= 4:
        bits.append(bit)
        bit //= 2
    if len(bits) < 2:
        return [[b] for b in bits]
    return [[bits[1], bits[0], bits[0] | bits[1]]] + [[b] for b in bits[2:]]


def swap(value, axis, mask):
    count = lax.axis_size(axis)
    return lax.ppermute(value, axis, [(i, i ^ mask) for i in range(count)])


def cx_slab(cov_rows, offsets, device, rows):
    nxb = offsets.shape[0]
    global_rows = device * rows + jnp.arange(rows)
    row_block = global_rows // BLK
    target = (row_block[:, None] + offsets[row_block]) % nxb
    blocks = jnp.arange(nxb)
    hit = target[:, :, None, None] == blocks[None, None, :, None]
    slab = jnp.sum(jnp.where(hit, cov_rows.astype(jnp.float32)[:, :, None, :], 0.0), axis=1)
    return slab.reshape(rows, -1)


def mixed_rows(local, slab, axis):
    count = lax.axis_size(axis)
    me = lax.axis_index(axis)
    rows = local.shape[0]
    per_device = slab.reshape(slab.shape[0], count, rows)

    def product(piece, masks):
        cols = jnp.take(per_device, me ^ jnp.array(masks, jnp.int32), axis=1).reshape(slab.shape[0], -1)
        return jnp.dot(cols, piece.reshape(-1, piece.shape[-1]), precision=precise, preferred_element_type=jnp.float32)

    buf = local[None]
    entries = [0]
    total = product(buf, entries)
    for masks in gather_rounds(count):
        others = [swap(buf, axis, m) for m in masks]
        for m, other in zip(masks, others):
            total = total + product(other, [m ^ q for q in entries])
        buf = jnp.concatenate([buf] + others, axis=0)
        entries = entries + [m ^ q for m in masks for q in entries]
    parts = total.reshape(4, rows, total.shape[-1])
    got = swap(parts[1::2], axis, 1)
    near = parts[0::2] + got
    return near[0] + swap(near[1], axis, 2)


def body(
    adjoint_state,
    speed_x,
    speed_y,
    speed_z,
    dispersion,
    face_flags,
    layer_weight,
    cov_x,
    offsets_x,
    cov_y,
    offsets_y,
):
    count = lax.axis_size("gx")
    me = lax.axis_index("gx")
    depth, rows, cols = adjoint_state.shape

    partial, to_prev, last_s, up_x0 = stencil(
        layer_weight, adjoint_state, face_flags, speed_x, speed_y, speed_z, dispersion
    )
    from_next = passed_along(to_prev, "gx", -1)
    from_prev = passed_along(last_s, "gx", 1)

    recharge = corrected(layer_weight, partial, up_x0, from_prev, from_next, last_s)

    own_slab = cx_slab(cov_x, offsets_x, me, rows)
    late_slab, _ = lax.optimization_barrier((own_slab, recharge))
    slab = jnp.concatenate([own_slab] + [swap(late_slab, "gx", m) for m in (1, 2, 3)], axis=0)
    mixed = mixed_rows(recharge, slab, "gx")

    nyb = offsets_y.shape[0]
    col_block = (jnp.arange(nyb)[:, None] + offsets_y) % nyb
    picked = jnp.take(mixed.reshape(rows, nyb, BLK), col_block, axis=1)
    prior = jnp.einsum(
        "xrkc,rikc->xri",
        picked,
        cov_y.reshape(nyb, BLK, cov_y.shape[1], BLK),
        precision=precise,
        preferred_element_type=jnp.float32,
    ).reshape(rows, cols)
    return (recharge, prior)


def solution(mesh):
    return jax.shard_map(
        body,
        mesh=mesh,
        in_specs=(
            P(None, ("grp", "gx"), None),
            P(None, ("grp", "gx"), None),
            P(None, ("grp", "gx"), None),
            P(None, ("grp", "gx"), None),
            P(None, ("grp", "gx"), None),
            P(None, ("grp", "gx"), None),
            P(),
            P("gx", None, None),
            P(),
            P(),
            P(),
        ),
        out_specs=(P(("grp", "gx"), None), P(("grp", "gx"), None)),
        check_vma=False,
    )
```

```python
import jax
import jax.numpy as jnp
from jax import lax
from jax.experimental import pallas as pl
from jax.experimental.pallas import tpu as pltpu
from jax.sharding import Mesh, PartitionSpec as P

BLK = 128
AX = ("zq", "xq", "cq")
Z_CHUNK = 8

precise = lax.Precision.HIGH


def passed_along(value, axis, steps):
    count = lax.axis_size(axis)
    first, last = (max(0, -steps), min(count, count - steps))
    return lax.ppermute(value, axis, [(source, source + steps) for source in range(first, last)])


def coefs(flags, bit, speed, spread):
    on = (flags & bit) != 0
    lower = spread + jnp.where(on, speed, 0.0)
    upper = spread + jnp.where(on, 0.0, speed)
    return lower, upper


def stencil_kernel(w_ref, s_ref, sprev_ref, f_ref, vx_ref, vy_ref, vz_ref, d_ref, out_ref, to_prev_ref, last_ref, up_ref):
    c = pl.program_id(0)
    rows, cols = out_ref.shape
    sub = lax.broadcasted_iota(jnp.int32, (rows, cols), 0)
    lane = lax.broadcasted_iota(jnp.int32, (rows, cols), 1)

    @pl.when(c == 0)
    def _():
        out_ref[...] = jnp.zeros_like(out_ref)

    prev = jnp.where(c > 0, sprev_ref[0], 0.0)
    acc = jnp.zeros((rows, cols), jnp.float32)
    for j in range(s_ref.shape[0]):
        z = c * s_ref.shape[0] + j
        s = s_ref[j]
        f = f_ref[j]
        d = d_ref[j]
        lo_x, up_x = coefs(f, 1, vx_ref[j], d)
        to_prev_ref[0, pl.ds(z, 1), :] = s[0:1, :]
        to_prev_ref[1, pl.ds(z, 1), :] = lo_x[0:1, :]
        last_ref[pl.ds(z, 1), :] = s[rows - 1:rows, :]
        up_ref[pl.ds(z, 1), :] = up_x[0:1, :]
        lo_y, up_y = coefs(f, 2, vy_ref[j], d)
        lo_z, up_z = coefs(f, 4, vz_ref[j], d)
        s_xm = jnp.where(sub == 0, 0.0, pltpu.roll(s, 1, 0))
        jx = s - s_xm
        ax = lo_x * jx
        ax_next = jnp.where(sub == rows - 1, 0.0, pltpu.roll(ax, rows - 1, 0))
        img = up_x * jx - ax_next
        s_ym = jnp.where(lane == 0, 0.0, pltpu.roll(s, 1, 1))
        jy = s - s_ym
        ay = lo_y * jy
        ay_next = jnp.where(lane == cols - 1, 0.0, pltpu.roll(ay, cols - 1, 1))
        img = img + (up_y * jy - ay_next)
        jz = s - prev
        img = img + up_z * jz
        acc = acc + w_ref[z] * img
        w_before = jnp.where(z > 0, w_ref[jnp.maximum(z - 1, 0)], 0.0)
        acc = acc - w_before * (lo_z * jz)
        prev = s
    out_ref[...] += acc


def stencil(layer_weight, s, f, vx, vy, vz, d):
    depth, rows, cols = s.shape
    zc = Z_CHUNK if depth % Z_CHUNK == 0 else depth
    block = pl.BlockSpec((zc, rows, cols), lambda c: (c, 0, 0))
    prev_block = pl.BlockSpec((1, rows, cols), lambda c: (jnp.maximum(c * zc - 1, 0), 0, 0))
    return pl.pallas_call(
        stencil_kernel,
        grid=(depth // zc,),
        in_specs=[
            pl.BlockSpec(memory_space=pltpu.SMEM),
            block,
            prev_block,
            block,
            block,
            block,
            block,
            block,
        ],
        out_specs=[
            pl.BlockSpec((rows, cols), lambda c: (0, 0)),
            pl.BlockSpec((2, depth, cols), lambda c: (0, 0, 0)),
            pl.BlockSpec((depth, cols), lambda c: (0, 0)),
            pl.BlockSpec((depth, cols), lambda c: (0, 0)),
        ],
        out_shape=[
            jax.ShapeDtypeStruct((rows, cols), jnp.float32),
            jax.ShapeDtypeStruct((2, depth, cols), jnp.float32),
            jax.ShapeDtypeStruct((depth, cols), jnp.float32),
            jax.ShapeDtypeStruct((depth, cols), jnp.float32),
        ],
        compiler_params=pltpu.CompilerParams(dimension_semantics=("arbitrary",)),
    )(layer_weight, s, s, f, vx, vy, vz, d)


def fix_kernel(w_ref, partial_ref, up_ref, prev_ref, next_ref, last_ref, out_ref):
    rows, cols = partial_ref.shape
    depth = up_ref.shape[0]
    corr_first = jnp.zeros((1, cols), jnp.float32)
    corr_last = jnp.zeros((1, cols), jnp.float32)
    for z in range(depth):
        w = w_ref[z]
        corr_first = corr_first - w * (up_ref[pl.ds(z, 1), :] * prev_ref[pl.ds(z, 1), :])
        jump = next_ref[0, pl.ds(z, 1), :] - last_ref[pl.ds(z, 1), :]
        corr_last = corr_last - w * (next_ref[1, pl.ds(z, 1), :] * jump)
    row = lax.broadcasted_iota(jnp.int32, (rows, cols), 0)
    out_ref[...] = (
        partial_ref[...] + jnp.where(row == 0, corr_first, 0.0) + jnp.where(row == rows - 1, corr_last, 0.0)
    )


def corrected(w, partial, up_x0, from_prev, from_next, last_s):
    vmem = pl.BlockSpec(memory_space=pltpu.VMEM)
    return pl.pallas_call(
        fix_kernel,
        in_specs=[pl.BlockSpec(memory_space=pltpu.SMEM)] + [vmem] * 5,
        out_shape=jax.ShapeDtypeStruct(partial.shape, jnp.float32),
    )(w, partial, up_x0, from_prev, from_next, last_s)


def gather_rounds(count):
    bits = []
    bit = count // 2
    while bit >= 4:
        bits.append(bit)
        bit //= 2
    if len(bits) < 2:
        return [[b] for b in bits]
    return [[bits[1], bits[0], bits[0] | bits[1]]] + [[b] for b in bits[2:]]


def swap(value, axis, mask):
    count = lax.axis_size(axis)
    return lax.ppermute(value, axis, [(i, i ^ mask) for i in range(count)])


def cx_slab(cov_rows, offsets, device, rows):
    nxb = offsets.shape[0]
    global_rows = device * rows + jnp.arange(rows)
    row_block = global_rows // BLK
    target = (row_block[:, None] + offsets[row_block]) % nxb
    blocks = jnp.arange(nxb)
    hit = target[:, :, None, None] == blocks[None, None, :, None]
    slab = jnp.sum(jnp.where(hit, cov_rows.astype(jnp.float32)[:, :, None, :], 0.0), axis=1)
    return slab.reshape(rows, -1)


def mixed_rows(local, slab, axis):
    count = lax.axis_size(axis)
    me = lax.axis_index(axis)
    rows = local.shape[0]
    lines = count // 4
    per_device = slab.reshape(slab.shape[0], count, rows)
    devices = jnp.arange(lines, dtype=jnp.int32) * 4 + me % 4
    cols = jnp.take(per_device, devices, axis=1).reshape(slab.shape[0], -1)
    spread = jnp.broadcast_to(local[None], (lines,) + local.shape)
    got = lax.all_to_all(spread, axis[0], 0, 0, tiled=True)
    total = jnp.dot(cols, got.reshape(-1, local.shape[-1]), precision=precise, preferred_element_type=jnp.float32)
    parts = total.reshape(4, rows, total.shape[-1])
    near = parts[0::2] + swap(parts[1::2], axis, 1)
    return near[0] + swap(near[1], axis, 2)


def body(
    adjoint_state,
    speed_x,
    speed_y,
    speed_z,
    dispersion,
    face_flags,
    layer_weight,
    cov_x,
    offsets_x,
    cov_y,
    offsets_y,
):
    count = lax.axis_size(AX)
    me = lax.axis_index(AX)
    depth, rows, cols = adjoint_state.shape

    partial, to_prev, last_s, up_x0 = stencil(
        layer_weight, adjoint_state, face_flags, speed_x, speed_y, speed_z, dispersion
    )
    from_next = passed_along(to_prev, AX, -1)
    from_prev = passed_along(last_s, AX, 1)

    recharge = corrected(layer_weight, partial, up_x0, from_prev, from_next, last_s)

    own_slab = cx_slab(cov_x, offsets_x, me, rows)
    slab = jnp.concatenate([own_slab] + [swap(own_slab, AX, m) for m in (1, 2, 3)], axis=0)
    mixed = mixed_rows(recharge, slab, AX)

    nyb = offsets_y.shape[0]
    col_block = (jnp.arange(nyb)[:, None] + offsets_y) % nyb
    picked = jnp.take(mixed.reshape(rows, nyb, BLK), col_block, axis=1)
    prior = jnp.einsum(
        "xrkc,rikc->xri",
        picked,
        cov_y.reshape(nyb, BLK, cov_y.shape[1], BLK),
        precision=precise,
        preferred_element_type=jnp.float32,
    ).reshape(rows, cols)
    return (recharge, prior)


def solution(mesh):
    count = mesh.shape["gx"]
    split = Mesh(mesh.devices.reshape(mesh.shape["grp"], count // 4, 2, 2), ("grp",) + AX)
    field = P(None, ("grp",) + AX, None)
    return jax.shard_map(
        body,
        mesh=split,
        in_specs=(field, field, field, field, field, field, P(), P(AX, None, None), P(), P(), P()),
        out_specs=(P(("grp",) + AX, None), P(("grp",) + AX, None)),
        check_vma=False,
    )
```

```python
import jax
import jax.numpy as jnp
from jax import lax
from jax.experimental import pallas as pl
from jax.experimental.pallas import tpu as pltpu
from jax.sharding import PartitionSpec as P

BLK = 128
Z_CHUNK = 8

precise = lax.Precision.HIGH


def passed_along(value, axis, steps):
    count = lax.axis_size(axis)
    first, last = (max(0, -steps), min(count, count - steps))
    return lax.ppermute(value, axis, [(source, source + steps) for source in range(first, last)])


def coefs(flags, bit, speed, spread):
    on = (flags & bit) != 0
    lower = spread + jnp.where(on, speed, 0.0)
    upper = spread + jnp.where(on, 0.0, speed)
    return lower, upper


def stencil_kernel(w_ref, s_ref, sprev_ref, f_ref, vx_ref, vy_ref, vz_ref, d_ref, out_ref, to_prev_ref, last_ref, up_ref):
    c = pl.program_id(0)
    rows, cols = out_ref.shape
    sub = lax.broadcasted_iota(jnp.int32, (rows, cols), 0)
    lane = lax.broadcasted_iota(jnp.int32, (rows, cols), 1)

    @pl.when(c == 0)
    def _():
        out_ref[...] = jnp.zeros_like(out_ref)

    prev = jnp.where(c > 0, sprev_ref[0], 0.0)
    acc = jnp.zeros((rows, cols), jnp.float32)
    for j in range(s_ref.shape[0]):
        z = c * s_ref.shape[0] + j
        s = s_ref[j]
        f = f_ref[j]
        d = d_ref[j]
        lo_x, up_x = coefs(f, 1, vx_ref[j], d)
        to_prev_ref[0, pl.ds(z, 1), :] = s[0:1, :]
        to_prev_ref[1, pl.ds(z, 1), :] = lo_x[0:1, :]
        last_ref[pl.ds(z, 1), :] = s[rows - 1:rows, :]
        up_ref[pl.ds(z, 1), :] = up_x[0:1, :]
        lo_y, up_y = coefs(f, 2, vy_ref[j], d)
        lo_z, up_z = coefs(f, 4, vz_ref[j], d)
        s_xm = jnp.where(sub == 0, 0.0, pltpu.roll(s, 1, 0))
        jx = s - s_xm
        ax = lo_x * jx
        ax_next = jnp.where(sub == rows - 1, 0.0, pltpu.roll(ax, rows - 1, 0))
        img = up_x * jx - ax_next
        s_ym = jnp.where(lane == 0, 0.0, pltpu.roll(s, 1, 1))
        jy = s - s_ym
        ay = lo_y * jy
        ay_next = jnp.where(lane == cols - 1, 0.0, pltpu.roll(ay, cols - 1, 1))
        img = img + (up_y * jy - ay_next)
        jz = s - prev
        img = img + up_z * jz
        acc = acc + w_ref[z] * img
        w_before = jnp.where(z > 0, w_ref[jnp.maximum(z - 1, 0)], 0.0)
        acc = acc - w_before * (lo_z * jz)
        prev = s
    out_ref[...] += acc


def stencil(layer_weight, s, f, vx, vy, vz, d):
    depth, rows, cols = s.shape
    zc = Z_CHUNK if depth % Z_CHUNK == 0 else depth
    block = pl.BlockSpec((zc, rows, cols), lambda c: (c, 0, 0))
    prev_block = pl.BlockSpec((1, rows, cols), lambda c: (jnp.maximum(c * zc - 1, 0), 0, 0))
    return pl.pallas_call(
        stencil_kernel,
        grid=(depth // zc,),
        in_specs=[
            pl.BlockSpec(memory_space=pltpu.SMEM),
            block,
            prev_block,
            block,
            block,
            block,
            block,
            block,
        ],
        out_specs=[
            pl.BlockSpec((rows, cols), lambda c: (0, 0)),
            pl.BlockSpec((2, depth, cols), lambda c: (0, 0, 0)),
            pl.BlockSpec((depth, cols), lambda c: (0, 0)),
            pl.BlockSpec((depth, cols), lambda c: (0, 0)),
        ],
        out_shape=[
            jax.ShapeDtypeStruct((rows, cols), jnp.float32),
            jax.ShapeDtypeStruct((2, depth, cols), jnp.float32),
            jax.ShapeDtypeStruct((depth, cols), jnp.float32),
            jax.ShapeDtypeStruct((depth, cols), jnp.float32),
        ],
        compiler_params=pltpu.CompilerParams(dimension_semantics=("arbitrary",)),
    )(layer_weight, s, s, f, vx, vy, vz, d)


def fix_kernel(w_ref, partial_ref, up_ref, prev_ref, next_ref, last_ref, out_ref):
    rows, cols = partial_ref.shape
    depth = up_ref.shape[0]
    corr_first = jnp.zeros((1, cols), jnp.float32)
    corr_last = jnp.zeros((1, cols), jnp.float32)
    for z in range(depth):
        w = w_ref[z]
        corr_first = corr_first - w * (up_ref[pl.ds(z, 1), :] * prev_ref[pl.ds(z, 1), :])
        jump = next_ref[0, pl.ds(z, 1), :] - last_ref[pl.ds(z, 1), :]
        corr_last = corr_last - w * (next_ref[1, pl.ds(z, 1), :] * jump)
    row = lax.broadcasted_iota(jnp.int32, (rows, cols), 0)
    out_ref[...] = (
        partial_ref[...] + jnp.where(row == 0, corr_first, 0.0) + jnp.where(row == rows - 1, corr_last, 0.0)
    )


def corrected(w, partial, up_x0, from_prev, from_next, last_s):
    vmem = pl.BlockSpec(memory_space=pltpu.VMEM)
    return pl.pallas_call(
        fix_kernel,
        in_specs=[pl.BlockSpec(memory_space=pltpu.SMEM)] + [vmem] * 5,
        out_shape=jax.ShapeDtypeStruct(partial.shape, jnp.float32),
    )(w, partial, up_x0, from_prev, from_next, last_s)


def gather_rounds(count):
    bits = []
    bit = count // 2
    while bit >= 4:
        bits.append(bit)
        bit //= 2
    if len(bits) < 2:
        return [[b] for b in bits]
    return [[bits[1], bits[0], bits[0] | bits[1]]] + [[b] for b in bits[2:]]


def swap(value, axis, mask):
    count = lax.axis_size(axis)
    return lax.ppermute(value, axis, [(i, i ^ mask) for i in range(count)])


def cx_slab(cov_rows, offsets, device, rows):
    nxb = offsets.shape[0]
    global_rows = device * rows + jnp.arange(rows)
    row_block = global_rows // BLK
    target = (row_block[:, None] + offsets[row_block]) % nxb
    blocks = jnp.arange(nxb)
    hit = target[:, :, None, None] == blocks[None, None, :, None]
    slab = jnp.sum(jnp.where(hit, cov_rows.astype(jnp.float32)[:, :, None, :], 0.0), axis=1)
    return slab.reshape(rows, -1)


def mixed_rows(local, slab, axis):
    count = lax.axis_size(axis)
    me = lax.axis_index(axis)
    rows = local.shape[0]
    per_device = slab.reshape(slab.shape[0], count, rows)

    def product(piece, masks):
        cols = jnp.take(per_device, me ^ jnp.array(masks, jnp.int32), axis=1).reshape(slab.shape[0], -1)
        return jnp.dot(cols, piece.reshape(-1, piece.shape[-1]), precision=precise, preferred_element_type=jnp.float32)

    buf = local[None]
    entries = [0]
    total = product(buf, entries)
    for masks in gather_rounds(count):
        others = [swap(buf, axis, m) for m in masks]
        for m, other in zip(masks, others):
            total = total + product(other, [m ^ q for q in entries])
        buf = jnp.concatenate([buf] + others, axis=0)
        entries = entries + [m ^ q for m in masks for q in entries]
    parts = total.reshape(4, rows, total.shape[-1])
    got = swap(parts[1::2], axis, 1)
    near = parts[0::2] + got
    return near[0] + swap(near[1], axis, 2)


def body(
    adjoint_state,
    speed_x,
    speed_y,
    speed_z,
    dispersion,
    face_flags,
    layer_weight,
    cov_x,
    offsets_x,
    cov_y,
    offsets_y,
):
    count = lax.axis_size("gx")
    me = lax.axis_index("gx")
    depth, rows, cols = adjoint_state.shape

    partial, to_prev, last_s, up_x0 = stencil(
        layer_weight, adjoint_state, face_flags, speed_x, speed_y, speed_z, dispersion
    )
    from_next = passed_along(to_prev, "gx", -1)
    from_prev = passed_along(last_s, "gx", 1)

    recharge = corrected(layer_weight, partial, up_x0, from_prev, from_next, last_s)

    own_slab = cx_slab(cov_x, offsets_x, me, rows)
    pair_slab = jnp.concatenate([own_slab, swap(own_slab, "gx", 1)], axis=0)
    late_pair, _ = lax.optimization_barrier((pair_slab, recharge))
    slab = jnp.concatenate([pair_slab, swap(late_pair, "gx", 2)], axis=0)
    mixed = mixed_rows(recharge, slab, "gx")

    nyb = offsets_y.shape[0]
    col_block = (jnp.arange(nyb)[:, None] + offsets_y) % nyb
    picked = jnp.take(mixed.reshape(rows, nyb, BLK), col_block, axis=1)
    prior = jnp.einsum(
        "xrkc,rikc->xri",
        picked,
        cov_y.reshape(nyb, BLK, cov_y.shape[1], BLK),
        precision=precise,
        preferred_element_type=jnp.float32,
    ).reshape(rows, cols)
    return (recharge, prior)


def solution(mesh):
    return jax.shard_map(
        body,
        mesh=mesh,
        in_specs=(
            P(None, ("grp", "gx"), None),
            P(None, ("grp", "gx"), None),
            P(None, ("grp", "gx"), None),
            P(None, ("grp", "gx"), None),
            P(None, ("grp", "gx"), None),
            P(None, ("grp", "gx"), None),
            P(),
            P("gx", None, None),
            P(),
            P(),
            P(),
        ),
        out_specs=(P(("grp", "gx"), None), P(("grp", "gx"), None)),
        check_vma=False,
    )
```

```python
import jax
import jax.numpy as jnp
from jax import lax
from jax.experimental import pallas as pl
from jax.experimental.pallas import tpu as pltpu
from jax.sharding import PartitionSpec as P

BLK = 128
Z_CHUNK = 8

precise = lax.Precision.HIGH


def passed_along(value, axis, steps):
    count = lax.axis_size(axis)
    first, last = (max(0, -steps), min(count, count - steps))
    return lax.ppermute(value, axis, [(source, source + steps) for source in range(first, last)])


def coefs(flags, bit, speed, spread):
    on = (flags & bit) != 0
    lower = spread + jnp.where(on, speed, 0.0)
    upper = spread + jnp.where(on, 0.0, speed)
    return lower, upper


def stencil_kernel(
    w_ref, s_ref, sprev_ref, f_ref, vx_ref, vy_ref, vz_ref, d_ref, planes_ref, out_ref, to_prev_ref, last_ref, up_ref
):
    c = pl.program_id(0)
    rows, cols = out_ref.shape
    sub = lax.broadcasted_iota(jnp.int32, (rows, cols), 0)
    lane = lax.broadcasted_iota(jnp.int32, (rows, cols), 1)

    @pl.when(c == 0)
    def _():
        out_ref[...] = jnp.zeros_like(out_ref)
        to_prev_ref[2:] = planes_ref[...]
        last_ref[1:] = planes_ref[...]

    prev = jnp.where(c > 0, sprev_ref[0], 0.0)
    acc = jnp.zeros((rows, cols), jnp.float32)
    for j in range(s_ref.shape[0]):
        z = c * s_ref.shape[0] + j
        s = s_ref[j]
        f = f_ref[j]
        d = d_ref[j]
        lo_x, up_x = coefs(f, 1, vx_ref[j], d)
        to_prev_ref[0, pl.ds(z, 1), :] = s[0:1, :]
        to_prev_ref[1, pl.ds(z, 1), :] = lo_x[0:1, :]
        last_ref[0, pl.ds(z, 1), :] = s[rows - 1:rows, :]
        up_ref[pl.ds(z, 1), :] = up_x[0:1, :]
        lo_y, up_y = coefs(f, 2, vy_ref[j], d)
        lo_z, up_z = coefs(f, 4, vz_ref[j], d)
        s_xm = jnp.where(sub == 0, 0.0, pltpu.roll(s, 1, 0))
        jx = s - s_xm
        ax = lo_x * jx
        ax_next = jnp.where(sub == rows - 1, 0.0, pltpu.roll(ax, rows - 1, 0))
        img = up_x * jx - ax_next
        s_ym = jnp.where(lane == 0, 0.0, pltpu.roll(s, 1, 1))
        jy = s - s_ym
        ay = lo_y * jy
        ay_next = jnp.where(lane == cols - 1, 0.0, pltpu.roll(ay, cols - 1, 1))
        img = img + (up_y * jy - ay_next)
        jz = s - prev
        img = img + up_z * jz
        acc = acc + w_ref[z] * img
        w_before = jnp.where(z > 0, w_ref[jnp.maximum(z - 1, 0)], 0.0)
        acc = acc - w_before * (lo_z * jz)
        prev = s
    out_ref[...] += acc


def stencil(layer_weight, s, f, vx, vy, vz, d, planes):
    depth, rows, cols = s.shape
    extra = planes.shape[0]
    zc = Z_CHUNK if depth % Z_CHUNK == 0 else depth
    block = pl.BlockSpec((zc, rows, cols), lambda c: (c, 0, 0))
    prev_block = pl.BlockSpec((1, rows, cols), lambda c: (jnp.maximum(c * zc - 1, 0), 0, 0))
    return pl.pallas_call(
        stencil_kernel,
        grid=(depth // zc,),
        in_specs=[
            pl.BlockSpec(memory_space=pltpu.SMEM),
            block,
            prev_block,
            block,
            block,
            block,
            block,
            block,
            pl.BlockSpec(planes.shape, lambda c: (0, 0, 0)),
        ],
        out_specs=[
            pl.BlockSpec((rows, cols), lambda c: (0, 0)),
            pl.BlockSpec((2 + extra, depth, cols), lambda c: (0, 0, 0)),
            pl.BlockSpec((1 + extra, depth, cols), lambda c: (0, 0, 0)),
            pl.BlockSpec((depth, cols), lambda c: (0, 0)),
        ],
        out_shape=[
            jax.ShapeDtypeStruct((rows, cols), jnp.float32),
            jax.ShapeDtypeStruct((2 + extra, depth, cols), jnp.float32),
            jax.ShapeDtypeStruct((1 + extra, depth, cols), jnp.float32),
            jax.ShapeDtypeStruct((depth, cols), jnp.float32),
        ],
        compiler_params=pltpu.CompilerParams(dimension_semantics=("arbitrary",)),
    )(layer_weight, s, s, f, vx, vy, vz, d, planes)


def fix_kernel(w_ref, partial_ref, up_ref, prev_ref, next_ref, last_ref, out_ref):
    rows, cols = partial_ref.shape
    depth = up_ref.shape[0]
    corr_first = jnp.zeros((1, cols), jnp.float32)
    corr_last = jnp.zeros((1, cols), jnp.float32)
    for z in range(depth):
        w = w_ref[z]
        corr_first = corr_first - w * (up_ref[pl.ds(z, 1), :] * prev_ref[0, pl.ds(z, 1), :])
        jump = next_ref[0, pl.ds(z, 1), :] - last_ref[0, pl.ds(z, 1), :]
        corr_last = corr_last - w * (next_ref[1, pl.ds(z, 1), :] * jump)
    row = lax.broadcasted_iota(jnp.int32, (rows, cols), 0)
    out_ref[...] = (
        partial_ref[...] + jnp.where(row == 0, corr_first, 0.0) + jnp.where(row == rows - 1, corr_last, 0.0)
    )


def corrected(w, partial, up_x0, from_prev, from_next, last_s):
    vmem = pl.BlockSpec(memory_space=pltpu.VMEM)
    return pl.pallas_call(
        fix_kernel,
        in_specs=[pl.BlockSpec(memory_space=pltpu.SMEM)] + [vmem] * 5,
        out_shape=jax.ShapeDtypeStruct(partial.shape, jnp.float32),
    )(w, partial, up_x0, from_prev, from_next, last_s)


def gather_rounds(count):
    bits = []
    bit = count // 2
    while bit >= 4:
        bits.append(bit)
        bit //= 2
    if len(bits) < 2:
        return [[b] for b in bits]
    return [[bits[1], bits[0], bits[0] | bits[1]]] + [[b] for b in bits[2:]]


def swap(value, axis, mask):
    count = lax.axis_size(axis)
    return lax.ppermute(value, axis, [(i, i ^ mask) for i in range(count)])


def cx_slab(cov_rows, offsets, device, rows):
    nxb = offsets.shape[0]
    global_rows = device * rows + jnp.arange(rows)
    row_block = global_rows // BLK
    target = (row_block[:, None] + offsets[row_block]) % nxb
    blocks = jnp.arange(nxb)
    hit = target[:, :, None, None] == blocks[None, None, :, None]
    slab = jnp.sum(jnp.where(hit, cov_rows.astype(jnp.float32)[:, :, None, :], 0.0), axis=1)
    return slab.reshape(rows, -1)


def mixed_rows(local, slab, axis):
    count = lax.axis_size(axis)
    me = lax.axis_index(axis)
    rows = local.shape[0]
    per_device = slab.reshape(slab.shape[0], count, rows)

    def product(piece, masks):
        cols = jnp.take(per_device, me ^ jnp.array(masks, jnp.int32), axis=1).reshape(slab.shape[0], -1)
        return jnp.dot(cols, piece.reshape(-1, piece.shape[-1]), precision=precise, preferred_element_type=jnp.float32)

    buf = local[None]
    entries = [0]
    total = product(buf, entries)
    for masks in gather_rounds(count):
        others = [swap(buf, axis, m) for m in masks]
        for m, other in zip(masks, others):
            total = total + product(other, [m ^ q for q in entries])
        buf = jnp.concatenate([buf] + others, axis=0)
        entries = entries + [m ^ q for m in masks for q in entries]
    parts = total.reshape(4, rows, total.shape[-1])
    got = swap(parts[1::2], axis, 1)
    near = parts[0::2] + got
    return near[0] + swap(near[1], axis, 2)


def body(
    adjoint_state,
    speed_x,
    speed_y,
    speed_z,
    dispersion,
    face_flags,
    layer_weight,
    cov_x,
    offsets_x,
    cov_y,
    offsets_y,
):
    count = lax.axis_size("gx")
    me = lax.axis_index("gx")
    depth, rows, cols = adjoint_state.shape

    own_slab = cx_slab(cov_x, offsets_x, me, rows)
    flat = own_slab.reshape(-1)
    plane = depth * cols
    extra = -(-flat.shape[0] // plane)
    planes = jnp.pad(flat, (0, extra * plane - flat.shape[0])).reshape(extra, depth, cols)
    partial, to_prev, last_ext, up_x0 = stencil(
        layer_weight, adjoint_state, face_flags, speed_x, speed_y, speed_z, dispersion, planes
    )
    from_next = passed_along(to_prev, "gx", -1)
    from_prev = passed_along(last_ext, "gx", 1)

    recharge = corrected(layer_weight, partial, up_x0, from_prev, from_next, last_ext)

    size = own_slab.size
    from_up = from_next[2:].reshape(-1)[:size].reshape(own_slab.shape)
    from_down = from_prev[1:].reshape(-1)[:size].reshape(own_slab.shape)
    partner_slab = jnp.where(me % 2 == 0, from_up, from_down)
    pair_slab = jnp.concatenate([own_slab, partner_slab], axis=0)
    late_pair, _ = lax.optimization_barrier((pair_slab, recharge))
    slab = jnp.concatenate([pair_slab, swap(late_pair, "gx", 2)], axis=0)
    mixed = mixed_rows(recharge, slab, "gx")

    nyb = offsets_y.shape[0]
    col_block = (jnp.arange(nyb)[:, None] + offsets_y) % nyb
    picked = jnp.take(mixed.reshape(rows, nyb, BLK), col_block, axis=1)
    prior = jnp.einsum(
        "xrkc,rikc->xri",
        picked,
        cov_y.reshape(nyb, BLK, cov_y.shape[1], BLK),
        precision=precise,
        preferred_element_type=jnp.float32,
    ).reshape(rows, cols)
    return (recharge, prior)


def solution(mesh):
    return jax.shard_map(
        body,
        mesh=mesh,
        in_specs=(
            P(None, ("grp", "gx"), None),
            P(None, ("grp", "gx"), None),
            P(None, ("grp", "gx"), None),
            P(None, ("grp", "gx"), None),
            P(None, ("grp", "gx"), None),
            P(None, ("grp", "gx"), None),
            P(),
            P("gx", None, None),
            P(),
            P(),
            P(),
        ),
        out_specs=(P(("grp", "gx"), None), P(("grp", "gx"), None)),
        check_vma=False,
    )
```

```python
import jax
import jax.numpy as jnp
from jax import lax
from jax.experimental import pallas as pl
from jax.experimental.pallas import tpu as pltpu
from jax.sharding import PartitionSpec as P

BLK = 128
Z_CHUNK = 8

precise = lax.Precision.HIGH


def passed_along(value, axis, steps):
    count = lax.axis_size(axis)
    first, last = (max(0, -steps), min(count, count - steps))
    return lax.ppermute(value, axis, [(source, source + steps) for source in range(first, last)])


def coefs(flags, bit, speed, spread):
    on = (flags & bit) != 0
    lower = spread + jnp.where(on, speed, 0.0)
    upper = spread + jnp.where(on, 0.0, speed)
    return lower, upper


def stencil_kernel(w_ref, s_ref, sprev_ref, f_ref, vx_ref, vy_ref, vz_ref, d_ref, out_ref, to_prev_ref, last_ref, up_ref):
    c = pl.program_id(0)
    rows, cols = out_ref.shape
    sub = lax.broadcasted_iota(jnp.int32, (rows, cols), 0)
    lane = lax.broadcasted_iota(jnp.int32, (rows, cols), 1)

    @pl.when(c == 0)
    def _():
        out_ref[...] = jnp.zeros_like(out_ref)

    prev = jnp.where(c > 0, sprev_ref[0], 0.0)
    acc = jnp.zeros((rows, cols), jnp.float32)
    for j in range(s_ref.shape[0]):
        z = c * s_ref.shape[0] + j
        s = s_ref[j]
        f = f_ref[j]
        d = d_ref[j]
        lo_x, up_x = coefs(f, 1, vx_ref[j], d)
        to_prev_ref[0, pl.ds(z, 1), :] = s[0:1, :]
        to_prev_ref[1, pl.ds(z, 1), :] = lo_x[0:1, :]
        last_ref[pl.ds(z, 1), :] = s[rows - 1:rows, :]
        up_ref[pl.ds(z, 1), :] = up_x[0:1, :]
        lo_y, up_y = coefs(f, 2, vy_ref[j], d)
        lo_z, up_z = coefs(f, 4, vz_ref[j], d)
        s_xm = jnp.where(sub == 0, 0.0, pltpu.roll(s, 1, 0))
        jx = s - s_xm
        ax = lo_x * jx
        ax_next = jnp.where(sub == rows - 1, 0.0, pltpu.roll(ax, rows - 1, 0))
        img = up_x * jx - ax_next
        s_ym = jnp.where(lane == 0, 0.0, pltpu.roll(s, 1, 1))
        jy = s - s_ym
        ay = lo_y * jy
        ay_next = jnp.where(lane == cols - 1, 0.0, pltpu.roll(ay, cols - 1, 1))
        img = img + (up_y * jy - ay_next)
        jz = s - prev
        img = img + up_z * jz
        acc = acc + w_ref[z] * img
        w_before = jnp.where(z > 0, w_ref[jnp.maximum(z - 1, 0)], 0.0)
        acc = acc - w_before * (lo_z * jz)
        prev = s
    out_ref[...] += acc


def stencil(layer_weight, s, f, vx, vy, vz, d):
    depth, rows, cols = s.shape
    zc = Z_CHUNK if depth % Z_CHUNK == 0 else depth
    block = pl.BlockSpec((zc, rows, cols), lambda c: (c, 0, 0))
    prev_block = pl.BlockSpec((1, rows, cols), lambda c: (jnp.maximum(c * zc - 1, 0), 0, 0))
    return pl.pallas_call(
        stencil_kernel,
        grid=(depth // zc,),
        in_specs=[
            pl.BlockSpec(memory_space=pltpu.SMEM),
            block,
            prev_block,
            block,
            block,
            block,
            block,
            block,
        ],
        out_specs=[
            pl.BlockSpec((rows, cols), lambda c: (0, 0)),
            pl.BlockSpec((2, depth, cols), lambda c: (0, 0, 0)),
            pl.BlockSpec((depth, cols), lambda c: (0, 0)),
            pl.BlockSpec((depth, cols), lambda c: (0, 0)),
        ],
        out_shape=[
            jax.ShapeDtypeStruct((rows, cols), jnp.float32),
            jax.ShapeDtypeStruct((2, depth, cols), jnp.float32),
            jax.ShapeDtypeStruct((depth, cols), jnp.float32),
            jax.ShapeDtypeStruct((depth, cols), jnp.float32),
        ],
        compiler_params=pltpu.CompilerParams(dimension_semantics=("arbitrary",)),
    )(layer_weight, s, s, f, vx, vy, vz, d)


def fix_kernel(w_ref, partial_ref, up_ref, prev_ref, next_ref, last_ref, out_ref):
    rows, cols = partial_ref.shape
    depth = up_ref.shape[0]
    corr_first = jnp.zeros((1, cols), jnp.float32)
    corr_last = jnp.zeros((1, cols), jnp.float32)
    for z in range(depth):
        w = w_ref[z]
        corr_first = corr_first - w * (up_ref[pl.ds(z, 1), :] * prev_ref[pl.ds(z, 1), :])
        jump = next_ref[0, pl.ds(z, 1), :] - last_ref[pl.ds(z, 1), :]
        corr_last = corr_last - w * (next_ref[1, pl.ds(z, 1), :] * jump)
    row = lax.broadcasted_iota(jnp.int32, (rows, cols), 0)
    out_ref[...] = (
        partial_ref[...] + jnp.where(row == 0, corr_first, 0.0) + jnp.where(row == rows - 1, corr_last, 0.0)
    )


def corrected(w, partial, up_x0, from_prev, from_next, last_s):
    vmem = pl.BlockSpec(memory_space=pltpu.VMEM)
    return pl.pallas_call(
        fix_kernel,
        in_specs=[pl.BlockSpec(memory_space=pltpu.SMEM)] + [vmem] * 5,
        out_shape=jax.ShapeDtypeStruct(partial.shape, jnp.float32),
    )(w, partial, up_x0, from_prev, from_next, last_s)


def gather_rounds(count):
    bits = []
    bit = count // 2
    while bit >= 4:
        bits.append(bit)
        bit //= 2
    if len(bits) < 2:
        return [[b] for b in bits]
    return [[bits[1], bits[0], bits[0] | bits[1]]] + [[b] for b in bits[2:]]


def swap(value, axis, mask):
    count = lax.axis_size(axis)
    return lax.ppermute(value, axis, [(i, i ^ mask) for i in range(count)])


def cx_slab(cov_rows, offsets, device, rows):
    nxb = offsets.shape[0]
    global_rows = device * rows + jnp.arange(rows)
    row_block = global_rows // BLK
    target = (row_block[:, None] + offsets[row_block]) % nxb
    blocks = jnp.arange(nxb)
    hit = target[:, :, None, None] == blocks[None, None, :, None]
    slab = jnp.sum(jnp.where(hit, cov_rows.astype(jnp.float32)[:, :, None, :], 0.0), axis=1)
    return slab.reshape(rows, -1)


def mixed_rows(local, slab, axis):
    count = lax.axis_size(axis)
    me = lax.axis_index(axis)
    rows = local.shape[0]
    per_device = slab.reshape(slab.shape[0], count, rows)

    def product(piece, masks):
        cols = jnp.take(per_device, me ^ jnp.array(masks, jnp.int32), axis=1).reshape(slab.shape[0], -1)
        return jnp.dot(cols, piece.reshape(-1, piece.shape[-1]), precision=precise, preferred_element_type=jnp.float32)

    buf = local[None]
    entries = [0]
    total = product(buf, entries)
    for masks in gather_rounds(count):
        others = [swap(buf, axis, m) for m in masks]
        for m, other in zip(masks, others):
            total = total + product(other, [m ^ q for q in entries])
        buf = jnp.concatenate([buf] + others, axis=0)
        entries = entries + [m ^ q for m in masks for q in entries]
    parts = total.reshape(4, rows, total.shape[-1])
    got = swap(parts[1::2], axis, 1)
    near = parts[0::2] + got
    return near[0] + swap(near[1], axis, 2)


def body(
    adjoint_state,
    speed_x,
    speed_y,
    speed_z,
    dispersion,
    face_flags,
    layer_weight,
    cov_x,
    offsets_x,
    cov_y,
    offsets_y,
):
    count = lax.axis_size("gx")
    me = lax.axis_index("gx")
    depth, rows, cols = adjoint_state.shape

    partial, to_prev, last_s, up_x0 = stencil(
        layer_weight, adjoint_state, face_flags, speed_x, speed_y, speed_z, dispersion
    )
    from_next = passed_along(to_prev, "gx", -1)
    from_prev = passed_along(last_s, "gx", 1)

    recharge = corrected(layer_weight, partial, up_x0, from_prev, from_next, last_s)

    own_slab = cx_slab(cov_x, offsets_x, me, rows)
    pair_slab = jnp.concatenate([own_slab, swap(own_slab, "gx", 1)], axis=0)
    late_pair, _ = lax.optimization_barrier((pair_slab, recharge))
    slab = jnp.concatenate([pair_slab, swap(late_pair, "gx", 2)], axis=0)
    mixed = mixed_rows(recharge, slab, "gx")

    nyb = offsets_y.shape[0]
    col_block = (jnp.arange(nyb)[:, None] + offsets_y) % nyb
    blocks_y = mixed.reshape(rows, nyb, BLK)
    fixed = [blocks_y, jnp.roll(blocks_y, 1, axis=1), jnp.roll(blocks_y, -(nyb // 2), axis=1)]
    rest = jnp.take(blocks_y, col_block[:, 3:], axis=1)
    picked = jnp.concatenate([jnp.stack(fixed, axis=2), rest], axis=2)
    prior = jnp.einsum(
        "xrkc,rikc->xri",
        picked,
        cov_y.reshape(nyb, BLK, cov_y.shape[1], BLK),
        precision=precise,
        preferred_element_type=jnp.float32,
    ).reshape(rows, cols)
    return (recharge, prior)


def solution(mesh):
    return jax.shard_map(
        body,
        mesh=mesh,
        in_specs=(
            P(None, ("grp", "gx"), None),
            P(None, ("grp", "gx"), None),
            P(None, ("grp", "gx"), None),
            P(None, ("grp", "gx"), None),
            P(None, ("grp", "gx"), None),
            P(None, ("grp", "gx"), None),
            P(),
            P("gx", None, None),
            P(),
            P(),
            P(),
        ),
        out_specs=(P(("grp", "gx"), None), P(("grp", "gx"), None)),
        check_vma=False,
    )
```

```python
import jax
import jax.numpy as jnp
from jax import lax
from jax.experimental import pallas as pl
from jax.experimental.pallas import tpu as pltpu
from jax.sharding import PartitionSpec as P

BLK = 128
Z_CHUNK = 8

precise = lax.Precision.HIGH


def passed_along(value, axis, steps):
    count = lax.axis_size(axis)
    first, last = (max(0, -steps), min(count, count - steps))
    return lax.ppermute(value, axis, [(source, source + steps) for source in range(first, last)])


def coefs(flags, bit, speed, spread):
    on = (flags & bit) != 0
    lower = spread + jnp.where(on, speed, 0.0)
    upper = spread + jnp.where(on, 0.0, speed)
    return lower, upper


def stencil_kernel(w_ref, s_ref, sprev_ref, f_ref, vx_ref, vy_ref, vz_ref, d_ref, out_ref, to_prev_ref, last_ref, up_ref):
    c = pl.program_id(0)
    rows, cols = out_ref.shape
    sub = lax.broadcasted_iota(jnp.int32, (rows, cols), 0)
    lane = lax.broadcasted_iota(jnp.int32, (rows, cols), 1)

    @pl.when(c == 0)
    def _():
        out_ref[...] = jnp.zeros_like(out_ref)

    prev = jnp.where(c > 0, sprev_ref[0], 0.0)
    acc = jnp.zeros((rows, cols), jnp.float32)
    for j in range(s_ref.shape[0]):
        z = c * s_ref.shape[0] + j
        s = s_ref[j]
        f = f_ref[j]
        d = d_ref[j]
        lo_x, up_x = coefs(f, 1, vx_ref[j], d)
        to_prev_ref[0, pl.ds(z, 1), :] = s[0:1, :]
        to_prev_ref[1, pl.ds(z, 1), :] = lo_x[0:1, :]
        last_ref[pl.ds(z, 1), :] = s[rows - 1:rows, :]
        up_ref[pl.ds(z, 1), :] = up_x[0:1, :]
        lo_y, up_y = coefs(f, 2, vy_ref[j], d)
        lo_z, up_z = coefs(f, 4, vz_ref[j], d)
        s_xm = jnp.where(sub == 0, 0.0, pltpu.roll(s, 1, 0))
        jx = s - s_xm
        ax = lo_x * jx
        ax_next = jnp.where(sub == rows - 1, 0.0, pltpu.roll(ax, rows - 1, 0))
        img = up_x * jx - ax_next
        s_ym = jnp.where(lane == 0, 0.0, pltpu.roll(s, 1, 1))
        jy = s - s_ym
        ay = lo_y * jy
        ay_next = jnp.where(lane == cols - 1, 0.0, pltpu.roll(ay, cols - 1, 1))
        img = img + (up_y * jy - ay_next)
        jz = s - prev
        img = img + up_z * jz
        acc = acc + w_ref[z] * img
        w_before = jnp.where(z > 0, w_ref[jnp.maximum(z - 1, 0)], 0.0)
        acc = acc - w_before * (lo_z * jz)
        prev = s
    out_ref[...] += acc


def stencil(layer_weight, s, f, vx, vy, vz, d):
    depth, rows, cols = s.shape
    zc = Z_CHUNK if depth % Z_CHUNK == 0 else depth
    block = pl.BlockSpec((zc, rows, cols), lambda c: (c, 0, 0))
    prev_block = pl.BlockSpec((1, rows, cols), lambda c: (jnp.maximum(c * zc - 1, 0), 0, 0))
    return pl.pallas_call(
        stencil_kernel,
        grid=(depth // zc,),
        in_specs=[
            pl.BlockSpec(memory_space=pltpu.SMEM),
            block,
            prev_block,
            block,
            block,
            block,
            block,
            block,
        ],
        out_specs=[
            pl.BlockSpec((rows, cols), lambda c: (0, 0)),
            pl.BlockSpec((2, depth, cols), lambda c: (0, 0, 0)),
            pl.BlockSpec((depth, cols), lambda c: (0, 0)),
            pl.BlockSpec((depth, cols), lambda c: (0, 0)),
        ],
        out_shape=[
            jax.ShapeDtypeStruct((rows, cols), jnp.float32),
            jax.ShapeDtypeStruct((2, depth, cols), jnp.float32),
            jax.ShapeDtypeStruct((depth, cols), jnp.float32),
            jax.ShapeDtypeStruct((depth, cols), jnp.float32),
        ],
        compiler_params=pltpu.CompilerParams(dimension_semantics=("arbitrary",)),
    )(layer_weight, s, s, f, vx, vy, vz, d)


def fix_kernel(w_ref, partial_ref, up_ref, prev_ref, next_ref, last_ref, out_ref):
    rows, cols = partial_ref.shape
    depth = up_ref.shape[0]
    corr_first = jnp.zeros((1, cols), jnp.float32)
    corr_last = jnp.zeros((1, cols), jnp.float32)
    for z in range(depth):
        w = w_ref[z]
        corr_first = corr_first - w * (up_ref[pl.ds(z, 1), :] * prev_ref[pl.ds(z, 1), :])
        jump = next_ref[0, pl.ds(z, 1), :] - last_ref[pl.ds(z, 1), :]
        corr_last = corr_last - w * (next_ref[1, pl.ds(z, 1), :] * jump)
    row = lax.broadcasted_iota(jnp.int32, (rows, cols), 0)
    out_ref[...] = (
        partial_ref[...] + jnp.where(row == 0, corr_first, 0.0) + jnp.where(row == rows - 1, corr_last, 0.0)
    )


def corrected(w, partial, up_x0, from_prev, from_next, last_s):
    vmem = pl.BlockSpec(memory_space=pltpu.VMEM)
    return pl.pallas_call(
        fix_kernel,
        in_specs=[pl.BlockSpec(memory_space=pltpu.SMEM)] + [vmem] * 5,
        out_shape=jax.ShapeDtypeStruct(partial.shape, jnp.float32),
    )(w, partial, up_x0, from_prev, from_next, last_s)


def gather_rounds(count):
    bits = []
    bit = count // 2
    while bit >= 4:
        bits.append(bit)
        bit //= 2
    if len(bits) < 2:
        return [[b] for b in bits]
    return [[bits[1], bits[0], bits[0] | bits[1]]] + [[b] for b in bits[2:]]


def swap(value, axis, mask):
    count = lax.axis_size(axis)
    return lax.ppermute(value, axis, [(i, i ^ mask) for i in range(count)])


def cx_slab(cov_rows, offsets, device, rows):
    nxb = offsets.shape[0]
    global_rows = device * rows + jnp.arange(rows)
    row_block = global_rows // BLK
    target = (row_block[:, None] + offsets[row_block]) % nxb
    blocks = jnp.arange(nxb)
    hit = target[:, :, None, None] == blocks[None, None, :, None]
    slab = jnp.sum(jnp.where(hit, cov_rows.astype(jnp.float32)[:, :, None, :], 0.0), axis=1)
    return slab.reshape(rows, -1)


def mixed_rows(local, slab, axis):
    count = lax.axis_size(axis)
    me = lax.axis_index(axis)
    rows = local.shape[0]
    per_device = slab.reshape(slab.shape[0], count, rows)

    def product(piece, masks):
        cols = jnp.take(per_device, me ^ jnp.array(masks, jnp.int32), axis=1).reshape(slab.shape[0], -1)
        return jnp.dot(cols, piece.reshape(-1, piece.shape[-1]), precision=precise, preferred_element_type=jnp.float32)

    buf = local[None]
    entries = [0]
    total = product(buf, entries)
    for masks in gather_rounds(count):
        others = [swap(buf, axis, m) for m in masks]
        for m, other in zip(masks, others):
            total = total + product(other, [m ^ q for q in entries])
        buf = jnp.concatenate([buf] + others, axis=0)
        entries = entries + [m ^ q for m in masks for q in entries]
    parts = total.reshape(4, rows, total.shape[-1])
    got = swap(parts[1::2], axis, 1)
    near = parts[0::2] + got
    return near[0] + swap(near[1], axis, 2)


def body(
    adjoint_state,
    speed_x,
    speed_y,
    speed_z,
    dispersion,
    face_flags,
    layer_weight,
    cov_x,
    offsets_x,
    cov_y,
    offsets_y,
):
    count = lax.axis_size("gx")
    me = lax.axis_index("gx")
    depth, rows, cols = adjoint_state.shape

    partial, to_prev, last_s, up_x0 = stencil(
        layer_weight, adjoint_state, face_flags, speed_x, speed_y, speed_z, dispersion
    )
    from_next = passed_along(to_prev, "gx", -1)
    from_prev = passed_along(last_s, "gx", 1)

    recharge = corrected(layer_weight, partial, up_x0, from_prev, from_next, last_s)

    own_slab = cx_slab(cov_x, offsets_x, me, rows)
    pair_slab = jnp.concatenate([own_slab, swap(own_slab, "gx", 1)], axis=0)
    late_pair, _ = lax.optimization_barrier((pair_slab, recharge))
    slab = jnp.concatenate([pair_slab, swap(late_pair, "gx", 2)], axis=0)
    mixed = mixed_rows(recharge, slab, "gx")

    nyb = offsets_y.shape[0]
    col_block = (jnp.arange(nyb)[:, None] + offsets_y) % nyb
    blocks_y = mixed.reshape(rows, nyb, BLK)
    fixed = [blocks_y, jnp.roll(blocks_y, 1, axis=1), jnp.roll(blocks_y, -(nyb // 2), axis=1)]
    hit = col_block[:, 3:, None] == jnp.arange(nyb)[None, None, :]
    rest = jnp.sum(jnp.where(hit[None, :, :, :, None], blocks_y[:, None, None, :, :], 0.0), axis=3)
    picked = jnp.concatenate([jnp.stack(fixed, axis=2), rest], axis=2)
    prior = jnp.einsum(
        "xrkc,rikc->xri",
        picked,
        cov_y.reshape(nyb, BLK, cov_y.shape[1], BLK),
        precision=precise,
        preferred_element_type=jnp.float32,
    ).reshape(rows, cols)
    return (recharge, prior)


def solution(mesh):
    return jax.shard_map(
        body,
        mesh=mesh,
        in_specs=(
            P(None, ("grp", "gx"), None),
            P(None, ("grp", "gx"), None),
            P(None, ("grp", "gx"), None),
            P(None, ("grp", "gx"), None),
            P(None, ("grp", "gx"), None),
            P(None, ("grp", "gx"), None),
            P(),
            P("gx", None, None),
            P(),
            P(),
            P(),
        ),
        out_specs=(P(("grp", "gx"), None), P(("grp", "gx"), None)),
        check_vma=False,
    )
```

```python
import jax
import jax.numpy as jnp
from jax import lax
from jax.experimental import pallas as pl
from jax.experimental.pallas import tpu as pltpu
from jax.sharding import PartitionSpec as P

BLK = 128
Z_CHUNK = 8

precise = lax.Precision.HIGH


def passed_along(value, axis, steps):
    count = lax.axis_size(axis)
    first, last = (max(0, -steps), min(count, count - steps))
    return lax.ppermute(value, axis, [(source, source + steps) for source in range(first, last)])


def coefs(flags, bit, speed, spread):
    on = (flags & bit) != 0
    lower = spread + jnp.where(on, speed, 0.0)
    upper = spread + jnp.where(on, 0.0, speed)
    return lower, upper


def stencil_kernel(w_ref, s_ref, sprev_ref, f_ref, vx_ref, vy_ref, vz_ref, d_ref, out_ref, to_prev_ref, last_ref, up_ref):
    c = pl.program_id(0)
    rows, cols = out_ref.shape
    sub = lax.broadcasted_iota(jnp.int32, (rows, cols), 0)
    lane = lax.broadcasted_iota(jnp.int32, (rows, cols), 1)

    @pl.when(c == 0)
    def _():
        out_ref[...] = jnp.zeros_like(out_ref)

    prev = jnp.where(c > 0, sprev_ref[0], 0.0)
    acc = jnp.zeros((rows, cols), jnp.float32)
    for j in range(s_ref.shape[0]):
        z = c * s_ref.shape[0] + j
        s = s_ref[j]
        f = f_ref[j]
        d = d_ref[j]
        lo_x, up_x = coefs(f, 1, vx_ref[j], d)
        to_prev_ref[0, pl.ds(z, 1), :] = s[0:1, :]
        to_prev_ref[1, pl.ds(z, 1), :] = lo_x[0:1, :]
        last_ref[pl.ds(z, 1), :] = s[rows - 1:rows, :]
        up_ref[pl.ds(z, 1), :] = up_x[0:1, :]
        lo_y, up_y = coefs(f, 2, vy_ref[j], d)
        lo_z, up_z = coefs(f, 4, vz_ref[j], d)
        s_xm = jnp.where(sub == 0, 0.0, pltpu.roll(s, 1, 0))
        jx = s - s_xm
        ax = lo_x * jx
        ax_next = jnp.where(sub == rows - 1, 0.0, pltpu.roll(ax, rows - 1, 0))
        img = up_x * jx - ax_next
        s_ym = jnp.where(lane == 0, 0.0, pltpu.roll(s, 1, 1))
        jy = s - s_ym
        ay = lo_y * jy
        ay_next = jnp.where(lane == cols - 1, 0.0, pltpu.roll(ay, cols - 1, 1))
        img = img + (up_y * jy - ay_next)
        jz = s - prev
        img = img + up_z * jz
        acc = acc + w_ref[z] * img
        w_before = jnp.where(z > 0, w_ref[jnp.maximum(z - 1, 0)], 0.0)
        acc = acc - w_before * (lo_z * jz)
        prev = s
    out_ref[...] += acc


def stencil(layer_weight, s, f, vx, vy, vz, d):
    depth, rows, cols = s.shape
    zc = Z_CHUNK if depth % Z_CHUNK == 0 else depth
    block = pl.BlockSpec((zc, rows, cols), lambda c: (c, 0, 0))
    prev_block = pl.BlockSpec((1, rows, cols), lambda c: (jnp.maximum(c * zc - 1, 0), 0, 0))
    return pl.pallas_call(
        stencil_kernel,
        grid=(depth // zc,),
        in_specs=[
            pl.BlockSpec(memory_space=pltpu.SMEM),
            block,
            prev_block,
            block,
            block,
            block,
            block,
            block,
        ],
        out_specs=[
            pl.BlockSpec((rows, cols), lambda c: (0, 0)),
            pl.BlockSpec((2, depth, cols), lambda c: (0, 0, 0)),
            pl.BlockSpec((depth, cols), lambda c: (0, 0)),
            pl.BlockSpec((depth, cols), lambda c: (0, 0)),
        ],
        out_shape=[
            jax.ShapeDtypeStruct((rows, cols), jnp.float32),
            jax.ShapeDtypeStruct((2, depth, cols), jnp.float32),
            jax.ShapeDtypeStruct((depth, cols), jnp.float32),
            jax.ShapeDtypeStruct((depth, cols), jnp.float32),
        ],
        compiler_params=pltpu.CompilerParams(dimension_semantics=("arbitrary",)),
    )(layer_weight, s, s, f, vx, vy, vz, d)


def fix_kernel(w_ref, partial_ref, up_ref, prev_ref, next_ref, last_ref, out_ref):
    rows, cols = partial_ref.shape
    depth = up_ref.shape[0]
    corr_first = jnp.zeros((1, cols), jnp.float32)
    corr_last = jnp.zeros((1, cols), jnp.float32)
    for z in range(depth):
        w = w_ref[z]
        corr_first = corr_first - w * (up_ref[pl.ds(z, 1), :] * prev_ref[pl.ds(z, 1), :])
        jump = next_ref[0, pl.ds(z, 1), :] - last_ref[pl.ds(z, 1), :]
        corr_last = corr_last - w * (next_ref[1, pl.ds(z, 1), :] * jump)
    row = lax.broadcasted_iota(jnp.int32, (rows, cols), 0)
    out_ref[...] = (
        partial_ref[...] + jnp.where(row == 0, corr_first, 0.0) + jnp.where(row == rows - 1, corr_last, 0.0)
    )


def corrected(w, partial, up_x0, from_prev, from_next, last_s):
    vmem = pl.BlockSpec(memory_space=pltpu.VMEM)
    return pl.pallas_call(
        fix_kernel,
        in_specs=[pl.BlockSpec(memory_space=pltpu.SMEM)] + [vmem] * 5,
        out_shape=jax.ShapeDtypeStruct(partial.shape, jnp.float32),
    )(w, partial, up_x0, from_prev, from_next, last_s)


def gather_rounds(count):
    bits = []
    bit = count // 2
    while bit >= 4:
        bits.append(bit)
        bit //= 2
    if len(bits) < 2:
        return [[b] for b in bits]
    return [[bits[1], bits[0], bits[0] | bits[1]]] + [[b] for b in bits[2:]]


def swap(value, axis, mask):
    count = lax.axis_size(axis)
    return lax.ppermute(value, axis, [(i, i ^ mask) for i in range(count)])


def cx_slab(cov_rows, offsets, device, rows):
    nxb = offsets.shape[0]
    global_rows = device * rows + jnp.arange(rows)
    row_block = global_rows // BLK
    target = (row_block[:, None] + offsets[row_block]) % nxb
    blocks = jnp.arange(nxb)
    hit = target[:, :, None, None] == blocks[None, None, :, None]
    slab = jnp.sum(jnp.where(hit, cov_rows.astype(jnp.float32)[:, :, None, :], 0.0), axis=1)
    return slab.reshape(rows, -1)


def mixed_rows(local, slab, axis):
    count = lax.axis_size(axis)
    me = lax.axis_index(axis)
    rows = local.shape[0]
    per_device = slab.reshape(slab.shape[0], count, rows)

    def product(piece, masks):
        hit = (me ^ jnp.array(masks, jnp.int32))[:, None] == jnp.arange(count)[None, :]
        picked = jnp.sum(jnp.where(hit[None, :, :, None], per_device[:, None, :, :], 0.0), axis=2)
        cols = picked.reshape(slab.shape[0], -1)
        return jnp.dot(cols, piece.reshape(-1, piece.shape[-1]), precision=precise, preferred_element_type=jnp.float32)

    buf = local[None]
    entries = [0]
    total = product(buf, entries)
    for masks in gather_rounds(count):
        others = [swap(buf, axis, m) for m in masks]
        for m, other in zip(masks, others):
            total = total + product(other, [m ^ q for q in entries])
        buf = jnp.concatenate([buf] + others, axis=0)
        entries = entries + [m ^ q for m in masks for q in entries]
    parts = total.reshape(4, rows, total.shape[-1])
    got = swap(parts[1::2], axis, 1)
    near = parts[0::2] + got
    return near[0] + swap(near[1], axis, 2)


def body(
    adjoint_state,
    speed_x,
    speed_y,
    speed_z,
    dispersion,
    face_flags,
    layer_weight,
    cov_x,
    offsets_x,
    cov_y,
    offsets_y,
):
    count = lax.axis_size("gx")
    me = lax.axis_index("gx")
    depth, rows, cols = adjoint_state.shape

    partial, to_prev, last_s, up_x0 = stencil(
        layer_weight, adjoint_state, face_flags, speed_x, speed_y, speed_z, dispersion
    )
    from_next = passed_along(to_prev, "gx", -1)
    from_prev = passed_along(last_s, "gx", 1)

    recharge = corrected(layer_weight, partial, up_x0, from_prev, from_next, last_s)

    own_slab = cx_slab(cov_x, offsets_x, me, rows)
    pair_slab = jnp.concatenate([own_slab, swap(own_slab, "gx", 1)], axis=0)
    late_pair, _ = lax.optimization_barrier((pair_slab, recharge))
    slab = jnp.concatenate([pair_slab, swap(late_pair, "gx", 2)], axis=0)
    mixed = mixed_rows(recharge, slab, "gx")

    nyb = offsets_y.shape[0]
    col_block = (jnp.arange(nyb)[:, None] + offsets_y) % nyb
    blocks_y = mixed.reshape(rows, nyb, BLK)
    fixed = [blocks_y, jnp.roll(blocks_y, 1, axis=1), jnp.roll(blocks_y, -(nyb // 2), axis=1)]
    hit = col_block[:, 3:, None] == jnp.arange(nyb)[None, None, :]
    rest = jnp.sum(jnp.where(hit[None, :, :, :, None], blocks_y[:, None, None, :, :], 0.0), axis=3)
    picked = jnp.concatenate([jnp.stack(fixed, axis=2), rest], axis=2)
    prior = jnp.einsum(
        "xrkc,rikc->xri",
        picked,
        cov_y.reshape(nyb, BLK, cov_y.shape[1], BLK),
        precision=precise,
        preferred_element_type=jnp.float32,
    ).reshape(rows, cols)
    return (recharge, prior)


def solution(mesh):
    return jax.shard_map(
        body,
        mesh=mesh,
        in_specs=(
            P(None, ("grp", "gx"), None),
            P(None, ("grp", "gx"), None),
            P(None, ("grp", "gx"), None),
            P(None, ("grp", "gx"), None),
            P(None, ("grp", "gx"), None),
            P(None, ("grp", "gx"), None),
            P(),
            P("gx", None, None),
            P(),
            P(),
            P(),
        ),
        out_specs=(P(("grp", "gx"), None), P(("grp", "gx"), None)),
        check_vma=False,
    )
```

```python
import jax
import jax.numpy as jnp
from jax import lax
from jax.experimental import pallas as pl
from jax.experimental.pallas import tpu as pltpu
from jax.sharding import PartitionSpec as P

BLK = 128
Z_CHUNK = 8

precise = lax.Precision.HIGH


def passed_along(value, axis, steps):
    count = lax.axis_size(axis)
    first, last = (max(0, -steps), min(count, count - steps))
    return lax.ppermute(value, axis, [(source, source + steps) for source in range(first, last)])


def coefs(flags, bit, speed, spread):
    on = (flags & bit) != 0
    lower = spread + jnp.where(on, speed, 0.0)
    upper = spread + jnp.where(on, 0.0, speed)
    return lower, upper


def stencil_kernel(w_ref, s_ref, sprev_ref, f_ref, vx_ref, vy_ref, vz_ref, d_ref, out_ref, to_prev_ref, last_ref, up_ref):
    c = pl.program_id(0)
    rows, cols = out_ref.shape
    sub = lax.broadcasted_iota(jnp.int32, (rows, cols), 0)
    lane = lax.broadcasted_iota(jnp.int32, (rows, cols), 1)

    @pl.when(c == 0)
    def _():
        out_ref[...] = jnp.zeros_like(out_ref)

    prev = jnp.where(c > 0, sprev_ref[0], 0.0)
    acc = jnp.zeros((rows, cols), jnp.float32)
    for j in range(s_ref.shape[0]):
        z = c * s_ref.shape[0] + j
        s = s_ref[j]
        f = f_ref[j]
        d = d_ref[j]
        lo_x, up_x = coefs(f, 1, vx_ref[j], d)
        to_prev_ref[0, pl.ds(z, 1), :] = s[0:1, :]
        to_prev_ref[1, pl.ds(z, 1), :] = lo_x[0:1, :]
        last_ref[pl.ds(z, 1), :] = s[rows - 1:rows, :]
        up_ref[pl.ds(z, 1), :] = up_x[0:1, :]
        lo_y, up_y = coefs(f, 2, vy_ref[j], d)
        lo_z, up_z = coefs(f, 4, vz_ref[j], d)
        s_xm = jnp.where(sub == 0, 0.0, pltpu.roll(s, 1, 0))
        jx = s - s_xm
        ax = lo_x * jx
        ax_next = jnp.where(sub == rows - 1, 0.0, pltpu.roll(ax, rows - 1, 0))
        img = up_x * jx - ax_next
        s_ym = jnp.where(lane == 0, 0.0, pltpu.roll(s, 1, 1))
        jy = s - s_ym
        ay = lo_y * jy
        ay_next = jnp.where(lane == cols - 1, 0.0, pltpu.roll(ay, cols - 1, 1))
        img = img + (up_y * jy - ay_next)
        jz = s - prev
        img = img + up_z * jz
        acc = acc + w_ref[z] * img
        w_before = jnp.where(z > 0, w_ref[jnp.maximum(z - 1, 0)], 0.0)
        acc = acc - w_before * (lo_z * jz)
        prev = s
    out_ref[...] += acc


def stencil(layer_weight, s, f, vx, vy, vz, d):
    depth, rows, cols = s.shape
    zc = Z_CHUNK if depth % Z_CHUNK == 0 else depth
    block = pl.BlockSpec((zc, rows, cols), lambda c: (c, 0, 0))
    prev_block = pl.BlockSpec((1, rows, cols), lambda c: (jnp.maximum(c * zc - 1, 0), 0, 0))
    return pl.pallas_call(
        stencil_kernel,
        grid=(depth // zc,),
        in_specs=[
            pl.BlockSpec(memory_space=pltpu.SMEM),
            block,
            prev_block,
            block,
            block,
            block,
            block,
            block,
        ],
        out_specs=[
            pl.BlockSpec((rows, cols), lambda c: (0, 0)),
            pl.BlockSpec((2, depth, cols), lambda c: (0, 0, 0)),
            pl.BlockSpec((depth, cols), lambda c: (0, 0)),
            pl.BlockSpec((depth, cols), lambda c: (0, 0)),
        ],
        out_shape=[
            jax.ShapeDtypeStruct((rows, cols), jnp.float32),
            jax.ShapeDtypeStruct((2, depth, cols), jnp.float32),
            jax.ShapeDtypeStruct((depth, cols), jnp.float32),
            jax.ShapeDtypeStruct((depth, cols), jnp.float32),
        ],
        compiler_params=pltpu.CompilerParams(dimension_semantics=("arbitrary",)),
    )(layer_weight, s, s, f, vx, vy, vz, d)


def fix_kernel(w_ref, partial_ref, up_ref, prev_ref, next_ref, last_ref, out_ref):
    rows, cols = partial_ref.shape
    depth = up_ref.shape[0]
    corr_first = jnp.zeros((1, cols), jnp.float32)
    corr_last = jnp.zeros((1, cols), jnp.float32)
    for z in range(depth):
        w = w_ref[z]
        corr_first = corr_first - w * (up_ref[pl.ds(z, 1), :] * prev_ref[pl.ds(z, 1), :])
        jump = next_ref[0, pl.ds(z, 1), :] - last_ref[pl.ds(z, 1), :]
        corr_last = corr_last - w * (next_ref[1, pl.ds(z, 1), :] * jump)
    row = lax.broadcasted_iota(jnp.int32, (rows, cols), 0)
    out_ref[...] = (
        partial_ref[...] + jnp.where(row == 0, corr_first, 0.0) + jnp.where(row == rows - 1, corr_last, 0.0)
    )


def corrected(w, partial, up_x0, from_prev, from_next, last_s):
    vmem = pl.BlockSpec(memory_space=pltpu.VMEM)
    return pl.pallas_call(
        fix_kernel,
        in_specs=[pl.BlockSpec(memory_space=pltpu.SMEM)] + [vmem] * 5,
        out_shape=jax.ShapeDtypeStruct(partial.shape, jnp.float32),
    )(w, partial, up_x0, from_prev, from_next, last_s)


def gather_rounds(count):
    bits = []
    bit = count // 2
    while bit >= 4:
        bits.append(bit)
        bit //= 2
    if len(bits) < 2:
        return [[b] for b in bits]
    return [[bits[1], bits[0], bits[0] | bits[1]]] + [[b] for b in bits[2:]]


def swap(value, axis, mask):
    count = lax.axis_size(axis)
    return lax.ppermute(value, axis, [(i, i ^ mask) for i in range(count)])


def cx_slab(cov_rows, offsets, device, rows):
    nxb = offsets.shape[0]
    global_rows = device * rows + jnp.arange(rows)
    row_block = global_rows // BLK
    target = (row_block[:, None] + offsets[row_block]) % nxb
    blocks = jnp.arange(nxb)
    hit = target[:, :, None, None] == blocks[None, None, :, None]
    slab = jnp.sum(jnp.where(hit, cov_rows.astype(jnp.float32)[:, :, None, :], 0.0), axis=1)
    return slab.reshape(rows, -1)


def mixed_rows(local, slab, axis):
    count = lax.axis_size(axis)
    me = lax.axis_index(axis)
    rows = local.shape[0]
    per_device = slab.reshape(slab.shape[0], count, rows)

    def product(piece, masks):
        cols = jnp.take(per_device, me ^ jnp.array(masks, jnp.int32), axis=1).reshape(slab.shape[0], -1)
        return jnp.dot(cols, piece.reshape(-1, piece.shape[-1]), precision=precise, preferred_element_type=jnp.float32)

    buf = local[None]
    entries = [0]
    own_cols = lax.dynamic_slice_in_dim(per_device, me, 1, axis=1).reshape(slab.shape[0], -1)
    total = jnp.dot(own_cols, local, precision=precise, preferred_element_type=jnp.float32)
    for masks in gather_rounds(count):
        others = [swap(buf, axis, m) for m in masks]
        for m, other in zip(masks, others):
            total = total + product(other, [m ^ q for q in entries])
        buf = jnp.concatenate([buf] + others, axis=0)
        entries = entries + [m ^ q for m in masks for q in entries]
    parts = total.reshape(4, rows, total.shape[-1])
    got = swap(parts[1::2], axis, 1)
    near = parts[0::2] + got
    return near[0] + swap(near[1], axis, 2)


def body(
    adjoint_state,
    speed_x,
    speed_y,
    speed_z,
    dispersion,
    face_flags,
    layer_weight,
    cov_x,
    offsets_x,
    cov_y,
    offsets_y,
):
    count = lax.axis_size("gx")
    me = lax.axis_index("gx")
    depth, rows, cols = adjoint_state.shape

    partial, to_prev, last_s, up_x0 = stencil(
        layer_weight, adjoint_state, face_flags, speed_x, speed_y, speed_z, dispersion
    )
    from_next = passed_along(to_prev, "gx", -1)
    from_prev = passed_along(last_s, "gx", 1)

    recharge = corrected(layer_weight, partial, up_x0, from_prev, from_next, last_s)

    own_slab = cx_slab(cov_x, offsets_x, me, rows)
    pair_slab = jnp.concatenate([own_slab, swap(own_slab, "gx", 1)], axis=0)
    late_pair, _ = lax.optimization_barrier((pair_slab, recharge))
    slab = jnp.concatenate([pair_slab, swap(late_pair, "gx", 2)], axis=0)
    mixed = mixed_rows(recharge, slab, "gx")

    nyb = offsets_y.shape[0]
    col_block = (jnp.arange(nyb)[:, None] + offsets_y) % nyb
    blocks_y = mixed.reshape(rows, nyb, BLK)
    fixed = [blocks_y, jnp.roll(blocks_y, 1, axis=1), jnp.roll(blocks_y, -(nyb // 2), axis=1)]
    hit = col_block[:, 3:, None] == jnp.arange(nyb)[None, None, :]
    rest = jnp.sum(jnp.where(hit[None, :, :, :, None], blocks_y[:, None, None, :, :], 0.0), axis=3)
    picked = jnp.concatenate([jnp.stack(fixed, axis=2), rest], axis=2)
    prior = jnp.einsum(
        "xrkc,rikc->xri",
        picked,
        cov_y.reshape(nyb, BLK, cov_y.shape[1], BLK),
        precision=precise,
        preferred_element_type=jnp.float32,
    ).reshape(rows, cols)
    return (recharge, prior)


def solution(mesh):
    return jax.shard_map(
        body,
        mesh=mesh,
        in_specs=(
            P(None, ("grp", "gx"), None),
            P(None, ("grp", "gx"), None),
            P(None, ("grp", "gx"), None),
            P(None, ("grp", "gx"), None),
            P(None, ("grp", "gx"), None),
            P(None, ("grp", "gx"), None),
            P(),
            P("gx", None, None),
            P(),
            P(),
            P(),
        ),
        out_specs=(P(("grp", "gx"), None), P(("grp", "gx"), None)),
        check_vma=False,
    )
```
